512 devices in a mesh: panel: 2 (over x_lo), lat: 8 (over y, core), lon: 32 (over z, x_hi).
Axes of the slice: x: 4 (x_hi: 2, x_lo: 2; x = x_hi * 2 + x_lo), y: 4, z: 16, core: 2. Of those that a mesh axis runs over, the one named last changes fastest.
Arguments:
- fields: float32 [2, 6, 4, 1024, 4096], P('panel', None, None, 'lat', 'lon'), may hold values from -6 to 6
- viscosity: float32 [2, 4, 1024, 4096], P('panel', None, 'lat', 'lon'), may hold values from 0.01 to 0.1
- partner: int32 [2, 8, 1024, 1], P('panel', 'lat', 'lon'), may hold values from 0 to 31; in each aligned block of 32 rows (0 to 31, 32 to 63, ..., all dimensions but the last counted through in order) at most 2 rows name the same one
- src_row: int32 [2, 8, 65536], P('panel', 'lat', 'lon'), may hold values from 0 to 126
- src_col: int32 [2, 8, 65536], P('panel', 'lat', 'lon'), may hold values from 0 to 126
- weight_id: int32 [2, 8, 65536], P('panel', 'lat', 'lon'), may hold values from 0 to 63
- border_angle: float32 [2, 8, 65536], P('panel', 'lat', 'lon'), may hold values from -3.140625 to 3.140625
- dest_cell: int32 [2, 8, 65536], P('panel', 'lat', 'lon'), may hold values from 0 to 16383, as said below
Outputs:
- new_fields: float32 [2, 6, 4, 1024, 4096], P('panel', None, None, 'lat', 'lon')
- pressure: float32 [2, 4, 1024, 4096], P('panel', None, 'lat', 'lon')
The draws below stay inside these ranges and needn't reach their ends.
Inputs may be any that keep to these rules, and one draw needn't show every extreme that they name: `partner`: A border block's sources lie on the device of the other panel with the same lat index and this lon index; among the 32 blocks of one device no lon index is named by more than 2 blocks. `dest_cell`: the 2048 border cells of one device are distinct cells of its block.
All inputs are finite; a program needn't handle non-finite values.
Results may differ from the reference program's by a relative error of at most 0.0002.
Values sent between devices are 32-bit elements; how exact they have to be, the bound alone decides.
No kernel may reach another device: no remote copies, remote signals or barrier semaphores. Data moves between devices by JAX's collectives and lax.ppermute only.
A program may use at most 128 MiB of HBM per device.

```python
import math
import jax
import jax.numpy as jnp
import numpy as np
from jax import lax

NR = 4
CLAT = 128
CLON = 128
BC = 64
CAP = 2
WQ = 8
NB = 32
NTH = 1024
NPH = 4096
N_LAT = 8
N_LON = 32


def draw_dest_cell(key, part):
    devices = 2 * N_LAT * N_LON
    key_list = jax.random.split(key, devices)
    orders = jax.vmap(lambda sub_key: jax.random.permutation(sub_key, CLAT * CLON))(key_list)
    return orders[:, :NB * BC].astype(jnp.int32).reshape(2, N_LAT, N_LON * NB * BC)


def place_ends(entries, key, low, high):
    shape = entries.shape
    index_at = [jax.random.randint(jax.random.fold_in(key, axis), (), 0, shape[axis]) for axis in range(len(shape))]
    entries = entries.at[tuple(index_at)].set(low)
    longest = shape.index(max(shape))
    index_at[longest] = (index_at[longest] + 1) % shape[longest]
    return entries.at[tuple(index_at)].set(high)


def level_of(stream_key, shape, cuts, least, largest):
    level = 1.0
    for axis_at, parts in cuts:
        heights = jax.random.uniform(jax.random.fold_in(jax.random.fold_in(stream_key, 6), axis_at), (parts,), jnp.float32, least / len(cuts), largest / len(cuts))
        level = level * jnp.repeat(jnp.exp(heights), shape[axis_at] // parts).reshape((-1,) + (1,) * (len(shape) - 1 - axis_at))
    return level


def routed_block(stream_key, own, number, rows, count, top, limit, skew):
    ranking = jax.random.permutation(stream_key, count)
    crowded, common = portions_of(count, rows * top, limit, skew, True), portions_of(count, rows * top, limit, skew, False)
    places = jnp.arange(count)

    def named(lengths, turn):
        used = int((lengths > 0).sum())
        fixed = max(1, used // 4)
        moved = fixed + (places - fixed + turn * (used - fixed)) % max(1, count - fixed)
        return jnp.zeros((count,), jnp.int32).at[ranking[jnp.where(places < fixed, places, moved)]].set(jnp.asarray(lengths, jnp.int32))

    lengths = jnp.where(number % 4 == 0, named(crowded, number // 4), named(common, number - number // 4 - 1))
    mixed = jax.random.permutation(jax.random.fold_in(own, 3), count)
    source_of, sink = mixed[0:count // 2 * 2:2], mixed[1:count // 2 * 2:2]
    margin = jnp.minimum(lengths[source_of] - 1, limit - lengths[sink]) // 2
    margin = jnp.where((source_of == ranking[0]) | (sink == ranking[0]) | (lengths[sink] == 0), 0, jnp.maximum(margin, 0))
    moved = jax.random.randint(jax.random.fold_in(own, 4), (count // 2,), 0, 1 << 20) % (margin + 1)
    lengths = lengths.at[source_of].add(-moved).at[sink].add(moved)
    items = jnp.searchsorted(jnp.cumsum(lengths), jnp.arange(rows * top), side="right").astype(jnp.int32)
    grid = items.reshape(top, rows).T
    grid = grid[jax.random.permutation(jax.random.fold_in(own, 1), rows)]
    turn = jax.random.randint(jax.random.fold_in(own, 2), (rows, 1), 0, top)
    return jnp.take_along_axis(grid, (jnp.arange(top)[None, :] + turn) % top, axis=1)


def portions_of(amount, total, bound, skew, full):
    weights = [(1 << 20) // math.isqrt(rank ** skew) + 1 for rank in range(1, amount + 1)]
    largest = bound if full else min(bound, max(-(-total // amount), total * weights[0] // sum(weights)))
    least = 1 if total - largest >= amount - 1 else 0
    holding, spare = [largest] + [least] * (amount - 1), total - largest - least * (amount - 1)
    while spare > 0:
        movable = [i for i in range(1, amount) if holding[i] < largest] or [i for i in range(1, amount) if holding[i] < bound]
        whole, left = sum([weights[i] for i in movable]), spare
        for i in movable:
            addition = min(bound - holding[i], max(1, left * weights[i] // whole), spare)
            holding[i] = holding[i] + addition
            spare = spare - addition
    return np.array(holding)


def bell_draw(rng, extent, deviation, limit, shards=(), kind=jnp.bfloat16):
    entries = jax.random.normal(rng, extent, jnp.float32) * deviation
    if len(shards) > 0:
        entries = level_of(rng, extent, shards, -0.22, 0.18) * entries
    return jnp.clip(entries, min=-limit, max=limit).astype(kind)


def setup_inputs(seed: int = 0) -> dict:
    key_of = jax.random.split(jax.random.key(seed), 9)
    fields = bell_draw(key_of[0], (2, 6, NR, NTH, NPH), 1.0, 6.0, ((0, 2), (3, 8), (4, 32)), jnp.float32)
    viscosity = jnp.clip(jnp.exp(math.log(0.1) - 2.3025851 * jax.random.uniform(key_of[1], (2, NR, NTH, NPH), jnp.float32) ** level_of(key_of[1], (2, NR, NTH, NPH), ((0, 2), (2, 8), (3, 32)), -0.2, 0.2)), 0.01, 0.1)
    partner_keys = jax.random.split(jax.random.fold_in(key_of[2], 1), 2 * N_LAT * (N_LON * NB) // NB)
    partner_turns = jax.random.permutation(jax.random.fold_in(key_of[2], 3), 2 * N_LAT * (N_LON * NB) // NB)
    partner = jax.vmap(lambda own, number: routed_block(jax.random.fold_in(key_of[2], 2), own, number, NB, N_LON, 1, CAP, 1))(partner_keys, partner_turns).reshape((2, N_LAT, N_LON * NB, 1))
    src_row = place_ends(jax.random.randint(key_of[3], (2, N_LAT, N_LON * NB * BC), 0, CLAT - 1), jax.random.fold_in(key_of[3], 1), 0, (CLAT - 1) - 1).astype(jnp.int32)
    src_col = place_ends(jax.random.randint(key_of[4], (2, N_LAT, N_LON * NB * BC), 0, CLON - 1), jax.random.fold_in(key_of[4], 1), 0, (CLON - 1) - 1).astype(jnp.int32)
    weight_id = place_ends(jax.random.randint(key_of[5], (2, N_LAT, N_LON * NB * BC), 0, WQ * WQ), jax.random.fold_in(key_of[5], 1), 0, (WQ * WQ) - 1).astype(jnp.int32)
    border_angle = jnp.clip(jax.random.uniform(key_of[6], (2, N_LAT, N_LON * NB * BC), jnp.float32, -3.140625, 3.140625), -3.140625, 3.140625)
    dest_cell = draw_dest_cell(jax.random.fold_in(key_of[8], 71), 0)
    return {"fields": fields, "viscosity": viscosity, "partner": partner, "src_row": src_row, "src_col": src_col, "weight_id": weight_id, "border_angle": border_angle, "dest_cell": dest_cell}


BUOYANCY = 0.5

def metric(row_index, total_rows):
    colatitude = math.pi / 4.0 + (row_index.astype(jnp.float32) + 0.5) * (math.pi / 2.0) / total_rows
    inv_sine = 1.0 / jnp.sin(colatitude)
    return (inv_sine, inv_sine * inv_sine)

def lap_shrink(field, row_gain):
    centre = field[..., 1:-1, 1:-1]
    padded = jnp.pad(centre, [(0, 0)] * (centre.ndim - 3) + [(1, 1), (0, 0), (0, 0)])
    lat_term = field[..., 2:, 1:-1] + field[..., :-2, 1:-1] - 2.0 * centre
    lon_term = field[..., 1:-1, 2:] + field[..., 1:-1, :-2] - 2.0 * centre
    radial = padded[..., 2:, :, :] + padded[..., :-2, :, :] - 2.0 * centre
    return lat_term + row_gain[:, None] * lon_term + radial

def diverge(velocity, inv_sine):
    radial_pad = jnp.pad(velocity[0, :, 1:-1, 1:-1], ((1, 1), (0, 0), (0, 0)))
    lat_part = velocity[1, :, 2:, 1:-1] - velocity[1, :, :-2, 1:-1]
    lon_part = velocity[2, :, 1:-1, 2:] - velocity[2, :, 1:-1, :-2]
    rad_part = radial_pad[2:] - radial_pad[:-2]
    return 0.5 * (lat_part + inv_sine[:, None] * lon_part + rad_part)

def gradient(pressure, inv_sine):
    radial_pad = jnp.pad(pressure[:, 1:-1, 1:-1], ((1, 1), (0, 0), (0, 0)))
    grad_rad = 0.5 * (radial_pad[2:] - radial_pad[:-2])
    grad_lat = 0.5 * (pressure[:, 2:, 1:-1] - pressure[:, :-2, 1:-1])
    grad_lon = 0.5 * inv_sine[:, None] * (pressure[:, 1:-1, 2:] - pressure[:, 1:-1, :-2])
    return (grad_rad, grad_lat, grad_lon)

def cosine_table(length):
    mode_ids = jnp.arange(length, dtype=jnp.float32)
    cell_mid = jnp.arange(length, dtype=jnp.float32) + 0.5
    row_norm = jnp.sqrt(jnp.where(mode_ids > 0, 2.0, 1.0) / length)
    cos_table = row_norm[:, None] * jnp.cos(math.pi * mode_ids[:, None] * cell_mid[None, :] / length)
    eigenvalue = 4.0 * jnp.sin(math.pi * mode_ids / (2.0 * length)) ** 2
    return (cos_table, eigenvalue)

def coarse_divisor(levels, n_lat, n_lon):
    eig_rad = cosine_table(levels)[1]
    eig_lat = cosine_table(n_lat)[1]
    eig_lon = cosine_table(n_lon)[1]
    return eig_rad[:, None, None] + eig_lat[None, :, None] + eig_lon[None, None, :] + 1.0 / (n_lat * n_lon)

def coarse_solve(block_sum, n_lat, n_lon):
    highest = lax.Precision.HIGHEST
    tab_rad = cosine_table(block_sum.shape[0])[0]
    tab_lat = cosine_table(n_lat)[0]
    tab_lon = cosine_table(n_lon)[0]
    spectrum = jnp.einsum('kr,rlo->klo', tab_rad, block_sum, precision=highest)
    spectrum = jnp.einsum('kl,rlo->rko', tab_lat, spectrum, precision=highest)
    spectrum = jnp.einsum('ko,rlo->rlk', tab_lon, spectrum, precision=highest)
    spectrum = spectrum / coarse_divisor(block_sum.shape[0], n_lat, n_lon)
    restored = jnp.einsum('kr,klo->rlo', tab_rad, spectrum, precision=highest)
    restored = jnp.einsum('kl,rko->rlo', tab_lat, restored, precision=highest)
    restored = jnp.einsum('ko,rlk->rlo', tab_lon, restored, precision=highest)
    return restored / math.sqrt(n_lat * n_lon)

def fractions(weight_ids):
    frac_lat = ((weight_ids // WQ).astype(jnp.float32) + 0.5) / WQ
    frac_lon = ((weight_ids % WQ).astype(jnp.float32) + 0.5) / WQ
    return (frac_lat, frac_lon)

def bilinear(lower_left, lower_right, upper_left, upper_right, frac_lat, frac_lon):
    return (1.0 - frac_lat) * (1.0 - frac_lon) * lower_left + (1.0 - frac_lat) * frac_lon * lower_right + frac_lat * (1.0 - frac_lon) * upper_left + frac_lat * frac_lon * upper_right

def reference(fields, viscosity, partner, src_row, src_col, weight_id, border_angle, dest_cell):
    n_lat, n_lon = (N_LAT, N_LON)
    total_rows, total_cols = (CLAT * n_lat, CLON * n_lon)
    channels = 6 * NR
    cells = jnp.transpose(fields.reshape(2, channels, total_rows, total_cols), (0, 2, 3, 1))
    shape = (2, n_lat, n_lon, NB, BC)
    panel_ids = jnp.arange(2, dtype=jnp.int32).reshape(2, 1, 1, 1, 1)
    lat_ids = jnp.arange(n_lat, dtype=jnp.int32).reshape(1, n_lat, 1, 1, 1)
    lon_ids = jnp.arange(n_lon, dtype=jnp.int32).reshape(1, 1, n_lon, 1, 1)
    target = partner.reshape(2, n_lat, n_lon, NB, 1)
    other = jnp.broadcast_to(1 - panel_ids, shape)
    src_lat = jnp.broadcast_to(lat_ids * CLAT + src_row.reshape(shape), shape)
    src_lon = jnp.broadcast_to(target * CLON + src_col.reshape(shape), shape)
    lower_left = cells[other, src_lat, src_lon]
    lower_right = cells[other, src_lat, src_lon + 1]
    upper_left = cells[other, src_lat + 1, src_lon]
    upper_right = cells[other, src_lat + 1, src_lon + 1]
    frac_lat, frac_lon = fractions(weight_id.reshape(shape))
    values = bilinear(lower_left, lower_right, upper_left, upper_right, frac_lat[..., None], frac_lon[..., None])
    values = values.reshape(shape + (6, NR))
    turn = border_angle.reshape(shape)[..., None]
    cos_angle = jnp.cos(turn)
    sin_angle = jnp.sin(turn)
    rotated = jnp.stack([values[..., 0, :], cos_angle * values[..., 1, :] + sin_angle * values[..., 2, :], cos_angle * values[..., 2, :] - sin_angle * values[..., 1, :], values[..., 3, :], cos_angle * values[..., 4, :] + sin_angle * values[..., 5, :], cos_angle * values[..., 5, :] - sin_angle * values[..., 4, :]], axis=-2).reshape(shape + (channels,))
    dest = dest_cell.reshape(shape)
    dest_lat = jnp.broadcast_to(lat_ids * CLAT + dest // CLON, shape)
    dest_lon = jnp.broadcast_to(lon_ids * CLON + dest % CLON, shape)
    cells = cells.at[jnp.broadcast_to(panel_ids, shape), dest_lat, dest_lon].set(rotated)
    filled = jnp.transpose(cells, (0, 3, 1, 2)).reshape(2, 6, NR, total_rows, total_cols)
    row_index = jnp.arange(total_rows, dtype=jnp.int32)
    inv_sine, row_gain = metric(row_index, total_rows)
    rim_four = ((0, 0), (0, 0), (1, 1), (1, 1))
    rim_three = ((0, 0), (1, 1), (1, 1))
    outputs = []
    pressures = []
    for panel in range(2):
        current = filled[panel]
        stepped = current + viscosity[panel][None] * lap_shrink(jnp.pad(current, rim_four), row_gain)
        stepped = jnp.concatenate([stepped[0:1] + BUOYANCY * current[3:4], stepped[1:]], axis=0)
        divergence = diverge(jnp.pad(stepped[0:3], rim_four), inv_sine)
        press_one = -divergence / (4.0 + 2.0 * row_gain)[:, None]
        resid_one = -divergence + lap_shrink(jnp.pad(press_one, rim_three), row_gain)
        block_sum = resid_one.reshape(NR, n_lat, CLAT, n_lon, CLON).sum(axis=(2, 4)) * (1.0 / math.sqrt(CLAT * CLON))
        coarse = coarse_solve(block_sum, n_lat, n_lon)
        pressure = press_one + jnp.repeat(jnp.repeat(coarse, CLAT, axis=1), CLON, axis=2)
        grad_rad, grad_lat, grad_lon = gradient(jnp.pad(pressure, rim_three), inv_sine)
        outputs.append(jnp.stack([stepped[0] - grad_rad, stepped[1] - grad_lat, stepped[2] - grad_lon, stepped[3], stepped[4], stepped[5]], axis=0))
        pressures.append(pressure)
    return (jnp.stack(outputs, axis=0), jnp.stack(pressures, axis=0))
```

```python
import math

import jax
import jax.numpy as jnp
from jax import lax
from jax.sharding import PartitionSpec as P

CAP = 2
WQ = 8


BUOYANCY = 0.5


def partner_2(block, axis, apart):
    count = lax.axis_size(axis)
    route = []
    for low in range(count):
        high = low | 1 << apart
        if high != low and high < count:
            route += [(low, high), (high, low)]
    return lax.ppermute(block, axis, route)


def padded_2(shard, sides, width):
    for axis, dim in sides:
        size, length = (lax.axis_size(axis), shard.shape[dim])
        up = [(i, (i + 1) % size) for i in range(size - 1)]
        down = [(j, i) for i, j in up]
        last = lax.slice_in_dim(shard, length - width, length, axis=dim)
        leading = lax.slice_in_dim(shard, 0, width, axis=dim)
        before = lax.ppermute(last, axis, up)
        after = lax.ppermute(leading, axis, down)
        shard = jnp.concatenate([before, shard, after], axis=dim)
    return shard


def doubling_gather(block, axis):
    count = lax.axis_size(axis)
    index = lax.axis_index(axis)
    step = 1
    while step < count:
        other = lax.ppermute(block, axis, [(i, i ^ step) for i in range(count)])
        low = (index & step) == 0
        block = jnp.where(
            low, jnp.concatenate([block, other], 0), jnp.concatenate([other, block], 0)
        )
        step *= 2
    return block


def metric(row_index, total_rows):
    colatitude = (
        math.pi / 4.0 + (row_index.astype(jnp.float32) + 0.5) * (math.pi / 2.0) / total_rows
    )
    inv_sine = 1.0 / jnp.sin(colatitude)
    return (inv_sine, inv_sine * inv_sine)


def lap_shrink(field, row_gain):
    centre = field[..., 1:-1, 1:-1]
    padded = jnp.pad(centre, [(0, 0)] * (centre.ndim - 3) + [(1, 1), (0, 0), (0, 0)])
    lat_term = field[..., 2:, 1:-1] + field[..., :-2, 1:-1] - 2.0 * centre
    lon_term = field[..., 1:-1, 2:] + field[..., 1:-1, :-2] - 2.0 * centre
    radial = padded[..., 2:, :, :] + padded[..., :-2, :, :] - 2.0 * centre
    return lat_term + row_gain[:, None] * lon_term + radial


def diverge(velocity, inv_sine):
    radial_pad = jnp.pad(velocity[0, :, 1:-1, 1:-1], ((1, 1), (0, 0), (0, 0)))
    lat_part = velocity[1, :, 2:, 1:-1] - velocity[1, :, :-2, 1:-1]
    lon_part = velocity[2, :, 1:-1, 2:] - velocity[2, :, 1:-1, :-2]
    rad_part = radial_pad[2:] - radial_pad[:-2]
    return 0.5 * (lat_part + inv_sine[:, None] * lon_part + rad_part)


def gradient(pressure, inv_sine):
    radial_pad = jnp.pad(pressure[:, 1:-1, 1:-1], ((1, 1), (0, 0), (0, 0)))
    grad_rad = 0.5 * (radial_pad[2:] - radial_pad[:-2])
    grad_lat = 0.5 * (pressure[:, 2:, 1:-1] - pressure[:, :-2, 1:-1])
    grad_lon = 0.5 * inv_sine[:, None] * (pressure[:, 1:-1, 2:] - pressure[:, 1:-1, :-2])
    return (grad_rad, grad_lat, grad_lon)


def cosine_table(length):
    mode_ids = jnp.arange(length, dtype=jnp.float32)
    cell_mid = jnp.arange(length, dtype=jnp.float32) + 0.5
    row_norm = jnp.sqrt(jnp.where(mode_ids > 0, 2.0, 1.0) / length)
    cos_table = row_norm[:, None] * jnp.cos(
        math.pi * mode_ids[:, None] * cell_mid[None, :] / length
    )
    eigenvalue = 4.0 * jnp.sin(math.pi * mode_ids / (2.0 * length)) ** 2
    return (cos_table, eigenvalue)


def coarse_divisor(levels, n_lat, n_lon):
    eig_rad = cosine_table(levels)[1]
    eig_lat = cosine_table(n_lat)[1]
    eig_lon = cosine_table(n_lon)[1]
    return (
        eig_rad[:, None, None]
        + eig_lat[None, :, None]
        + eig_lon[None, None, :]
        + 1.0 / (n_lat * n_lon)
    )


def coarse_solve(block_sum, n_lat, n_lon):
    highest = lax.Precision.HIGHEST
    tab_rad = cosine_table(block_sum.shape[0])[0]
    tab_lat = cosine_table(n_lat)[0]
    tab_lon = cosine_table(n_lon)[0]
    spectrum = jnp.einsum("kr,rlo->klo", tab_rad, block_sum, precision=highest)
    spectrum = jnp.einsum("kl,rlo->rko", tab_lat, spectrum, precision=highest)
    spectrum = jnp.einsum("ko,rlo->rlk", tab_lon, spectrum, precision=highest)
    spectrum = spectrum / coarse_divisor(block_sum.shape[0], n_lat, n_lon)
    restored = jnp.einsum("kr,klo->rlo", tab_rad, spectrum, precision=highest)
    restored = jnp.einsum("kl,rko->rlo", tab_lat, restored, precision=highest)
    restored = jnp.einsum("ko,rlk->rlo", tab_lon, restored, precision=highest)
    return restored / math.sqrt(n_lat * n_lon)


def fractions(weight_ids):
    frac_lat = ((weight_ids // WQ).astype(jnp.float32) + 0.5) / WQ
    frac_lon = ((weight_ids % WQ).astype(jnp.float32) + 0.5) / WQ
    return (frac_lat, frac_lon)


def bilinear(lower_left, lower_right, upper_left, upper_right, frac_lat, frac_lon):
    return (
        (1.0 - frac_lat) * (1.0 - frac_lon) * lower_left
        + (1.0 - frac_lat) * frac_lon * lower_right
        + frac_lat * (1.0 - frac_lon) * upper_left
        + frac_lat * frac_lon * upper_right
    )


def shards(fields, viscosity, partner, src_row, src_col, weight_id, border_angle, dest_cell):
    n_lat = lax.axis_size("lat")
    n_lon = lax.axis_size("lon")
    lat_pos = lax.axis_index("lat")
    lon_pos = lax.axis_index("lon")
    own_fields = fields[0]
    levels, rows_dev, cols_dev = (own_fields.shape[1], own_fields.shape[2], own_fields.shape[3])
    channels = 6 * levels
    blocks = partner.shape[2]
    block_cells = src_row.shape[2] // blocks
    capacity = CAP
    slot_count = n_lon * capacity
    total_rows = rows_dev * n_lat
    flat_cells = own_fields.reshape(channels, rows_dev * cols_dev)
    target = partner[0, 0, :, 0]
    onehot = (target[:, None] == jnp.arange(n_lon, dtype=jnp.int32)[None, :]).astype(jnp.int32)
    before = jnp.sum(
        (jnp.cumsum(onehot, axis=0, dtype=jnp.int32) - onehot) * onehot, axis=1, dtype=jnp.int32
    )
    slot_of = target * capacity + before
    base_cell = (src_row[0, 0] * cols_dev + src_col[0, 0]).reshape(blocks, block_cells)
    weight_ids = weight_id[0, 0].reshape(blocks, block_cells)
    empty = jnp.zeros((slot_count, block_cells), jnp.int32)
    requests = partner_2(
        empty.at[slot_of].set(base_cell).reshape(n_lon, capacity * block_cells), "panel", 0
    )
    requests = lax.all_to_all(requests, "lon", split_axis=0, concat_axis=0, tiled=True)
    served = jnp.stack(
        tuple(
            (
                jnp.take(flat_cells, requests + offset, axis=1)
                for offset in (0, 1, cols_dev, cols_dev + 1)
            )
        ),
        axis=0,
    )
    served = lax.all_to_all(served, "lon", split_axis=2, concat_axis=2, tiled=True)
    served = partner_2(served, "panel", 0)
    picked = served.reshape(4, channels, slot_count, block_cells)[:, :, slot_of, :]
    frac_lat, frac_lon = fractions(weight_ids)
    values = bilinear(picked[0], picked[1], picked[2], picked[3], frac_lat, frac_lon)
    values = values.reshape(6, levels, blocks * block_cells)
    turn = border_angle[0, 0]
    cos_angle = jnp.cos(turn)
    sin_angle = jnp.sin(turn)
    rotated = jnp.stack(
        [
            values[0],
            cos_angle * values[1] + sin_angle * values[2],
            cos_angle * values[2] - sin_angle * values[1],
            values[3],
            cos_angle * values[4] + sin_angle * values[5],
            cos_angle * values[5] - sin_angle * values[4],
        ],
        axis=0,
    ).reshape(channels, blocks * block_cells)
    filled = flat_cells.at[:, dest_cell[0, 0]].set(rotated).reshape(6, levels, rows_dev, cols_dev)
    diffusivity = viscosity[0]
    inv_own, gain_own = metric(
        lat_pos * rows_dev + jnp.arange(-0, rows_dev + 0, dtype=jnp.int32), total_rows
    )
    widened = padded_2(filled, (("lat", 2), ("lon", 3)), 1)
    stepped = filled + diffusivity[None] * lap_shrink(widened, gain_own)
    stepped = jnp.concatenate([stepped[0:1] + BUOYANCY * filled[3:4], stepped[1:]], axis=0)
    velocity = padded_2(stepped[0:3], (("lat", 2), ("lon", 3)), 1)
    divergence = diverge(velocity, inv_own)
    press_one = -divergence / (4.0 + 2.0 * gain_own)[:, None]
    press_wide = padded_2(press_one, (("lat", 1), ("lon", 2)), 1)
    resid_one = -divergence + lap_shrink(press_wide, gain_own)
    block_sum = jnp.sum(resid_one, axis=(1, 2)) * (1.0 / math.sqrt(rows_dev * cols_dev))
    gathered = doubling_gather(block_sum[None], "lon")
    gathered = doubling_gather(gathered[None], "lat")
    coarse = coarse_solve(jnp.transpose(gathered, (2, 0, 1)), n_lat, n_lon)
    start = jnp.zeros((), jnp.int32)
    near = lax.dynamic_slice(
        jnp.pad(coarse, ((0, 0), (1, 1), (1, 1))), (start, lat_pos, lon_pos), (levels, 3, 3)
    )
    own_coarse = near[:, 1, 1]
    pressure = press_one + own_coarse[:, None, None]
    row_at = lax.broadcasted_iota(jnp.int32, (rows_dev + 2, cols_dev + 2), 0)
    col_at = lax.broadcasted_iota(jnp.int32, (rows_dev + 2, cols_dev + 2), 1)
    rim_coarse = jnp.where(
        row_at == 0,
        near[:, 0, 1][:, None, None],
        jnp.where(
            row_at == rows_dev + 1,
            near[:, 2, 1][:, None, None],
            jnp.where(
                col_at == 0,
                near[:, 1, 0][:, None, None],
                jnp.where(
                    col_at == cols_dev + 1, near[:, 1, 2][:, None, None], own_coarse[:, None, None]
                ),
            ),
        ),
    )
    press_rim = press_wide + rim_coarse
    grad_rad, grad_lat, grad_lon = gradient(press_rim, inv_own)
    result = jnp.stack(
        [
            stepped[0] - grad_rad,
            stepped[1] - grad_lat,
            stepped[2] - grad_lon,
            stepped[3],
            stepped[4],
            stepped[5],
        ],
        axis=0,
    )
    return (result[None], pressure[None])


def solution(mesh):
    return jax.shard_map(
        shards,
        mesh=mesh,
        in_specs=(
            P("panel", None, None, "lat", "lon"),
            P("panel", None, "lat", "lon"),
            P("panel", "lat", "lon", None),
            P("panel", "lat", "lon"),
            P("panel", "lat", "lon"),
            P("panel", "lat", "lon"),
            P("panel", "lat", "lon"),
            P("panel", "lat", "lon"),
        ),
        out_specs=(P("panel", None, None, "lat", "lon"), P("panel", None, "lat", "lon")),
        check_vma=False,
    )
```

```python
import math

import jax
import jax.numpy as jnp
from jax import lax
from jax.sharding import PartitionSpec as P

CAP = 2
WQ = 8


BUOYANCY = 0.5


def partner_2(block, axis, apart):
    count = lax.axis_size(axis)
    route = []
    for low in range(count):
        high = low | 1 << apart
        if high != low and high < count:
            route += [(low, high), (high, low)]
    return lax.ppermute(block, axis, route)


def padded_2(shard, sides, width):
    for axis, dim in sides:
        size, length = (lax.axis_size(axis), shard.shape[dim])
        up = [(i, (i + 1) % size) for i in range(size - 1)]
        down = [(j, i) for i, j in up]
        last = lax.slice_in_dim(shard, length - width, length, axis=dim)
        leading = lax.slice_in_dim(shard, 0, width, axis=dim)
        before = lax.ppermute(last, axis, up)
        after = lax.ppermute(leading, axis, down)
        shard = jnp.concatenate([before, shard, after], axis=dim)
    return shard


def doubling_gather(block, axis):
    count = lax.axis_size(axis)
    index = lax.axis_index(axis)
    step = 1
    while step < count:
        other = lax.ppermute(block, axis, [(i, i ^ step) for i in range(count)])
        low = (index & step) == 0
        block = jnp.where(
            low, jnp.concatenate([block, other], 0), jnp.concatenate([other, block], 0)
        )
        step *= 2
    return block


def metric(row_index, total_rows):
    colatitude = (
        math.pi / 4.0 + (row_index.astype(jnp.float32) + 0.5) * (math.pi / 2.0) / total_rows
    )
    inv_sine = 1.0 / jnp.sin(colatitude)
    return (inv_sine, inv_sine * inv_sine)


def lap_shrink(field, row_gain):
    centre = field[..., 1:-1, 1:-1]
    padded = jnp.pad(centre, [(0, 0)] * (centre.ndim - 3) + [(1, 1), (0, 0), (0, 0)])
    lat_term = field[..., 2:, 1:-1] + field[..., :-2, 1:-1] - 2.0 * centre
    lon_term = field[..., 1:-1, 2:] + field[..., 1:-1, :-2] - 2.0 * centre
    radial = padded[..., 2:, :, :] + padded[..., :-2, :, :] - 2.0 * centre
    return lat_term + row_gain[:, None] * lon_term + radial


def diverge(velocity, inv_sine):
    radial_pad = jnp.pad(velocity[0, :, 1:-1, 1:-1], ((1, 1), (0, 0), (0, 0)))
    lat_part = velocity[1, :, 2:, 1:-1] - velocity[1, :, :-2, 1:-1]
    lon_part = velocity[2, :, 1:-1, 2:] - velocity[2, :, 1:-1, :-2]
    rad_part = radial_pad[2:] - radial_pad[:-2]
    return 0.5 * (lat_part + inv_sine[:, None] * lon_part + rad_part)


def gradient(pressure, inv_sine):
    radial_pad = jnp.pad(pressure[:, 1:-1, 1:-1], ((1, 1), (0, 0), (0, 0)))
    grad_rad = 0.5 * (radial_pad[2:] - radial_pad[:-2])
    grad_lat = 0.5 * (pressure[:, 2:, 1:-1] - pressure[:, :-2, 1:-1])
    grad_lon = 0.5 * inv_sine[:, None] * (pressure[:, 1:-1, 2:] - pressure[:, 1:-1, :-2])
    return (grad_rad, grad_lat, grad_lon)


def cosine_table(length):
    mode_ids = jnp.arange(length, dtype=jnp.float32)
    cell_mid = jnp.arange(length, dtype=jnp.float32) + 0.5
    row_norm = jnp.sqrt(jnp.where(mode_ids > 0, 2.0, 1.0) / length)
    cos_table = row_norm[:, None] * jnp.cos(
        math.pi * mode_ids[:, None] * cell_mid[None, :] / length
    )
    eigenvalue = 4.0 * jnp.sin(math.pi * mode_ids / (2.0 * length)) ** 2
    return (cos_table, eigenvalue)


def coarse_divisor(levels, n_lat, n_lon):
    eig_rad = cosine_table(levels)[1]
    eig_lat = cosine_table(n_lat)[1]
    eig_lon = cosine_table(n_lon)[1]
    return (
        eig_rad[:, None, None]
        + eig_lat[None, :, None]
        + eig_lon[None, None, :]
        + 1.0 / (n_lat * n_lon)
    )


def coarse_solve(block_sum, n_lat, n_lon):
    highest = lax.Precision.HIGHEST
    tab_rad = cosine_table(block_sum.shape[0])[0]
    tab_lat = cosine_table(n_lat)[0]
    tab_lon = cosine_table(n_lon)[0]
    spectrum = jnp.einsum("kr,rlo->klo", tab_rad, block_sum, precision=highest)
    spectrum = jnp.einsum("kl,rlo->rko", tab_lat, spectrum, precision=highest)
    spectrum = jnp.einsum("ko,rlo->rlk", tab_lon, spectrum, precision=highest)
    spectrum = spectrum / coarse_divisor(block_sum.shape[0], n_lat, n_lon)
    restored = jnp.einsum("kr,klo->rlo", tab_rad, spectrum, precision=highest)
    restored = jnp.einsum("kl,rko->rlo", tab_lat, restored, precision=highest)
    restored = jnp.einsum("ko,rlk->rlo", tab_lon, restored, precision=highest)
    return restored / math.sqrt(n_lat * n_lon)


def fractions(weight_ids):
    frac_lat = ((weight_ids // WQ).astype(jnp.float32) + 0.5) / WQ
    frac_lon = ((weight_ids % WQ).astype(jnp.float32) + 0.5) / WQ
    return (frac_lat, frac_lon)


def bilinear(lower_left, lower_right, upper_left, upper_right, frac_lat, frac_lon):
    return (
        (1.0 - frac_lat) * (1.0 - frac_lon) * lower_left
        + (1.0 - frac_lat) * frac_lon * lower_right
        + frac_lat * (1.0 - frac_lon) * upper_left
        + frac_lat * frac_lon * upper_right
    )


def shards(fields, viscosity, partner, src_row, src_col, weight_id, border_angle, dest_cell):
    n_lat = lax.axis_size("lat")
    n_lon = lax.axis_size("lon")
    lat_pos = lax.axis_index("lat")
    lon_pos = lax.axis_index("lon")
    own_fields = fields[0]
    levels, rows_dev, cols_dev = (own_fields.shape[1], own_fields.shape[2], own_fields.shape[3])
    channels = 6 * levels
    blocks = partner.shape[2]
    block_cells = src_row.shape[2] // blocks
    capacity = CAP
    slot_count = n_lon * capacity
    total_rows = rows_dev * n_lat
    flat_cells = own_fields.reshape(channels, rows_dev * cols_dev)
    target = partner[0, 0, :, 0]
    onehot = (target[:, None] == jnp.arange(n_lon, dtype=jnp.int32)[None, :]).astype(jnp.int32)
    before = jnp.sum(
        (jnp.cumsum(onehot, axis=0, dtype=jnp.int32) - onehot) * onehot, axis=1, dtype=jnp.int32
    )
    slot_of = target * capacity + before
    base_cell = (src_row[0, 0] * cols_dev + src_col[0, 0]).reshape(blocks, block_cells)
    weight_ids = weight_id[0, 0].reshape(blocks, block_cells)
    empty = jnp.zeros((slot_count, block_cells), jnp.int32)
    asked = jnp.stack(
        [empty.at[slot_of].set(base_cell), empty.at[slot_of].set(weight_ids)], axis=1
    ).reshape(n_lon, capacity, 2, block_cells)
    requests = partner_2(asked, "panel", 0)
    requests = lax.all_to_all(requests, "lon", split_axis=0, concat_axis=0, tiled=True)
    cells_asked = requests[:, :, 0, :]
    frac_lat, frac_lon = fractions(requests[:, :, 1, :])
    corners = [
        jnp.take(flat_cells, cells_asked + offset, axis=1)
        for offset in (0, 1, cols_dev, cols_dev + 1)
    ]
    served = bilinear(*corners, frac_lat, frac_lon)
    served = lax.all_to_all(served, "lon", split_axis=1, concat_axis=1, tiled=True)
    served = partner_2(served, "panel", 0)
    values = served.reshape(channels, slot_count, block_cells)[:, slot_of, :]
    values = values.reshape(6, levels, blocks * block_cells)
    turn = border_angle[0, 0]
    cos_angle = jnp.cos(turn)
    sin_angle = jnp.sin(turn)
    rotated = jnp.stack(
        [
            values[0],
            cos_angle * values[1] + sin_angle * values[2],
            cos_angle * values[2] - sin_angle * values[1],
            values[3],
            cos_angle * values[4] + sin_angle * values[5],
            cos_angle * values[5] - sin_angle * values[4],
        ],
        axis=0,
    ).reshape(channels, blocks * block_cells)
    filled = flat_cells.at[:, dest_cell[0, 0]].set(rotated).reshape(6, levels, rows_dev, cols_dev)
    diffusivity = viscosity[0]
    inv_own, gain_own = metric(
        lat_pos * rows_dev + jnp.arange(-0, rows_dev + 0, dtype=jnp.int32), total_rows
    )
    widened = padded_2(filled, (("lat", 2), ("lon", 3)), 1)
    stepped = filled + diffusivity[None] * lap_shrink(widened, gain_own)
    stepped = jnp.concatenate([stepped[0:1] + BUOYANCY * filled[3:4], stepped[1:]], axis=0)
    velocity = padded_2(stepped[0:3], (("lat", 2), ("lon", 3)), 1)
    divergence = diverge(velocity, inv_own)
    press_one = -divergence / (4.0 + 2.0 * gain_own)[:, None]
    press_wide = padded_2(press_one, (("lat", 1), ("lon", 2)), 1)
    resid_one = -divergence + lap_shrink(press_wide, gain_own)
    block_sum = jnp.sum(resid_one, axis=(1, 2)) * (1.0 / math.sqrt(rows_dev * cols_dev))
    gathered = doubling_gather(block_sum[None], "lon")
    gathered = doubling_gather(gathered[None], "lat")
    coarse = coarse_solve(jnp.transpose(gathered, (2, 0, 1)), n_lat, n_lon)
    start = jnp.zeros((), jnp.int32)
    near = lax.dynamic_slice(
        jnp.pad(coarse, ((0, 0), (1, 1), (1, 1))), (start, lat_pos, lon_pos), (levels, 3, 3)
    )
    own_coarse = near[:, 1, 1]
    pressure = press_one + own_coarse[:, None, None]
    row_at = lax.broadcasted_iota(jnp.int32, (rows_dev + 2, cols_dev + 2), 0)
    col_at = lax.broadcasted_iota(jnp.int32, (rows_dev + 2, cols_dev + 2), 1)
    rim_coarse = jnp.where(
        row_at == 0,
        near[:, 0, 1][:, None, None],
        jnp.where(
            row_at == rows_dev + 1,
            near[:, 2, 1][:, None, None],
            jnp.where(
                col_at == 0,
                near[:, 1, 0][:, None, None],
                jnp.where(
                    col_at == cols_dev + 1, near[:, 1, 2][:, None, None], own_coarse[:, None, None]
                ),
            ),
        ),
    )
    press_rim = press_wide + rim_coarse
    grad_rad, grad_lat, grad_lon = gradient(press_rim, inv_own)
    result = jnp.stack(
        [
            stepped[0] - grad_rad,
            stepped[1] - grad_lat,
            stepped[2] - grad_lon,
            stepped[3],
            stepped[4],
            stepped[5],
        ],
        axis=0,
    )
    return (result[None], pressure[None])


def solution(mesh):
    return jax.shard_map(
        shards,
        mesh=mesh,
        in_specs=(
            P("panel", None, None, "lat", "lon"),
            P("panel", None, "lat", "lon"),
            P("panel", "lat", "lon", None),
            P("panel", "lat", "lon"),
            P("panel", "lat", "lon"),
            P("panel", "lat", "lon"),
            P("panel", "lat", "lon"),
            P("panel", "lat", "lon"),
        ),
        out_specs=(P("panel", None, None, "lat", "lon"), P("panel", None, "lat", "lon")),
        check_vma=False,
    )
```

```python
import math

import jax
import jax.numpy as jnp
from jax import lax
from jax.sharding import PartitionSpec as P

CAP = 2
WQ = 8


BUOYANCY = 0.5


def partner_2(block, axis, apart):
    count = lax.axis_size(axis)
    route = []
    for low in range(count):
        high = low | 1 << apart
        if high != low and high < count:
            route += [(low, high), (high, low)]
    return lax.ppermute(block, axis, route)


def padded_2(shard, sides, width):
    for axis, dim in sides:
        size, length = (lax.axis_size(axis), shard.shape[dim])
        up = [(i, (i + 1) % size) for i in range(size - 1)]
        down = [(j, i) for i, j in up]
        last = lax.slice_in_dim(shard, length - width, length, axis=dim)
        leading = lax.slice_in_dim(shard, 0, width, axis=dim)
        before = lax.ppermute(last, axis, up)
        after = lax.ppermute(leading, axis, down)
        shard = jnp.concatenate([before, shard, after], axis=dim)
    return shard


def doubling_gather(block, axis):
    count = lax.axis_size(axis)
    index = lax.axis_index(axis)
    step = 1
    while step < count:
        other = lax.ppermute(block, axis, [(i, i ^ step) for i in range(count)])
        low = (index & step) == 0
        block = jnp.where(
            low, jnp.concatenate([block, other], 0), jnp.concatenate([other, block], 0)
        )
        step *= 2
    return block


def metric(row_index, total_rows):
    colatitude = (
        math.pi / 4.0 + (row_index.astype(jnp.float32) + 0.5) * (math.pi / 2.0) / total_rows
    )
    inv_sine = 1.0 / jnp.sin(colatitude)
    return (inv_sine, inv_sine * inv_sine)


def lap_shrink(field, row_gain):
    centre = field[..., 1:-1, 1:-1]
    padded = jnp.pad(centre, [(0, 0)] * (centre.ndim - 3) + [(1, 1), (0, 0), (0, 0)])
    lat_term = field[..., 2:, 1:-1] + field[..., :-2, 1:-1] - 2.0 * centre
    lon_term = field[..., 1:-1, 2:] + field[..., 1:-1, :-2] - 2.0 * centre
    radial = padded[..., 2:, :, :] + padded[..., :-2, :, :] - 2.0 * centre
    return lat_term + row_gain[:, None] * lon_term + radial


def diverge(velocity, inv_sine):
    radial_pad = jnp.pad(velocity[0, :, 1:-1, 1:-1], ((1, 1), (0, 0), (0, 0)))
    lat_part = velocity[1, :, 2:, 1:-1] - velocity[1, :, :-2, 1:-1]
    lon_part = velocity[2, :, 1:-1, 2:] - velocity[2, :, 1:-1, :-2]
    rad_part = radial_pad[2:] - radial_pad[:-2]
    return 0.5 * (lat_part + inv_sine[:, None] * lon_part + rad_part)


def gradient(pressure, inv_sine):
    radial_pad = jnp.pad(pressure[:, 1:-1, 1:-1], ((1, 1), (0, 0), (0, 0)))
    grad_rad = 0.5 * (radial_pad[2:] - radial_pad[:-2])
    grad_lat = 0.5 * (pressure[:, 2:, 1:-1] - pressure[:, :-2, 1:-1])
    grad_lon = 0.5 * inv_sine[:, None] * (pressure[:, 1:-1, 2:] - pressure[:, 1:-1, :-2])
    return (grad_rad, grad_lat, grad_lon)


def cosine_table(length):
    mode_ids = jnp.arange(length, dtype=jnp.float32)
    cell_mid = jnp.arange(length, dtype=jnp.float32) + 0.5
    row_norm = jnp.sqrt(jnp.where(mode_ids > 0, 2.0, 1.0) / length)
    cos_table = row_norm[:, None] * jnp.cos(
        math.pi * mode_ids[:, None] * cell_mid[None, :] / length
    )
    eigenvalue = 4.0 * jnp.sin(math.pi * mode_ids / (2.0 * length)) ** 2
    return (cos_table, eigenvalue)


def coarse_divisor(levels, n_lat, n_lon):
    eig_rad = cosine_table(levels)[1]
    eig_lat = cosine_table(n_lat)[1]
    eig_lon = cosine_table(n_lon)[1]
    return (
        eig_rad[:, None, None]
        + eig_lat[None, :, None]
        + eig_lon[None, None, :]
        + 1.0 / (n_lat * n_lon)
    )


def coarse_solve(block_sum, n_lat, n_lon):
    highest = lax.Precision.HIGHEST
    tab_rad = cosine_table(block_sum.shape[0])[0]
    tab_lat = cosine_table(n_lat)[0]
    tab_lon = cosine_table(n_lon)[0]
    spectrum = jnp.einsum("kr,rlo->klo", tab_rad, block_sum, precision=highest)
    spectrum = jnp.einsum("kl,rlo->rko", tab_lat, spectrum, precision=highest)
    spectrum = jnp.einsum("ko,rlo->rlk", tab_lon, spectrum, precision=highest)
    spectrum = spectrum / coarse_divisor(block_sum.shape[0], n_lat, n_lon)
    restored = jnp.einsum("kr,klo->rlo", tab_rad, spectrum, precision=highest)
    restored = jnp.einsum("kl,rko->rlo", tab_lat, restored, precision=highest)
    restored = jnp.einsum("ko,rlk->rlo", tab_lon, restored, precision=highest)
    return restored / math.sqrt(n_lat * n_lon)


def fractions(weight_ids):
    frac_lat = ((weight_ids // WQ).astype(jnp.float32) + 0.5) / WQ
    frac_lon = ((weight_ids % WQ).astype(jnp.float32) + 0.5) / WQ
    return (frac_lat, frac_lon)


def bilinear(lower_left, lower_right, upper_left, upper_right, frac_lat, frac_lon):
    return (
        (1.0 - frac_lat) * (1.0 - frac_lon) * lower_left
        + (1.0 - frac_lat) * frac_lon * lower_right
        + frac_lat * (1.0 - frac_lon) * upper_left
        + frac_lat * frac_lon * upper_right
    )


def shards(fields, viscosity, partner, src_row, src_col, weight_id, border_angle, dest_cell):
    n_lat = lax.axis_size("lat")
    n_lon = lax.axis_size("lon")
    lat_pos = lax.axis_index("lat")
    lon_pos = lax.axis_index("lon")
    own_fields = fields[0]
    levels, rows_dev, cols_dev = (own_fields.shape[1], own_fields.shape[2], own_fields.shape[3])
    channels = 6 * levels
    blocks = partner.shape[2]
    block_cells = src_row.shape[2] // blocks
    capacity = CAP
    slot_count = n_lon * capacity
    total_rows = rows_dev * n_lat
    flat_cells = own_fields.reshape(channels, rows_dev * cols_dev)
    target = partner[0, 0, :, 0]
    onehot = (target[:, None] == jnp.arange(n_lon, dtype=jnp.int32)[None, :]).astype(jnp.int32)
    before = jnp.sum(
        (jnp.cumsum(onehot, axis=0, dtype=jnp.int32) - onehot) * onehot, axis=1, dtype=jnp.int32
    )
    slot_of = target * capacity + before
    base_cell = (src_row[0, 0] * cols_dev + src_col[0, 0]).reshape(blocks, block_cells)
    weight_ids = weight_id[0, 0].reshape(blocks, block_cells)
    empty = jnp.zeros((slot_count, block_cells), jnp.int32)
    asked = jnp.stack(
        [empty.at[slot_of].set(base_cell), empty.at[slot_of].set(weight_ids)], axis=1
    ).reshape(n_lon, capacity, 2, block_cells)
    requests = partner_2(asked, "panel", 0)
    requests = lax.all_to_all(requests, "lon", split_axis=0, concat_axis=0, tiled=True)
    cells_asked = requests[:, :, 0, :]
    frac_lat, frac_lon = fractions(requests[:, :, 1, :])
    corners = [
        jnp.take(flat_cells, cells_asked + offset, axis=1)
        for offset in (0, 1, cols_dev, cols_dev + 1)
    ]
    served = bilinear(*corners, frac_lat, frac_lon)
    served = lax.all_to_all(served, "lon", split_axis=1, concat_axis=1, tiled=True)
    served = partner_2(served, "panel", 0)
    values = served.reshape(channels, slot_count, block_cells)[:, slot_of, :]
    values = values.reshape(6, levels, blocks * block_cells)
    turn = border_angle[0, 0]
    cos_angle = jnp.cos(turn)
    sin_angle = jnp.sin(turn)
    rotated = jnp.stack(
        [
            values[0],
            cos_angle * values[1] + sin_angle * values[2],
            cos_angle * values[2] - sin_angle * values[1],
            values[3],
            cos_angle * values[4] + sin_angle * values[5],
            cos_angle * values[5] - sin_angle * values[4],
        ],
        axis=0,
    ).reshape(channels, blocks * block_cells)
    filled = flat_cells.at[:, dest_cell[0, 0]].set(rotated).reshape(6, levels, rows_dev, cols_dev)
    diffusivity = viscosity[0]
    inv_own, gain_own = metric(
        lat_pos * rows_dev + jnp.arange(-0, rows_dev + 0, dtype=jnp.int32), total_rows
    )
    halo = 3
    total_cols = cols_dev * n_lon
    row_first = lat_pos * rows_dev
    col_first = lon_pos * cols_dev

    def inside(reach):
        rows = row_first - reach + jnp.arange(rows_dev + 2 * reach, dtype=jnp.int32)
        cols = col_first - reach + jnp.arange(cols_dev + 2 * reach, dtype=jnp.int32)
        return ((rows >= 0) & (rows < total_rows))[:, None] & ((cols >= 0) & (cols < total_cols))[
            None, :
        ]

    stack = jnp.concatenate([filled.reshape(channels, rows_dev, cols_dev), diffusivity], axis=0)
    wide = padded_2(stack, (("lat", 1), ("lon", 2)), halo)
    wide_fields = wide[:channels].reshape(6, levels, rows_dev + 2 * halo, cols_dev + 2 * halo)
    wide_visc = wide[channels:]
    inv_two, gain_two = metric(row_first + jnp.arange(-2, rows_dev + 2, dtype=jnp.int32), total_rows)
    inv_one, gain_one = metric(row_first + jnp.arange(-1, rows_dev + 1, dtype=jnp.int32), total_rows)
    centre = wide_fields[..., 1:-1, 1:-1]
    stepped_wide = centre + wide_visc[None, :, 1:-1, 1:-1] * lap_shrink(wide_fields, gain_two)
    stepped_wide = jnp.concatenate(
        [stepped_wide[0:1] + BUOYANCY * centre[3:4], stepped_wide[1:]], axis=0
    )
    velocity = jnp.where(inside(2), stepped_wide[0:3], 0.0)
    divergence_wide = diverge(velocity, inv_one)
    press_wide = jnp.where(inside(1), -divergence_wide / (4.0 + 2.0 * gain_one)[:, None], 0.0)
    divergence = divergence_wide[:, 1:-1, 1:-1]
    press_one = press_wide[:, 1:-1, 1:-1]
    stepped = stepped_wide[:, :, 2:-2, 2:-2]
    resid_one = -divergence + lap_shrink(press_wide, gain_own)
    block_sum = jnp.sum(resid_one, axis=(1, 2)) * (1.0 / math.sqrt(rows_dev * cols_dev))
    gathered = doubling_gather(block_sum[None], "lon")
    gathered = doubling_gather(gathered[None], "lat")
    coarse = coarse_solve(jnp.transpose(gathered, (2, 0, 1)), n_lat, n_lon)
    start = jnp.zeros((), jnp.int32)
    near = lax.dynamic_slice(
        jnp.pad(coarse, ((0, 0), (1, 1), (1, 1))), (start, lat_pos, lon_pos), (levels, 3, 3)
    )
    own_coarse = near[:, 1, 1]
    pressure = press_one + own_coarse[:, None, None]
    row_at = lax.broadcasted_iota(jnp.int32, (rows_dev + 2, cols_dev + 2), 0)
    col_at = lax.broadcasted_iota(jnp.int32, (rows_dev + 2, cols_dev + 2), 1)
    rim_coarse = jnp.where(
        row_at == 0,
        near[:, 0, 1][:, None, None],
        jnp.where(
            row_at == rows_dev + 1,
            near[:, 2, 1][:, None, None],
            jnp.where(
                col_at == 0,
                near[:, 1, 0][:, None, None],
                jnp.where(
                    col_at == cols_dev + 1, near[:, 1, 2][:, None, None], own_coarse[:, None, None]
                ),
            ),
        ),
    )
    press_rim = press_wide + rim_coarse
    grad_rad, grad_lat, grad_lon = gradient(press_rim, inv_own)
    result = jnp.stack(
        [
            stepped[0] - grad_rad,
            stepped[1] - grad_lat,
            stepped[2] - grad_lon,
            stepped[3],
            stepped[4],
            stepped[5],
        ],
        axis=0,
    )
    return (result[None], pressure[None])


def solution(mesh):
    return jax.shard_map(
        shards,
        mesh=mesh,
        in_specs=(
            P("panel", None, None, "lat", "lon"),
            P("panel", None, "lat", "lon"),
            P("panel", "lat", "lon", None),
            P("panel", "lat", "lon"),
            P("panel", "lat", "lon"),
            P("panel", "lat", "lon"),
            P("panel", "lat", "lon"),
            P("panel", "lat", "lon"),
        ),
        out_specs=(P("panel", None, None, "lat", "lon"), P("panel", None, "lat", "lon")),
        check_vma=False,
    )
```

```python
import math

import jax
import jax.numpy as jnp
from jax import lax
from jax.experimental import pallas as pl
from jax.experimental.pallas import tpu as pltpu
from jax.sharding import PartitionSpec as P

CAP = 2
WQ = 8


BUOYANCY = 0.5


def partner_2(block, axis, apart):
    count = lax.axis_size(axis)
    route = []
    for low in range(count):
        high = low | 1 << apart
        if high != low and high < count:
            route += [(low, high), (high, low)]
    return lax.ppermute(block, axis, route)


def padded_2(shard, sides, width):
    for axis, dim in sides:
        size, length = (lax.axis_size(axis), shard.shape[dim])
        up = [(i, (i + 1) % size) for i in range(size - 1)]
        down = [(j, i) for i, j in up]
        last = lax.slice_in_dim(shard, length - width, length, axis=dim)
        leading = lax.slice_in_dim(shard, 0, width, axis=dim)
        before = lax.ppermute(last, axis, up)
        after = lax.ppermute(leading, axis, down)
        shard = jnp.concatenate([before, shard, after], axis=dim)
    return shard


def doubling_gather(block, axis):
    count = lax.axis_size(axis)
    index = lax.axis_index(axis)
    step = 1
    while step < count:
        other = lax.ppermute(block, axis, [(i, i ^ step) for i in range(count)])
        low = (index & step) == 0
        block = jnp.where(
            low, jnp.concatenate([block, other], 0), jnp.concatenate([other, block], 0)
        )
        step *= 2
    return block


def corner_gather(table, rows, width):
    count = rows.shape[0]

    def kernel(rows_ref, table_ref, out_ref):
        def body(t, carry):
            at = rows_ref[t]
            for k, offset in enumerate((0, 1, width, width + 1)):
                out_ref[k, pl.ds(t, 1), :] = table_ref[pl.ds(at + offset, 1), :]
            return carry

        lax.fori_loop(0, count, body, 0, unroll=16)

    return pl.pallas_call(
        kernel,
        out_shape=jax.ShapeDtypeStruct((4, count, table.shape[1]), table.dtype),
        in_specs=[pl.BlockSpec(memory_space=pltpu.SMEM), pl.BlockSpec(memory_space=pltpu.VMEM)],
        out_specs=pl.BlockSpec(memory_space=pltpu.VMEM),
    )(rows, table)


def metric(row_index, total_rows):
    colatitude = (
        math.pi / 4.0 + (row_index.astype(jnp.float32) + 0.5) * (math.pi / 2.0) / total_rows
    )
    inv_sine = 1.0 / jnp.sin(colatitude)
    return (inv_sine, inv_sine * inv_sine)


def lap_shrink(field, row_gain):
    centre = field[..., 1:-1, 1:-1]
    padded = jnp.pad(centre, [(0, 0)] * (centre.ndim - 3) + [(1, 1), (0, 0), (0, 0)])
    lat_term = field[..., 2:, 1:-1] + field[..., :-2, 1:-1] - 2.0 * centre
    lon_term = field[..., 1:-1, 2:] + field[..., 1:-1, :-2] - 2.0 * centre
    radial = padded[..., 2:, :, :] + padded[..., :-2, :, :] - 2.0 * centre
    return lat_term + row_gain[:, None] * lon_term + radial


def diverge(velocity, inv_sine):
    radial_pad = jnp.pad(velocity[0, :, 1:-1, 1:-1], ((1, 1), (0, 0), (0, 0)))
    lat_part = velocity[1, :, 2:, 1:-1] - velocity[1, :, :-2, 1:-1]
    lon_part = velocity[2, :, 1:-1, 2:] - velocity[2, :, 1:-1, :-2]
    rad_part = radial_pad[2:] - radial_pad[:-2]
    return 0.5 * (lat_part + inv_sine[:, None] * lon_part + rad_part)


def gradient(pressure, inv_sine):
    radial_pad = jnp.pad(pressure[:, 1:-1, 1:-1], ((1, 1), (0, 0), (0, 0)))
    grad_rad = 0.5 * (radial_pad[2:] - radial_pad[:-2])
    grad_lat = 0.5 * (pressure[:, 2:, 1:-1] - pressure[:, :-2, 1:-1])
    grad_lon = 0.5 * inv_sine[:, None] * (pressure[:, 1:-1, 2:] - pressure[:, 1:-1, :-2])
    return (grad_rad, grad_lat, grad_lon)


def cosine_table(length):
    mode_ids = jnp.arange(length, dtype=jnp.float32)
    cell_mid = jnp.arange(length, dtype=jnp.float32) + 0.5
    row_norm = jnp.sqrt(jnp.where(mode_ids > 0, 2.0, 1.0) / length)
    cos_table = row_norm[:, None] * jnp.cos(
        math.pi * mode_ids[:, None] * cell_mid[None, :] / length
    )
    eigenvalue = 4.0 * jnp.sin(math.pi * mode_ids / (2.0 * length)) ** 2
    return (cos_table, eigenvalue)


def coarse_divisor(levels, n_lat, n_lon):
    eig_rad = cosine_table(levels)[1]
    eig_lat = cosine_table(n_lat)[1]
    eig_lon = cosine_table(n_lon)[1]
    return (
        eig_rad[:, None, None]
        + eig_lat[None, :, None]
        + eig_lon[None, None, :]
        + 1.0 / (n_lat * n_lon)
    )


def coarse_solve(block_sum, n_lat, n_lon):
    highest = lax.Precision.HIGHEST
    tab_rad = cosine_table(block_sum.shape[0])[0]
    tab_lat = cosine_table(n_lat)[0]
    tab_lon = cosine_table(n_lon)[0]
    spectrum = jnp.einsum("kr,rlo->klo", tab_rad, block_sum, precision=highest)
    spectrum = jnp.einsum("kl,rlo->rko", tab_lat, spectrum, precision=highest)
    spectrum = jnp.einsum("ko,rlo->rlk", tab_lon, spectrum, precision=highest)
    spectrum = spectrum / coarse_divisor(block_sum.shape[0], n_lat, n_lon)
    restored = jnp.einsum("kr,klo->rlo", tab_rad, spectrum, precision=highest)
    restored = jnp.einsum("kl,rko->rlo", tab_lat, restored, precision=highest)
    restored = jnp.einsum("ko,rlk->rlo", tab_lon, restored, precision=highest)
    return restored / math.sqrt(n_lat * n_lon)


def fractions(weight_ids):
    frac_lat = ((weight_ids // WQ).astype(jnp.float32) + 0.5) / WQ
    frac_lon = ((weight_ids % WQ).astype(jnp.float32) + 0.5) / WQ
    return (frac_lat, frac_lon)


def bilinear(lower_left, lower_right, upper_left, upper_right, frac_lat, frac_lon):
    return (
        (1.0 - frac_lat) * (1.0 - frac_lon) * lower_left
        + (1.0 - frac_lat) * frac_lon * lower_right
        + frac_lat * (1.0 - frac_lon) * upper_left
        + frac_lat * frac_lon * upper_right
    )


def shards(fields, viscosity, partner, src_row, src_col, weight_id, border_angle, dest_cell):
    n_lat = lax.axis_size("lat")
    n_lon = lax.axis_size("lon")
    lat_pos = lax.axis_index("lat")
    lon_pos = lax.axis_index("lon")
    own_fields = fields[0]
    levels, rows_dev, cols_dev = (own_fields.shape[1], own_fields.shape[2], own_fields.shape[3])
    channels = 6 * levels
    blocks = partner.shape[2]
    block_cells = src_row.shape[2] // blocks
    capacity = CAP
    slot_count = n_lon * capacity
    total_rows = rows_dev * n_lat
    flat_cells = own_fields.reshape(channels, rows_dev * cols_dev)
    target = partner[0, 0, :, 0]
    onehot = (target[:, None] == jnp.arange(n_lon, dtype=jnp.int32)[None, :]).astype(jnp.int32)
    before = jnp.sum(
        (jnp.cumsum(onehot, axis=0, dtype=jnp.int32) - onehot) * onehot, axis=1, dtype=jnp.int32
    )
    slot_of = target * capacity + before
    base_cell = (src_row[0, 0] * cols_dev + src_col[0, 0]).reshape(blocks, block_cells)
    weight_ids = weight_id[0, 0].reshape(blocks, block_cells)
    empty = jnp.zeros((slot_count, block_cells), jnp.int32)
    asked = jnp.stack(
        [empty.at[slot_of].set(base_cell), empty.at[slot_of].set(weight_ids)], axis=1
    ).reshape(n_lon, capacity, 2, block_cells)
    requests = partner_2(asked, "panel", 0)
    requests = lax.all_to_all(requests, "lon", split_axis=0, concat_axis=0, tiled=True)
    cells_asked = requests[:, :, 0, :].reshape(-1)
    frac_lat, frac_lon = fractions(requests[:, :, 1, :].reshape(-1, 1))
    corners = corner_gather(flat_cells.T, cells_asked, cols_dev)
    served = bilinear(corners[0], corners[1], corners[2], corners[3], frac_lat, frac_lon)
    served = served.reshape(n_lon, capacity, block_cells, channels)
    served = lax.all_to_all(served, "lon", split_axis=0, concat_axis=0, tiled=True)
    served = partner_2(served, "panel", 0)
    values = served.reshape(slot_count, block_cells, channels)[slot_of]
    values = values.reshape(blocks * block_cells, channels).T.reshape(6, levels, blocks * block_cells)
    turn = border_angle[0, 0]
    cos_angle = jnp.cos(turn)
    sin_angle = jnp.sin(turn)
    rotated = jnp.stack(
        [
            values[0],
            cos_angle * values[1] + sin_angle * values[2],
            cos_angle * values[2] - sin_angle * values[1],
            values[3],
            cos_angle * values[4] + sin_angle * values[5],
            cos_angle * values[5] - sin_angle * values[4],
        ],
        axis=0,
    ).reshape(channels, blocks * block_cells)
    filled = flat_cells.at[:, dest_cell[0, 0]].set(rotated).reshape(6, levels, rows_dev, cols_dev)
    diffusivity = viscosity[0]
    inv_own, gain_own = metric(
        lat_pos * rows_dev + jnp.arange(-0, rows_dev + 0, dtype=jnp.int32), total_rows
    )
    halo = 3
    total_cols = cols_dev * n_lon
    row_first = lat_pos * rows_dev
    col_first = lon_pos * cols_dev

    def inside(reach):
        rows = row_first - reach + jnp.arange(rows_dev + 2 * reach, dtype=jnp.int32)
        cols = col_first - reach + jnp.arange(cols_dev + 2 * reach, dtype=jnp.int32)
        return ((rows >= 0) & (rows < total_rows))[:, None] & ((cols >= 0) & (cols < total_cols))[
            None, :
        ]

    stack = jnp.concatenate([filled.reshape(channels, rows_dev, cols_dev), diffusivity], axis=0)
    wide = padded_2(stack, (("lat", 1), ("lon", 2)), halo)
    wide_fields = wide[:channels].reshape(6, levels, rows_dev + 2 * halo, cols_dev + 2 * halo)
    wide_visc = wide[channels:]
    inv_two, gain_two = metric(row_first + jnp.arange(-2, rows_dev + 2, dtype=jnp.int32), total_rows)
    inv_one, gain_one = metric(row_first + jnp.arange(-1, rows_dev + 1, dtype=jnp.int32), total_rows)
    centre = wide_fields[..., 1:-1, 1:-1]
    stepped_wide = centre + wide_visc[None, :, 1:-1, 1:-1] * lap_shrink(wide_fields, gain_two)
    stepped_wide = jnp.concatenate(
        [stepped_wide[0:1] + BUOYANCY * centre[3:4], stepped_wide[1:]], axis=0
    )
    velocity = jnp.where(inside(2), stepped_wide[0:3], 0.0)
    divergence_wide = diverge(velocity, inv_one)
    press_wide = jnp.where(inside(1), -divergence_wide / (4.0 + 2.0 * gain_one)[:, None], 0.0)
    divergence = divergence_wide[:, 1:-1, 1:-1]
    press_one = press_wide[:, 1:-1, 1:-1]
    stepped = stepped_wide[:, :, 2:-2, 2:-2]
    resid_one = -divergence + lap_shrink(press_wide, gain_own)
    block_sum = jnp.sum(resid_one, axis=(1, 2)) * (1.0 / math.sqrt(rows_dev * cols_dev))
    gathered = doubling_gather(block_sum[None], "lon")
    gathered = doubling_gather(gathered[None], "lat")
    coarse = coarse_solve(jnp.transpose(gathered, (2, 0, 1)), n_lat, n_lon)
    start = jnp.zeros((), jnp.int32)
    near = lax.dynamic_slice(
        jnp.pad(coarse, ((0, 0), (1, 1), (1, 1))), (start, lat_pos, lon_pos), (levels, 3, 3)
    )
    own_coarse = near[:, 1, 1]
    pressure = press_one + own_coarse[:, None, None]
    row_at = lax.broadcasted_iota(jnp.int32, (rows_dev + 2, cols_dev + 2), 0)
    col_at = lax.broadcasted_iota(jnp.int32, (rows_dev + 2, cols_dev + 2), 1)
    rim_coarse = jnp.where(
        row_at == 0,
        near[:, 0, 1][:, None, None],
        jnp.where(
            row_at == rows_dev + 1,
            near[:, 2, 1][:, None, None],
            jnp.where(
                col_at == 0,
                near[:, 1, 0][:, None, None],
                jnp.where(
                    col_at == cols_dev + 1, near[:, 1, 2][:, None, None], own_coarse[:, None, None]
                ),
            ),
        ),
    )
    press_rim = press_wide + rim_coarse
    grad_rad, grad_lat, grad_lon = gradient(press_rim, inv_own)
    result = jnp.stack(
        [
            stepped[0] - grad_rad,
            stepped[1] - grad_lat,
            stepped[2] - grad_lon,
            stepped[3],
            stepped[4],
            stepped[5],
        ],
        axis=0,
    )
    return (result[None], pressure[None])


def solution(mesh):
    return jax.shard_map(
        shards,
        mesh=mesh,
        in_specs=(
            P("panel", None, None, "lat", "lon"),
            P("panel", None, "lat", "lon"),
            P("panel", "lat", "lon", None),
            P("panel", "lat", "lon"),
            P("panel", "lat", "lon"),
            P("panel", "lat", "lon"),
            P("panel", "lat", "lon"),
            P("panel", "lat", "lon"),
        ),
        out_specs=(P("panel", None, None, "lat", "lon"), P("panel", None, "lat", "lon")),
        check_vma=False,
    )
```

```python
import math

import jax
import jax.numpy as jnp
from jax import lax
from jax.experimental import pallas as pl
from jax.experimental.pallas import tpu as pltpu
from jax.sharding import PartitionSpec as P

CAP = 2
WQ = 8


BUOYANCY = 0.5


def partner_2(block, axis, apart):
    count = lax.axis_size(axis)
    route = []
    for low in range(count):
        high = low | 1 << apart
        if high != low and high < count:
            route += [(low, high), (high, low)]
    return lax.ppermute(block, axis, route)


def padded_2(shard, sides, width):
    for axis, dim in sides:
        size, length = (lax.axis_size(axis), shard.shape[dim])
        up = [(i, (i + 1) % size) for i in range(size - 1)]
        down = [(j, i) for i, j in up]
        last = lax.slice_in_dim(shard, length - width, length, axis=dim)
        leading = lax.slice_in_dim(shard, 0, width, axis=dim)
        before = lax.ppermute(last, axis, up)
        after = lax.ppermute(leading, axis, down)
        shard = jnp.concatenate([before, shard, after], axis=dim)
    return shard


def doubling_gather(block, axis):
    count = lax.axis_size(axis)
    index = lax.axis_index(axis)
    step = 1
    while step < count:
        other = lax.ppermute(block, axis, [(i, i ^ step) for i in range(count)])
        low = (index & step) == 0
        block = jnp.where(
            low, jnp.concatenate([block, other], 0), jnp.concatenate([other, block], 0)
        )
        step *= 2
    return block


def corner_blend(table, rows, weights, width):
    count = rows.shape[0]

    def kernel(rows_ref, weights_ref, table_ref, out_ref):
        def body(t, carry):
            at = rows_ref[t]
            total = weights_ref[0, t] * table_ref[pl.ds(at, 1), :]
            for k, offset in enumerate((1, width, width + 1)):
                total = total + weights_ref[k + 1, t] * table_ref[pl.ds(at + offset, 1), :]
            out_ref[pl.ds(t, 1), :] = total
            return carry

        lax.fori_loop(0, count, body, 0, unroll=16)

    return pl.pallas_call(
        kernel,
        out_shape=jax.ShapeDtypeStruct((count, table.shape[1]), table.dtype),
        in_specs=[
            pl.BlockSpec(memory_space=pltpu.SMEM),
            pl.BlockSpec(memory_space=pltpu.SMEM),
            pl.BlockSpec(memory_space=pltpu.VMEM),
        ],
        out_specs=pl.BlockSpec(memory_space=pltpu.VMEM),
    )(rows, weights, table)


def metric(row_index, total_rows):
    colatitude = (
        math.pi / 4.0 + (row_index.astype(jnp.float32) + 0.5) * (math.pi / 2.0) / total_rows
    )
    inv_sine = 1.0 / jnp.sin(colatitude)
    return (inv_sine, inv_sine * inv_sine)


def lap_shrink(field, row_gain):
    centre = field[..., 1:-1, 1:-1]
    padded = jnp.pad(centre, [(0, 0)] * (centre.ndim - 3) + [(1, 1), (0, 0), (0, 0)])
    lat_term = field[..., 2:, 1:-1] + field[..., :-2, 1:-1] - 2.0 * centre
    lon_term = field[..., 1:-1, 2:] + field[..., 1:-1, :-2] - 2.0 * centre
    radial = padded[..., 2:, :, :] + padded[..., :-2, :, :] - 2.0 * centre
    return lat_term + row_gain[:, None] * lon_term + radial


def diverge(velocity, inv_sine):
    radial_pad = jnp.pad(velocity[0, :, 1:-1, 1:-1], ((1, 1), (0, 0), (0, 0)))
    lat_part = velocity[1, :, 2:, 1:-1] - velocity[1, :, :-2, 1:-1]
    lon_part = velocity[2, :, 1:-1, 2:] - velocity[2, :, 1:-1, :-2]
    rad_part = radial_pad[2:] - radial_pad[:-2]
    return 0.5 * (lat_part + inv_sine[:, None] * lon_part + rad_part)


def gradient(pressure, inv_sine):
    radial_pad = jnp.pad(pressure[:, 1:-1, 1:-1], ((1, 1), (0, 0), (0, 0)))
    grad_rad = 0.5 * (radial_pad[2:] - radial_pad[:-2])
    grad_lat = 0.5 * (pressure[:, 2:, 1:-1] - pressure[:, :-2, 1:-1])
    grad_lon = 0.5 * inv_sine[:, None] * (pressure[:, 1:-1, 2:] - pressure[:, 1:-1, :-2])
    return (grad_rad, grad_lat, grad_lon)


def cosine_table(length):
    mode_ids = jnp.arange(length, dtype=jnp.float32)
    cell_mid = jnp.arange(length, dtype=jnp.float32) + 0.5
    row_norm = jnp.sqrt(jnp.where(mode_ids > 0, 2.0, 1.0) / length)
    cos_table = row_norm[:, None] * jnp.cos(
        math.pi * mode_ids[:, None] * cell_mid[None, :] / length
    )
    eigenvalue = 4.0 * jnp.sin(math.pi * mode_ids / (2.0 * length)) ** 2
    return (cos_table, eigenvalue)


def coarse_divisor(levels, n_lat, n_lon):
    eig_rad = cosine_table(levels)[1]
    eig_lat = cosine_table(n_lat)[1]
    eig_lon = cosine_table(n_lon)[1]
    return (
        eig_rad[:, None, None]
        + eig_lat[None, :, None]
        + eig_lon[None, None, :]
        + 1.0 / (n_lat * n_lon)
    )


def coarse_solve(block_sum, n_lat, n_lon):
    highest = lax.Precision.HIGHEST
    tab_rad = cosine_table(block_sum.shape[0])[0]
    tab_lat = cosine_table(n_lat)[0]
    tab_lon = cosine_table(n_lon)[0]
    spectrum = jnp.einsum("kr,rlo->klo", tab_rad, block_sum, precision=highest)
    spectrum = jnp.einsum("kl,rlo->rko", tab_lat, spectrum, precision=highest)
    spectrum = jnp.einsum("ko,rlo->rlk", tab_lon, spectrum, precision=highest)
    spectrum = spectrum / coarse_divisor(block_sum.shape[0], n_lat, n_lon)
    restored = jnp.einsum("kr,klo->rlo", tab_rad, spectrum, precision=highest)
    restored = jnp.einsum("kl,rko->rlo", tab_lat, restored, precision=highest)
    restored = jnp.einsum("ko,rlk->rlo", tab_lon, restored, precision=highest)
    return restored / math.sqrt(n_lat * n_lon)


def fractions(weight_ids):
    frac_lat = ((weight_ids // WQ).astype(jnp.float32) + 0.5) / WQ
    frac_lon = ((weight_ids % WQ).astype(jnp.float32) + 0.5) / WQ
    return (frac_lat, frac_lon)


def bilinear(lower_left, lower_right, upper_left, upper_right, frac_lat, frac_lon):
    return (
        (1.0 - frac_lat) * (1.0 - frac_lon) * lower_left
        + (1.0 - frac_lat) * frac_lon * lower_right
        + frac_lat * (1.0 - frac_lon) * upper_left
        + frac_lat * frac_lon * upper_right
    )


def shards(fields, viscosity, partner, src_row, src_col, weight_id, border_angle, dest_cell):
    n_lat = lax.axis_size("lat")
    n_lon = lax.axis_size("lon")
    lat_pos = lax.axis_index("lat")
    lon_pos = lax.axis_index("lon")
    own_fields = fields[0]
    levels, rows_dev, cols_dev = (own_fields.shape[1], own_fields.shape[2], own_fields.shape[3])
    channels = 6 * levels
    blocks = partner.shape[2]
    block_cells = src_row.shape[2] // blocks
    capacity = CAP
    slot_count = n_lon * capacity
    total_rows = rows_dev * n_lat
    flat_cells = own_fields.reshape(channels, rows_dev * cols_dev)
    target = partner[0, 0, :, 0]
    onehot = (target[:, None] == jnp.arange(n_lon, dtype=jnp.int32)[None, :]).astype(jnp.int32)
    before = jnp.sum(
        (jnp.cumsum(onehot, axis=0, dtype=jnp.int32) - onehot) * onehot, axis=1, dtype=jnp.int32
    )
    slot_of = target * capacity + before
    base_cell = (src_row[0, 0] * cols_dev + src_col[0, 0]).reshape(blocks, block_cells)
    weight_ids = weight_id[0, 0].reshape(blocks, block_cells)
    empty = jnp.zeros((slot_count, block_cells), jnp.int32)
    asked = jnp.stack(
        [empty.at[slot_of].set(base_cell), empty.at[slot_of].set(weight_ids)], axis=1
    ).reshape(n_lon, capacity, 2, block_cells)
    requests = partner_2(asked, "panel", 0)
    requests = lax.all_to_all(requests, "lon", split_axis=0, concat_axis=0, tiled=True)
    cells_asked = requests[:, :, 0, :].reshape(-1)
    frac_lat, frac_lon = fractions(requests[:, :, 1, :].reshape(-1))
    weights = jnp.stack(
        [
            (1.0 - frac_lat) * (1.0 - frac_lon),
            (1.0 - frac_lat) * frac_lon,
            frac_lat * (1.0 - frac_lon),
            frac_lat * frac_lon,
        ],
        axis=0,
    )
    served = corner_blend(flat_cells.T, cells_asked, weights, cols_dev)
    served = served.reshape(n_lon, capacity, block_cells, channels)
    served = lax.all_to_all(served, "lon", split_axis=0, concat_axis=0, tiled=True)
    served = partner_2(served, "panel", 0)
    values = served.reshape(slot_count, block_cells, channels)[slot_of]
    values = values.reshape(blocks * block_cells, channels).T.reshape(6, levels, blocks * block_cells)
    turn = border_angle[0, 0]
    cos_angle = jnp.cos(turn)
    sin_angle = jnp.sin(turn)
    rotated = jnp.stack(
        [
            values[0],
            cos_angle * values[1] + sin_angle * values[2],
            cos_angle * values[2] - sin_angle * values[1],
            values[3],
            cos_angle * values[4] + sin_angle * values[5],
            cos_angle * values[5] - sin_angle * values[4],
        ],
        axis=0,
    ).reshape(channels, blocks * block_cells)
    filled = flat_cells.at[:, dest_cell[0, 0]].set(rotated).reshape(6, levels, rows_dev, cols_dev)
    diffusivity = viscosity[0]
    inv_own, gain_own = metric(
        lat_pos * rows_dev + jnp.arange(-0, rows_dev + 0, dtype=jnp.int32), total_rows
    )
    halo = 3
    total_cols = cols_dev * n_lon
    row_first = lat_pos * rows_dev
    col_first = lon_pos * cols_dev

    def inside(reach):
        rows = row_first - reach + jnp.arange(rows_dev + 2 * reach, dtype=jnp.int32)
        cols = col_first - reach + jnp.arange(cols_dev + 2 * reach, dtype=jnp.int32)
        return ((rows >= 0) & (rows < total_rows))[:, None] & ((cols >= 0) & (cols < total_cols))[
            None, :
        ]

    stack = jnp.concatenate([filled.reshape(channels, rows_dev, cols_dev), diffusivity], axis=0)
    wide = padded_2(stack, (("lat", 1), ("lon", 2)), halo)
    wide_fields = wide[:channels].reshape(6, levels, rows_dev + 2 * halo, cols_dev + 2 * halo)
    wide_visc = wide[channels:]
    inv_two, gain_two = metric(row_first + jnp.arange(-2, rows_dev + 2, dtype=jnp.int32), total_rows)
    inv_one, gain_one = metric(row_first + jnp.arange(-1, rows_dev + 1, dtype=jnp.int32), total_rows)
    centre = wide_fields[..., 1:-1, 1:-1]
    stepped_wide = centre + wide_visc[None, :, 1:-1, 1:-1] * lap_shrink(wide_fields, gain_two)
    stepped_wide = jnp.concatenate(
        [stepped_wide[0:1] + BUOYANCY * centre[3:4], stepped_wide[1:]], axis=0
    )
    velocity = jnp.where(inside(2), stepped_wide[0:3], 0.0)
    divergence_wide = diverge(velocity, inv_one)
    press_wide = jnp.where(inside(1), -divergence_wide / (4.0 + 2.0 * gain_one)[:, None], 0.0)
    divergence = divergence_wide[:, 1:-1, 1:-1]
    press_one = press_wide[:, 1:-1, 1:-1]
    stepped = stepped_wide[:, :, 2:-2, 2:-2]
    resid_one = -divergence + lap_shrink(press_wide, gain_own)
    block_sum = jnp.sum(resid_one, axis=(1, 2)) * (1.0 / math.sqrt(rows_dev * cols_dev))
    gathered = doubling_gather(block_sum[None], "lon")
    gathered = doubling_gather(gathered[None], "lat")
    coarse = coarse_solve(jnp.transpose(gathered, (2, 0, 1)), n_lat, n_lon)
    start = jnp.zeros((), jnp.int32)
    near = lax.dynamic_slice(
        jnp.pad(coarse, ((0, 0), (1, 1), (1, 1))), (start, lat_pos, lon_pos), (levels, 3, 3)
    )
    own_coarse = near[:, 1, 1]
    pressure = press_one + own_coarse[:, None, None]
    row_at = lax.broadcasted_iota(jnp.int32, (rows_dev + 2, cols_dev + 2), 0)
    col_at = lax.broadcasted_iota(jnp.int32, (rows_dev + 2, cols_dev + 2), 1)
    rim_coarse = jnp.where(
        row_at == 0,
        near[:, 0, 1][:, None, None],
        jnp.where(
            row_at == rows_dev + 1,
            near[:, 2, 1][:, None, None],
            jnp.where(
                col_at == 0,
                near[:, 1, 0][:, None, None],
                jnp.where(
                    col_at == cols_dev + 1, near[:, 1, 2][:, None, None], own_coarse[:, None, None]
                ),
            ),
        ),
    )
    press_rim = press_wide + rim_coarse
    grad_rad, grad_lat, grad_lon = gradient(press_rim, inv_own)
    result = jnp.stack(
        [
            stepped[0] - grad_rad,
            stepped[1] - grad_lat,
            stepped[2] - grad_lon,
            stepped[3],
            stepped[4],
            stepped[5],
        ],
        axis=0,
    )
    return (result[None], pressure[None])


def solution(mesh):
    return jax.shard_map(
        shards,
        mesh=mesh,
        in_specs=(
            P("panel", None, None, "lat", "lon"),
            P("panel", None, "lat", "lon"),
            P("panel", "lat", "lon", None),
            P("panel", "lat", "lon"),
            P("panel", "lat", "lon"),
            P("panel", "lat", "lon"),
            P("panel", "lat", "lon"),
            P("panel", "lat", "lon"),
        ),
        out_specs=(P("panel", None, None, "lat", "lon"), P("panel", None, "lat", "lon")),
        check_vma=False,
    )
```

```python
import math

import jax
import jax.numpy as jnp
from jax import lax
from jax.experimental import pallas as pl
from jax.experimental.pallas import tpu as pltpu
from jax.sharding import PartitionSpec as P

CAP = 2
WQ = 8


BUOYANCY = 0.5


def partner_2(block, axis, apart):
    count = lax.axis_size(axis)
    route = []
    for low in range(count):
        high = low | 1 << apart
        if high != low and high < count:
            route += [(low, high), (high, low)]
    return lax.ppermute(block, axis, route)


def padded_2(shard, sides, width):
    for axis, dim in sides:
        size, length = (lax.axis_size(axis), shard.shape[dim])
        up = [(i, (i + 1) % size) for i in range(size - 1)]
        down = [(j, i) for i, j in up]
        last = lax.slice_in_dim(shard, length - width, length, axis=dim)
        leading = lax.slice_in_dim(shard, 0, width, axis=dim)
        before = lax.ppermute(last, axis, up)
        after = lax.ppermute(leading, axis, down)
        shard = jnp.concatenate([before, shard, after], axis=dim)
    return shard


def gather_by_exchange(block, axis):
    count = lax.axis_size(axis)
    repeated = jnp.broadcast_to(block[None], (count,) + block.shape)
    gathered = lax.all_to_all(repeated, axis, split_axis=0, concat_axis=0, tiled=True)
    return gathered.reshape((count * block.shape[0],) + block.shape[1:])


def corner_blend(table, rows, weights, width):
    count = rows.shape[0]

    def kernel(rows_ref, weights_ref, table_ref, out_ref):
        def body(t, carry):
            at = rows_ref[t]
            total = weights_ref[0, t] * table_ref[pl.ds(at, 1), :]
            for k, offset in enumerate((1, width, width + 1)):
                total = total + weights_ref[k + 1, t] * table_ref[pl.ds(at + offset, 1), :]
            out_ref[pl.ds(t, 1), :] = total
            return carry

        lax.fori_loop(0, count, body, 0, unroll=16)

    return pl.pallas_call(
        kernel,
        out_shape=jax.ShapeDtypeStruct((count, table.shape[1]), table.dtype),
        in_specs=[
            pl.BlockSpec(memory_space=pltpu.SMEM),
            pl.BlockSpec(memory_space=pltpu.SMEM),
            pl.BlockSpec(memory_space=pltpu.VMEM),
        ],
        out_specs=pl.BlockSpec(memory_space=pltpu.VMEM),
    )(rows, weights, table)


def metric(row_index, total_rows):
    colatitude = (
        math.pi / 4.0 + (row_index.astype(jnp.float32) + 0.5) * (math.pi / 2.0) / total_rows
    )
    inv_sine = 1.0 / jnp.sin(colatitude)
    return (inv_sine, inv_sine * inv_sine)


def lap_shrink(field, row_gain):
    centre = field[..., 1:-1, 1:-1]
    padded = jnp.pad(centre, [(0, 0)] * (centre.ndim - 3) + [(1, 1), (0, 0), (0, 0)])
    lat_term = field[..., 2:, 1:-1] + field[..., :-2, 1:-1] - 2.0 * centre
    lon_term = field[..., 1:-1, 2:] + field[..., 1:-1, :-2] - 2.0 * centre
    radial = padded[..., 2:, :, :] + padded[..., :-2, :, :] - 2.0 * centre
    return lat_term + row_gain[:, None] * lon_term + radial


def diverge(velocity, inv_sine):
    radial_pad = jnp.pad(velocity[0, :, 1:-1, 1:-1], ((1, 1), (0, 0), (0, 0)))
    lat_part = velocity[1, :, 2:, 1:-1] - velocity[1, :, :-2, 1:-1]
    lon_part = velocity[2, :, 1:-1, 2:] - velocity[2, :, 1:-1, :-2]
    rad_part = radial_pad[2:] - radial_pad[:-2]
    return 0.5 * (lat_part + inv_sine[:, None] * lon_part + rad_part)


def gradient(pressure, inv_sine):
    radial_pad = jnp.pad(pressure[:, 1:-1, 1:-1], ((1, 1), (0, 0), (0, 0)))
    grad_rad = 0.5 * (radial_pad[2:] - radial_pad[:-2])
    grad_lat = 0.5 * (pressure[:, 2:, 1:-1] - pressure[:, :-2, 1:-1])
    grad_lon = 0.5 * inv_sine[:, None] * (pressure[:, 1:-1, 2:] - pressure[:, 1:-1, :-2])
    return (grad_rad, grad_lat, grad_lon)


def cosine_table(length):
    mode_ids = jnp.arange(length, dtype=jnp.float32)
    cell_mid = jnp.arange(length, dtype=jnp.float32) + 0.5
    row_norm = jnp.sqrt(jnp.where(mode_ids > 0, 2.0, 1.0) / length)
    cos_table = row_norm[:, None] * jnp.cos(
        math.pi * mode_ids[:, None] * cell_mid[None, :] / length
    )
    eigenvalue = 4.0 * jnp.sin(math.pi * mode_ids / (2.0 * length)) ** 2
    return (cos_table, eigenvalue)


def coarse_divisor(levels, n_lat, n_lon):
    eig_rad = cosine_table(levels)[1]
    eig_lat = cosine_table(n_lat)[1]
    eig_lon = cosine_table(n_lon)[1]
    return (
        eig_rad[:, None, None]
        + eig_lat[None, :, None]
        + eig_lon[None, None, :]
        + 1.0 / (n_lat * n_lon)
    )


def coarse_solve(block_sum, n_lat, n_lon):
    highest = lax.Precision.HIGHEST
    tab_rad = cosine_table(block_sum.shape[0])[0]
    tab_lat = cosine_table(n_lat)[0]
    tab_lon = cosine_table(n_lon)[0]
    spectrum = jnp.einsum("kr,rlo->klo", tab_rad, block_sum, precision=highest)
    spectrum = jnp.einsum("kl,rlo->rko", tab_lat, spectrum, precision=highest)
    spectrum = jnp.einsum("ko,rlo->rlk", tab_lon, spectrum, precision=highest)
    spectrum = spectrum / coarse_divisor(block_sum.shape[0], n_lat, n_lon)
    restored = jnp.einsum("kr,klo->rlo", tab_rad, spectrum, precision=highest)
    restored = jnp.einsum("kl,rko->rlo", tab_lat, restored, precision=highest)
    restored = jnp.einsum("ko,rlk->rlo", tab_lon, restored, precision=highest)
    return restored / math.sqrt(n_lat * n_lon)


def fractions(weight_ids):
    frac_lat = ((weight_ids // WQ).astype(jnp.float32) + 0.5) / WQ
    frac_lon = ((weight_ids % WQ).astype(jnp.float32) + 0.5) / WQ
    return (frac_lat, frac_lon)


def bilinear(lower_left, lower_right, upper_left, upper_right, frac_lat, frac_lon):
    return (
        (1.0 - frac_lat) * (1.0 - frac_lon) * lower_left
        + (1.0 - frac_lat) * frac_lon * lower_right
        + frac_lat * (1.0 - frac_lon) * upper_left
        + frac_lat * frac_lon * upper_right
    )


def shards(fields, viscosity, partner, src_row, src_col, weight_id, border_angle, dest_cell):
    n_lat = lax.axis_size("lat")
    n_lon = lax.axis_size("lon")
    lat_pos = lax.axis_index("lat")
    lon_pos = lax.axis_index("lon")
    own_fields = fields[0]
    levels, rows_dev, cols_dev = (own_fields.shape[1], own_fields.shape[2], own_fields.shape[3])
    channels = 6 * levels
    blocks = partner.shape[2]
    block_cells = src_row.shape[2] // blocks
    capacity = CAP
    slot_count = n_lon * capacity
    total_rows = rows_dev * n_lat
    flat_cells = own_fields.reshape(channels, rows_dev * cols_dev)
    target = partner[0, 0, :, 0]
    onehot = (target[:, None] == jnp.arange(n_lon, dtype=jnp.int32)[None, :]).astype(jnp.int32)
    before = jnp.sum(
        (jnp.cumsum(onehot, axis=0, dtype=jnp.int32) - onehot) * onehot, axis=1, dtype=jnp.int32
    )
    slot_of = target * capacity + before
    base_cell = (src_row[0, 0] * cols_dev + src_col[0, 0]).reshape(blocks, block_cells)
    weight_ids = weight_id[0, 0].reshape(blocks, block_cells)
    empty = jnp.zeros((slot_count, block_cells), jnp.int32)
    asked = jnp.stack(
        [empty.at[slot_of].set(base_cell), empty.at[slot_of].set(weight_ids)], axis=1
    ).reshape(n_lon, capacity, 2, block_cells)
    requests = partner_2(asked, "panel", 0)
    requests = lax.all_to_all(requests, "lon", split_axis=0, concat_axis=0, tiled=True)
    cells_asked = requests[:, :, 0, :].reshape(-1)
    frac_lat, frac_lon = fractions(requests[:, :, 1, :].reshape(-1))
    weights = jnp.stack(
        [
            (1.0 - frac_lat) * (1.0 - frac_lon),
            (1.0 - frac_lat) * frac_lon,
            frac_lat * (1.0 - frac_lon),
            frac_lat * frac_lon,
        ],
        axis=0,
    )
    served = corner_blend(flat_cells.T, cells_asked, weights, cols_dev)
    served = served.reshape(n_lon, capacity, block_cells, channels)
    served = lax.all_to_all(served, "lon", split_axis=0, concat_axis=0, tiled=True)
    served = partner_2(served, "panel", 0)
    values = served.reshape(slot_count, block_cells, channels)[slot_of]
    values = values.reshape(blocks * block_cells, channels).T.reshape(6, levels, blocks * block_cells)
    turn = border_angle[0, 0]
    cos_angle = jnp.cos(turn)
    sin_angle = jnp.sin(turn)
    rotated = jnp.stack(
        [
            values[0],
            cos_angle * values[1] + sin_angle * values[2],
            cos_angle * values[2] - sin_angle * values[1],
            values[3],
            cos_angle * values[4] + sin_angle * values[5],
            cos_angle * values[5] - sin_angle * values[4],
        ],
        axis=0,
    ).reshape(channels, blocks * block_cells)
    filled = flat_cells.at[:, dest_cell[0, 0]].set(rotated).reshape(6, levels, rows_dev, cols_dev)
    diffusivity = viscosity[0]
    inv_own, gain_own = metric(
        lat_pos * rows_dev + jnp.arange(-0, rows_dev + 0, dtype=jnp.int32), total_rows
    )
    halo = 3
    total_cols = cols_dev * n_lon
    row_first = lat_pos * rows_dev
    col_first = lon_pos * cols_dev

    def inside(reach):
        rows = row_first - reach + jnp.arange(rows_dev + 2 * reach, dtype=jnp.int32)
        cols = col_first - reach + jnp.arange(cols_dev + 2 * reach, dtype=jnp.int32)
        return ((rows >= 0) & (rows < total_rows))[:, None] & ((cols >= 0) & (cols < total_cols))[
            None, :
        ]

    stack = jnp.concatenate([filled.reshape(channels, rows_dev, cols_dev), diffusivity], axis=0)
    wide = padded_2(stack, (("lat", 1), ("lon", 2)), halo)
    wide_fields = wide[:channels].reshape(6, levels, rows_dev + 2 * halo, cols_dev + 2 * halo)
    wide_visc = wide[channels:]
    inv_two, gain_two = metric(row_first + jnp.arange(-2, rows_dev + 2, dtype=jnp.int32), total_rows)
    inv_one, gain_one = metric(row_first + jnp.arange(-1, rows_dev + 1, dtype=jnp.int32), total_rows)
    centre = wide_fields[..., 1:-1, 1:-1]
    stepped_wide = centre + wide_visc[None, :, 1:-1, 1:-1] * lap_shrink(wide_fields, gain_two)
    stepped_wide = jnp.concatenate(
        [stepped_wide[0:1] + BUOYANCY * centre[3:4], stepped_wide[1:]], axis=0
    )
    velocity = jnp.where(inside(2), stepped_wide[0:3], 0.0)
    divergence_wide = diverge(velocity, inv_one)
    press_wide = jnp.where(inside(1), -divergence_wide / (4.0 + 2.0 * gain_one)[:, None], 0.0)
    divergence = divergence_wide[:, 1:-1, 1:-1]
    press_one = press_wide[:, 1:-1, 1:-1]
    stepped = stepped_wide[:, :, 2:-2, 2:-2]
    resid_one = -divergence + lap_shrink(press_wide, gain_own)
    block_sum = jnp.sum(resid_one, axis=(1, 2)) * (1.0 / math.sqrt(rows_dev * cols_dev))
    gathered = gather_by_exchange(block_sum[None], "lon")
    gathered = gather_by_exchange(gathered[None], "lat")
    coarse = coarse_solve(jnp.transpose(gathered, (2, 0, 1)), n_lat, n_lon)
    start = jnp.zeros((), jnp.int32)
    near = lax.dynamic_slice(
        jnp.pad(coarse, ((0, 0), (1, 1), (1, 1))), (start, lat_pos, lon_pos), (levels, 3, 3)
    )
    own_coarse = near[:, 1, 1]
    pressure = press_one + own_coarse[:, None, None]
    row_at = lax.broadcasted_iota(jnp.int32, (rows_dev + 2, cols_dev + 2), 0)
    col_at = lax.broadcasted_iota(jnp.int32, (rows_dev + 2, cols_dev + 2), 1)
    rim_coarse = jnp.where(
        row_at == 0,
        near[:, 0, 1][:, None, None],
        jnp.where(
            row_at == rows_dev + 1,
            near[:, 2, 1][:, None, None],
            jnp.where(
                col_at == 0,
                near[:, 1, 0][:, None, None],
                jnp.where(
                    col_at == cols_dev + 1, near[:, 1, 2][:, None, None], own_coarse[:, None, None]
                ),
            ),
        ),
    )
    press_rim = press_wide + rim_coarse
    grad_rad, grad_lat, grad_lon = gradient(press_rim, inv_own)
    result = jnp.stack(
        [
            stepped[0] - grad_rad,
            stepped[1] - grad_lat,
            stepped[2] - grad_lon,
            stepped[3],
            stepped[4],
            stepped[5],
        ],
        axis=0,
    )
    return (result[None], pressure[None])


def solution(mesh):
    return jax.shard_map(
        shards,
        mesh=mesh,
        in_specs=(
            P("panel", None, None, "lat", "lon"),
            P("panel", None, "lat", "lon"),
            P("panel", "lat", "lon", None),
            P("panel", "lat", "lon"),
            P("panel", "lat", "lon"),
            P("panel", "lat", "lon"),
            P("panel", "lat", "lon"),
            P("panel", "lat", "lon"),
        ),
        out_specs=(P("panel", None, None, "lat", "lon"), P("panel", None, "lat", "lon")),
        check_vma=False,
    )
```

```python
import math

import jax
import jax.numpy as jnp
from jax import lax
from jax.experimental import pallas as pl
from jax.experimental.pallas import tpu as pltpu
from jax.sharding import PartitionSpec as P

CAP = 2
WQ = 8


BUOYANCY = 0.5


def partner_2(block, axis, apart):
    count = lax.axis_size(axis)
    route = []
    for low in range(count):
        high = low | 1 << apart
        if high != low and high < count:
            route += [(low, high), (high, low)]
    return lax.ppermute(block, axis, route)


def padded_2(shard, sides, width):
    for axis, dim in sides:
        size, length = (lax.axis_size(axis), shard.shape[dim])
        up = [(i, (i + 1) % size) for i in range(size - 1)]
        down = [(j, i) for i, j in up]
        last = lax.slice_in_dim(shard, length - width, length, axis=dim)
        leading = lax.slice_in_dim(shard, 0, width, axis=dim)
        before = lax.ppermute(last, axis, up)
        after = lax.ppermute(leading, axis, down)
        shard = jnp.concatenate([before, shard, after], axis=dim)
    return shard


def gather_by_exchange(block, axis):
    count = lax.axis_size(axis)
    repeated = jnp.broadcast_to(block[None], (count,) + block.shape)
    gathered = lax.all_to_all(repeated, axis, split_axis=0, concat_axis=0, tiled=True)
    return gathered.reshape((count * block.shape[0],) + block.shape[1:])


def corner_blend(table, rows, weights, width):
    count = rows.shape[0]

    def kernel(rows_ref, weights_ref, table_ref, out_ref):
        def body(t, carry):
            at = rows_ref[t]
            total = weights_ref[0, t] * table_ref[pl.ds(at, 1), :]
            for k, offset in enumerate((1, width, width + 1)):
                total = total + weights_ref[k + 1, t] * table_ref[pl.ds(at + offset, 1), :]
            out_ref[pl.ds(t, 1), :] = total
            return carry

        lax.fori_loop(0, count, body, 0, unroll=16)

    return pl.pallas_call(
        kernel,
        out_shape=jax.ShapeDtypeStruct((count, table.shape[1]), table.dtype),
        in_specs=[
            pl.BlockSpec(memory_space=pltpu.SMEM),
            pl.BlockSpec(memory_space=pltpu.SMEM),
            pl.BlockSpec(memory_space=pltpu.VMEM),
        ],
        out_specs=pl.BlockSpec(memory_space=pltpu.VMEM),
    )(rows, weights, table)


def metric(row_index, total_rows):
    colatitude = (
        math.pi / 4.0 + (row_index.astype(jnp.float32) + 0.5) * (math.pi / 2.0) / total_rows
    )
    inv_sine = 1.0 / jnp.sin(colatitude)
    return (inv_sine, inv_sine * inv_sine)


def lap_shrink(field, row_gain):
    centre = field[..., 1:-1, 1:-1]
    padded = jnp.pad(centre, [(0, 0)] * (centre.ndim - 3) + [(1, 1), (0, 0), (0, 0)])
    lat_term = field[..., 2:, 1:-1] + field[..., :-2, 1:-1] - 2.0 * centre
    lon_term = field[..., 1:-1, 2:] + field[..., 1:-1, :-2] - 2.0 * centre
    radial = padded[..., 2:, :, :] + padded[..., :-2, :, :] - 2.0 * centre
    return lat_term + row_gain[:, None] * lon_term + radial


def diverge(velocity, inv_sine):
    radial_pad = jnp.pad(velocity[0, :, 1:-1, 1:-1], ((1, 1), (0, 0), (0, 0)))
    lat_part = velocity[1, :, 2:, 1:-1] - velocity[1, :, :-2, 1:-1]
    lon_part = velocity[2, :, 1:-1, 2:] - velocity[2, :, 1:-1, :-2]
    rad_part = radial_pad[2:] - radial_pad[:-2]
    return 0.5 * (lat_part + inv_sine[:, None] * lon_part + rad_part)


def gradient(pressure, inv_sine):
    radial_pad = jnp.pad(pressure[:, 1:-1, 1:-1], ((1, 1), (0, 0), (0, 0)))
    grad_rad = 0.5 * (radial_pad[2:] - radial_pad[:-2])
    grad_lat = 0.5 * (pressure[:, 2:, 1:-1] - pressure[:, :-2, 1:-1])
    grad_lon = 0.5 * inv_sine[:, None] * (pressure[:, 1:-1, 2:] - pressure[:, 1:-1, :-2])
    return (grad_rad, grad_lat, grad_lon)


def cosine_table(length):
    mode_ids = jnp.arange(length, dtype=jnp.float32)
    cell_mid = jnp.arange(length, dtype=jnp.float32) + 0.5
    row_norm = jnp.sqrt(jnp.where(mode_ids > 0, 2.0, 1.0) / length)
    cos_table = row_norm[:, None] * jnp.cos(
        math.pi * mode_ids[:, None] * cell_mid[None, :] / length
    )
    eigenvalue = 4.0 * jnp.sin(math.pi * mode_ids / (2.0 * length)) ** 2
    return (cos_table, eigenvalue)


def coarse_divisor(levels, n_lat, n_lon):
    eig_rad = cosine_table(levels)[1]
    eig_lat = cosine_table(n_lat)[1]
    eig_lon = cosine_table(n_lon)[1]
    return (
        eig_rad[:, None, None]
        + eig_lat[None, :, None]
        + eig_lon[None, None, :]
        + 1.0 / (n_lat * n_lon)
    )


def coarse_solve(block_sum, n_lat, n_lon):
    highest = lax.Precision.HIGHEST
    tab_rad = cosine_table(block_sum.shape[0])[0]
    tab_lat = cosine_table(n_lat)[0]
    tab_lon = cosine_table(n_lon)[0]
    spectrum = jnp.einsum("kr,rlo->klo", tab_rad, block_sum, precision=highest)
    spectrum = jnp.einsum("kl,rlo->rko", tab_lat, spectrum, precision=highest)
    spectrum = jnp.einsum("ko,rlo->rlk", tab_lon, spectrum, precision=highest)
    spectrum = spectrum / coarse_divisor(block_sum.shape[0], n_lat, n_lon)
    restored = jnp.einsum("kr,klo->rlo", tab_rad, spectrum, precision=highest)
    restored = jnp.einsum("kl,rko->rlo", tab_lat, restored, precision=highest)
    restored = jnp.einsum("ko,rlk->rlo", tab_lon, restored, precision=highest)
    return restored / math.sqrt(n_lat * n_lon)


def fractions(weight_ids):
    frac_lat = ((weight_ids // WQ).astype(jnp.float32) + 0.5) / WQ
    frac_lon = ((weight_ids % WQ).astype(jnp.float32) + 0.5) / WQ
    return (frac_lat, frac_lon)


def bilinear(lower_left, lower_right, upper_left, upper_right, frac_lat, frac_lon):
    return (
        (1.0 - frac_lat) * (1.0 - frac_lon) * lower_left
        + (1.0 - frac_lat) * frac_lon * lower_right
        + frac_lat * (1.0 - frac_lon) * upper_left
        + frac_lat * frac_lon * upper_right
    )


def shards(fields, viscosity, partner, src_row, src_col, weight_id, border_angle, dest_cell):
    n_lat = lax.axis_size("lat")
    n_lon = lax.axis_size("lon")
    lat_pos = lax.axis_index("lat")
    lon_pos = lax.axis_index("lon")
    own_fields = fields[0]
    levels, rows_dev, cols_dev = (own_fields.shape[1], own_fields.shape[2], own_fields.shape[3])
    channels = 6 * levels
    blocks = partner.shape[2]
    block_cells = src_row.shape[2] // blocks
    capacity = CAP
    slot_count = n_lon * capacity
    total_rows = rows_dev * n_lat
    flat_cells = own_fields.reshape(channels, rows_dev * cols_dev)
    target = partner[0, 0, :, 0]
    onehot = (target[:, None] == jnp.arange(n_lon, dtype=jnp.int32)[None, :]).astype(jnp.int32)
    before = jnp.sum(
        (jnp.cumsum(onehot, axis=0, dtype=jnp.int32) - onehot) * onehot, axis=1, dtype=jnp.int32
    )
    slot_of = target * capacity + before
    base_cell = (src_row[0, 0] * cols_dev + src_col[0, 0]).reshape(blocks, block_cells)
    weight_ids = weight_id[0, 0].reshape(blocks, block_cells)
    empty = jnp.zeros((slot_count, block_cells), jnp.int32)
    asked = jnp.stack(
        [empty.at[slot_of].set(base_cell), empty.at[slot_of].set(weight_ids)], axis=1
    ).reshape(n_lon, capacity, 2, block_cells)
    requests = partner_2(asked, "panel", 0)
    slot_mirror = partner_2(slot_of, "panel", 0)
    requests = lax.all_to_all(requests, "lon", split_axis=0, concat_axis=0, tiled=True)
    cells_asked = requests[:, :, 0, :].reshape(-1)
    frac_lat, frac_lon = fractions(requests[:, :, 1, :].reshape(-1))
    weights = jnp.stack(
        [
            (1.0 - frac_lat) * (1.0 - frac_lon),
            (1.0 - frac_lat) * frac_lon,
            frac_lat * (1.0 - frac_lon),
            frac_lat * frac_lon,
        ],
        axis=0,
    )
    served = corner_blend(flat_cells.T, cells_asked, weights, cols_dev)
    served = served.reshape(n_lon, capacity, block_cells, channels)
    served = lax.all_to_all(served, "lon", split_axis=0, concat_axis=0, tiled=True)
    served = served.reshape(slot_count, block_cells, channels)[slot_mirror]
    values = partner_2(served, "panel", 0)
    values = values.reshape(blocks * block_cells, channels).T.reshape(6, levels, blocks * block_cells)
    turn = border_angle[0, 0]
    cos_angle = jnp.cos(turn)
    sin_angle = jnp.sin(turn)
    rotated = jnp.stack(
        [
            values[0],
            cos_angle * values[1] + sin_angle * values[2],
            cos_angle * values[2] - sin_angle * values[1],
            values[3],
            cos_angle * values[4] + sin_angle * values[5],
            cos_angle * values[5] - sin_angle * values[4],
        ],
        axis=0,
    ).reshape(channels, blocks * block_cells)
    filled = flat_cells.at[:, dest_cell[0, 0]].set(rotated).reshape(6, levels, rows_dev, cols_dev)
    diffusivity = viscosity[0]
    inv_own, gain_own = metric(
        lat_pos * rows_dev + jnp.arange(-0, rows_dev + 0, dtype=jnp.int32), total_rows
    )
    halo = 3
    total_cols = cols_dev * n_lon
    row_first = lat_pos * rows_dev
    col_first = lon_pos * cols_dev

    def inside(reach):
        rows = row_first - reach + jnp.arange(rows_dev + 2 * reach, dtype=jnp.int32)
        cols = col_first - reach + jnp.arange(cols_dev + 2 * reach, dtype=jnp.int32)
        return ((rows >= 0) & (rows < total_rows))[:, None] & ((cols >= 0) & (cols < total_cols))[
            None, :
        ]

    stack = jnp.concatenate([filled.reshape(channels, rows_dev, cols_dev), diffusivity], axis=0)
    wide = padded_2(stack, (("lat", 1), ("lon", 2)), halo)
    wide_fields = wide[:channels].reshape(6, levels, rows_dev + 2 * halo, cols_dev + 2 * halo)
    wide_visc = wide[channels:]
    inv_two, gain_two = metric(row_first + jnp.arange(-2, rows_dev + 2, dtype=jnp.int32), total_rows)
    inv_one, gain_one = metric(row_first + jnp.arange(-1, rows_dev + 1, dtype=jnp.int32), total_rows)
    centre = wide_fields[..., 1:-1, 1:-1]
    stepped_wide = centre + wide_visc[None, :, 1:-1, 1:-1] * lap_shrink(wide_fields, gain_two)
    stepped_wide = jnp.concatenate(
        [stepped_wide[0:1] + BUOYANCY * centre[3:4], stepped_wide[1:]], axis=0
    )
    velocity = jnp.where(inside(2), stepped_wide[0:3], 0.0)
    divergence_wide = diverge(velocity, inv_one)
    press_wide = jnp.where(inside(1), -divergence_wide / (4.0 + 2.0 * gain_one)[:, None], 0.0)
    divergence = divergence_wide[:, 1:-1, 1:-1]
    press_one = press_wide[:, 1:-1, 1:-1]
    stepped = stepped_wide[:, :, 2:-2, 2:-2]
    resid_one = -divergence + lap_shrink(press_wide, gain_own)
    block_sum = jnp.sum(resid_one, axis=(1, 2)) * (1.0 / math.sqrt(rows_dev * cols_dev))
    gathered = gather_by_exchange(block_sum[None], "lon")
    gathered = gather_by_exchange(gathered[None], "lat")
    coarse = coarse_solve(jnp.transpose(gathered, (2, 0, 1)), n_lat, n_lon)
    start = jnp.zeros((), jnp.int32)
    near = lax.dynamic_slice(
        jnp.pad(coarse, ((0, 0), (1, 1), (1, 1))), (start, lat_pos, lon_pos), (levels, 3, 3)
    )
    own_coarse = near[:, 1, 1]
    pressure = press_one + own_coarse[:, None, None]
    row_at = lax.broadcasted_iota(jnp.int32, (rows_dev + 2, cols_dev + 2), 0)
    col_at = lax.broadcasted_iota(jnp.int32, (rows_dev + 2, cols_dev + 2), 1)
    rim_coarse = jnp.where(
        row_at == 0,
        near[:, 0, 1][:, None, None],
        jnp.where(
            row_at == rows_dev + 1,
            near[:, 2, 1][:, None, None],
            jnp.where(
                col_at == 0,
                near[:, 1, 0][:, None, None],
                jnp.where(
                    col_at == cols_dev + 1, near[:, 1, 2][:, None, None], own_coarse[:, None, None]
                ),
            ),
        ),
    )
    press_rim = press_wide + rim_coarse
    grad_rad, grad_lat, grad_lon = gradient(press_rim, inv_own)
    result = jnp.stack(
        [
            stepped[0] - grad_rad,
            stepped[1] - grad_lat,
            stepped[2] - grad_lon,
            stepped[3],
            stepped[4],
            stepped[5],
        ],
        axis=0,
    )
    return (result[None], pressure[None])


def solution(mesh):
    return jax.shard_map(
        shards,
        mesh=mesh,
        in_specs=(
            P("panel", None, None, "lat", "lon"),
            P("panel", None, "lat", "lon"),
            P("panel", "lat", "lon", None),
            P("panel", "lat", "lon"),
            P("panel", "lat", "lon"),
            P("panel", "lat", "lon"),
            P("panel", "lat", "lon"),
            P("panel", "lat", "lon"),
        ),
        out_specs=(P("panel", None, None, "lat", "lon"), P("panel", None, "lat", "lon")),
        check_vma=False,
    )
```

```python
import math

import jax
import jax.numpy as jnp
from jax import lax
from jax.experimental import pallas as pl
from jax.experimental.pallas import tpu as pltpu
from jax.sharding import PartitionSpec as P

CAP = 2
WQ = 8


BUOYANCY = 0.5


def partner_2(block, axis, apart):
    count = lax.axis_size(axis)
    route = []
    for low in range(count):
        high = low | 1 << apart
        if high != low and high < count:
            route += [(low, high), (high, low)]
    return lax.ppermute(block, axis, route)


def padded_2(shard, sides, width):
    for axis, dim in sides:
        size, length = (lax.axis_size(axis), shard.shape[dim])
        up = [(i, (i + 1) % size) for i in range(size - 1)]
        down = [(j, i) for i, j in up]
        last = lax.slice_in_dim(shard, length - width, length, axis=dim)
        leading = lax.slice_in_dim(shard, 0, width, axis=dim)
        before = lax.ppermute(last, axis, up)
        after = lax.ppermute(leading, axis, down)
        shard = jnp.concatenate([before, shard, after], axis=dim)
    return shard


def gather_by_exchange(block, axis):
    count = lax.axis_size(axis)
    repeated = jnp.broadcast_to(block[None], (count,) + block.shape)
    gathered = lax.all_to_all(repeated, axis, split_axis=0, concat_axis=0, tiled=True)
    return gathered.reshape((count * block.shape[0],) + block.shape[1:])


def corner_blend(table, rows, weights, width):
    count = rows.shape[0]

    def kernel(rows_ref, weights_ref, table_ref, out_ref):
        def body(t, carry):
            at = rows_ref[t]
            total = weights_ref[0, t] * table_ref[pl.ds(at, 1), :]
            for k, offset in enumerate((1, width, width + 1)):
                total = total + weights_ref[k + 1, t] * table_ref[pl.ds(at + offset, 1), :]
            out_ref[pl.ds(t, 1), :] = total
            return carry

        lax.fori_loop(0, count, body, 0, unroll=16)

    return pl.pallas_call(
        kernel,
        out_shape=jax.ShapeDtypeStruct((count, table.shape[1]), table.dtype),
        in_specs=[
            pl.BlockSpec(memory_space=pltpu.SMEM),
            pl.BlockSpec(memory_space=pltpu.SMEM),
            pl.BlockSpec(memory_space=pltpu.VMEM),
        ],
        out_specs=pl.BlockSpec(memory_space=pltpu.VMEM),
    )(rows, weights, table)


def metric(row_index, total_rows):
    colatitude = (
        math.pi / 4.0 + (row_index.astype(jnp.float32) + 0.5) * (math.pi / 2.0) / total_rows
    )
    inv_sine = 1.0 / jnp.sin(colatitude)
    return (inv_sine, inv_sine * inv_sine)


def lap_shrink(field, row_gain):
    centre = field[..., 1:-1, 1:-1]
    padded = jnp.pad(centre, [(0, 0)] * (centre.ndim - 3) + [(1, 1), (0, 0), (0, 0)])
    lat_term = field[..., 2:, 1:-1] + field[..., :-2, 1:-1] - 2.0 * centre
    lon_term = field[..., 1:-1, 2:] + field[..., 1:-1, :-2] - 2.0 * centre
    radial = padded[..., 2:, :, :] + padded[..., :-2, :, :] - 2.0 * centre
    return lat_term + row_gain[:, None] * lon_term + radial


def diverge(velocity, inv_sine):
    radial_pad = jnp.pad(velocity[0, :, 1:-1, 1:-1], ((1, 1), (0, 0), (0, 0)))
    lat_part = velocity[1, :, 2:, 1:-1] - velocity[1, :, :-2, 1:-1]
    lon_part = velocity[2, :, 1:-1, 2:] - velocity[2, :, 1:-1, :-2]
    rad_part = radial_pad[2:] - radial_pad[:-2]
    return 0.5 * (lat_part + inv_sine[:, None] * lon_part + rad_part)


def gradient(pressure, inv_sine):
    radial_pad = jnp.pad(pressure[:, 1:-1, 1:-1], ((1, 1), (0, 0), (0, 0)))
    grad_rad = 0.5 * (radial_pad[2:] - radial_pad[:-2])
    grad_lat = 0.5 * (pressure[:, 2:, 1:-1] - pressure[:, :-2, 1:-1])
    grad_lon = 0.5 * inv_sine[:, None] * (pressure[:, 1:-1, 2:] - pressure[:, 1:-1, :-2])
    return (grad_rad, grad_lat, grad_lon)


def cosine_table(length):
    mode_ids = jnp.arange(length, dtype=jnp.float32)
    cell_mid = jnp.arange(length, dtype=jnp.float32) + 0.5
    row_norm = jnp.sqrt(jnp.where(mode_ids > 0, 2.0, 1.0) / length)
    cos_table = row_norm[:, None] * jnp.cos(
        math.pi * mode_ids[:, None] * cell_mid[None, :] / length
    )
    eigenvalue = 4.0 * jnp.sin(math.pi * mode_ids / (2.0 * length)) ** 2
    return (cos_table, eigenvalue)


def coarse_divisor(levels, n_lat, n_lon):
    eig_rad = cosine_table(levels)[1]
    eig_lat = cosine_table(n_lat)[1]
    eig_lon = cosine_table(n_lon)[1]
    return (
        eig_rad[:, None, None]
        + eig_lat[None, :, None]
        + eig_lon[None, None, :]
        + 1.0 / (n_lat * n_lon)
    )


def coarse_solve(block_sum, n_lat, n_lon):
    highest = lax.Precision.HIGHEST
    tab_rad = cosine_table(block_sum.shape[0])[0]
    tab_lat = cosine_table(n_lat)[0]
    tab_lon = cosine_table(n_lon)[0]
    spectrum = jnp.einsum("kr,rlo->klo", tab_rad, block_sum, precision=highest)
    spectrum = jnp.einsum("kl,rlo->rko", tab_lat, spectrum, precision=highest)
    spectrum = jnp.einsum("ko,rlo->rlk", tab_lon, spectrum, precision=highest)
    spectrum = spectrum / coarse_divisor(block_sum.shape[0], n_lat, n_lon)
    restored = jnp.einsum("kr,klo->rlo", tab_rad, spectrum, precision=highest)
    restored = jnp.einsum("kl,rko->rlo", tab_lat, restored, precision=highest)
    restored = jnp.einsum("ko,rlk->rlo", tab_lon, restored, precision=highest)
    return restored / math.sqrt(n_lat * n_lon)


def fractions(weight_ids):
    frac_lat = ((weight_ids // WQ).astype(jnp.float32) + 0.5) / WQ
    frac_lon = ((weight_ids % WQ).astype(jnp.float32) + 0.5) / WQ
    return (frac_lat, frac_lon)


def bilinear(lower_left, lower_right, upper_left, upper_right, frac_lat, frac_lon):
    return (
        (1.0 - frac_lat) * (1.0 - frac_lon) * lower_left
        + (1.0 - frac_lat) * frac_lon * lower_right
        + frac_lat * (1.0 - frac_lon) * upper_left
        + frac_lat * frac_lon * upper_right
    )


def shards(fields, viscosity, partner, src_row, src_col, weight_id, border_angle, dest_cell):
    n_lat = lax.axis_size("lat")
    n_lon = lax.axis_size("lon")
    lat_pos = lax.axis_index("lat")
    lon_pos = lax.axis_index("lon")
    own_fields = fields[0]
    levels, rows_dev, cols_dev = (own_fields.shape[1], own_fields.shape[2], own_fields.shape[3])
    channels = 6 * levels
    blocks = partner.shape[2]
    block_cells = src_row.shape[2] // blocks
    capacity = CAP
    slot_count = n_lon * capacity
    total_rows = rows_dev * n_lat
    flat_cells = own_fields.reshape(channels, rows_dev * cols_dev)
    target = partner[0, 0, :, 0]
    onehot = (target[:, None] == jnp.arange(n_lon, dtype=jnp.int32)[None, :]).astype(jnp.int32)
    before = jnp.sum(
        (jnp.cumsum(onehot, axis=0, dtype=jnp.int32) - onehot) * onehot, axis=1, dtype=jnp.int32
    )
    slot_of = target * capacity + before
    base_cell = (src_row[0, 0] * cols_dev + src_col[0, 0]).reshape(blocks, block_cells)
    weight_ids = weight_id[0, 0].reshape(blocks, block_cells)
    empty = jnp.zeros((slot_count, block_cells), jnp.int32)
    asked = jnp.stack(
        [empty.at[slot_of].set(base_cell), empty.at[slot_of].set(weight_ids)], axis=1
    ).reshape(n_lon, capacity, 2, block_cells)
    requests = partner_2(asked, "panel", 0)
    slot_mirror = partner_2(slot_of, "panel", 0)
    requests = lax.all_to_all(requests, "lon", split_axis=0, concat_axis=0, tiled=True)
    table = flat_cells.T
    halves = []
    for half in range(capacity):
        cells_asked = requests[:, half, 0, :].reshape(-1)
        frac_lat, frac_lon = fractions(requests[:, half, 1, :].reshape(-1))
        weights = jnp.stack(
            [
                (1.0 - frac_lat) * (1.0 - frac_lon),
                (1.0 - frac_lat) * frac_lon,
                frac_lat * (1.0 - frac_lon),
                frac_lat * frac_lon,
            ],
            axis=0,
        )
        blended = corner_blend(table, cells_asked, weights, cols_dev)
        blended = blended.reshape(n_lon, block_cells, channels)
        halves.append(lax.all_to_all(blended, "lon", split_axis=0, concat_axis=0, tiled=True))
    served = jnp.stack(halves, axis=1)
    served = served.reshape(slot_count, block_cells, channels)[slot_mirror]
    values = partner_2(served, "panel", 0)
    values = values.reshape(blocks * block_cells, channels).T.reshape(6, levels, blocks * block_cells)
    turn = border_angle[0, 0]
    cos_angle = jnp.cos(turn)
    sin_angle = jnp.sin(turn)
    rotated = jnp.stack(
        [
            values[0],
            cos_angle * values[1] + sin_angle * values[2],
            cos_angle * values[2] - sin_angle * values[1],
            values[3],
            cos_angle * values[4] + sin_angle * values[5],
            cos_angle * values[5] - sin_angle * values[4],
        ],
        axis=0,
    ).reshape(channels, blocks * block_cells)
    filled = flat_cells.at[:, dest_cell[0, 0]].set(rotated).reshape(6, levels, rows_dev, cols_dev)
    diffusivity = viscosity[0]
    inv_own, gain_own = metric(
        lat_pos * rows_dev + jnp.arange(-0, rows_dev + 0, dtype=jnp.int32), total_rows
    )
    halo = 3
    total_cols = cols_dev * n_lon
    row_first = lat_pos * rows_dev
    col_first = lon_pos * cols_dev

    def inside(reach):
        rows = row_first - reach + jnp.arange(rows_dev + 2 * reach, dtype=jnp.int32)
        cols = col_first - reach + jnp.arange(cols_dev + 2 * reach, dtype=jnp.int32)
        return ((rows >= 0) & (rows < total_rows))[:, None] & ((cols >= 0) & (cols < total_cols))[
            None, :
        ]

    stack = jnp.concatenate([filled.reshape(channels, rows_dev, cols_dev), diffusivity], axis=0)
    wide = padded_2(stack, (("lat", 1), ("lon", 2)), halo)
    wide_fields = wide[:channels].reshape(6, levels, rows_dev + 2 * halo, cols_dev + 2 * halo)
    wide_visc = wide[channels:]
    inv_two, gain_two = metric(row_first + jnp.arange(-2, rows_dev + 2, dtype=jnp.int32), total_rows)
    inv_one, gain_one = metric(row_first + jnp.arange(-1, rows_dev + 1, dtype=jnp.int32), total_rows)
    centre = wide_fields[..., 1:-1, 1:-1]
    stepped_wide = centre + wide_visc[None, :, 1:-1, 1:-1] * lap_shrink(wide_fields, gain_two)
    stepped_wide = jnp.concatenate(
        [stepped_wide[0:1] + BUOYANCY * centre[3:4], stepped_wide[1:]], axis=0
    )
    velocity = jnp.where(inside(2), stepped_wide[0:3], 0.0)
    divergence_wide = diverge(velocity, inv_one)
    press_wide = jnp.where(inside(1), -divergence_wide / (4.0 + 2.0 * gain_one)[:, None], 0.0)
    divergence = divergence_wide[:, 1:-1, 1:-1]
    press_one = press_wide[:, 1:-1, 1:-1]
    stepped = stepped_wide[:, :, 2:-2, 2:-2]
    resid_one = -divergence + lap_shrink(press_wide, gain_own)
    block_sum = jnp.sum(resid_one, axis=(1, 2)) * (1.0 / math.sqrt(rows_dev * cols_dev))
    gathered = gather_by_exchange(block_sum[None], "lon")
    gathered = gather_by_exchange(gathered[None], "lat")
    coarse = coarse_solve(jnp.transpose(gathered, (2, 0, 1)), n_lat, n_lon)
    start = jnp.zeros((), jnp.int32)
    near = lax.dynamic_slice(
        jnp.pad(coarse, ((0, 0), (1, 1), (1, 1))), (start, lat_pos, lon_pos), (levels, 3, 3)
    )
    own_coarse = near[:, 1, 1]
    pressure = press_one + own_coarse[:, None, None]
    row_at = lax.broadcasted_iota(jnp.int32, (rows_dev + 2, cols_dev + 2), 0)
    col_at = lax.broadcasted_iota(jnp.int32, (rows_dev + 2, cols_dev + 2), 1)
    rim_coarse = jnp.where(
        row_at == 0,
        near[:, 0, 1][:, None, None],
        jnp.where(
            row_at == rows_dev + 1,
            near[:, 2, 1][:, None, None],
            jnp.where(
                col_at == 0,
                near[:, 1, 0][:, None, None],
                jnp.where(
                    col_at == cols_dev + 1, near[:, 1, 2][:, None, None], own_coarse[:, None, None]
                ),
            ),
        ),
    )
    press_rim = press_wide + rim_coarse
    grad_rad, grad_lat, grad_lon = gradient(press_rim, inv_own)
    result = jnp.stack(
        [
            stepped[0] - grad_rad,
            stepped[1] - grad_lat,
            stepped[2] - grad_lon,
            stepped[3],
            stepped[4],
            stepped[5],
        ],
        axis=0,
    )
    return (result[None], pressure[None])


def solution(mesh):
    return jax.shard_map(
        shards,
        mesh=mesh,
        in_specs=(
            P("panel", None, None, "lat", "lon"),
            P("panel", None, "lat", "lon"),
            P("panel", "lat", "lon", None),
            P("panel", "lat", "lon"),
            P("panel", "lat", "lon"),
            P("panel", "lat", "lon"),
            P("panel", "lat", "lon"),
            P("panel", "lat", "lon"),
        ),
        out_specs=(P("panel", None, None, "lat", "lon"), P("panel", None, "lat", "lon")),
        check_vma=False,
    )
```

```python
import math

import jax
import jax.numpy as jnp
from jax import lax
from jax.experimental import pallas as pl
from jax.experimental.pallas import tpu as pltpu
from jax.sharding import PartitionSpec as P

CAP = 2
WQ = 8


BUOYANCY = 0.5


def partner_2(block, axis, apart):
    count = lax.axis_size(axis)
    route = []
    for low in range(count):
        high = low | 1 << apart
        if high != low and high < count:
            route += [(low, high), (high, low)]
    return lax.ppermute(block, axis, route)


def padded_2(shard, sides, width):
    for axis, dim in sides:
        size, length = (lax.axis_size(axis), shard.shape[dim])
        up = [(i, (i + 1) % size) for i in range(size - 1)]
        down = [(j, i) for i, j in up]
        last = lax.slice_in_dim(shard, length - width, length, axis=dim)
        leading = lax.slice_in_dim(shard, 0, width, axis=dim)
        before = lax.ppermute(last, axis, up)
        after = lax.ppermute(leading, axis, down)
        shard = jnp.concatenate([before, shard, after], axis=dim)
    return shard


def gather_by_exchange(block, axis):
    count = lax.axis_size(axis)
    repeated = jnp.broadcast_to(block[None], (count,) + block.shape)
    gathered = lax.all_to_all(repeated, axis, split_axis=0, concat_axis=0, tiled=True)
    return gathered.reshape((count * block.shape[0],) + block.shape[1:])


def corner_blend(table, rows, weights, width):
    count = rows.shape[0]

    def kernel(rows_ref, weights_ref, table_ref, out_ref):
        def body(t, carry):
            at = rows_ref[t]
            total = weights_ref[0, t] * table_ref[pl.ds(at, 1), :]
            for k, offset in enumerate((1, width, width + 1)):
                total = total + weights_ref[k + 1, t] * table_ref[pl.ds(at + offset, 1), :]
            out_ref[pl.ds(t, 1), :] = total
            return carry

        lax.fori_loop(0, count, body, 0, unroll=16)

    return pl.pallas_call(
        kernel,
        out_shape=jax.ShapeDtypeStruct((count, table.shape[1]), table.dtype),
        in_specs=[
            pl.BlockSpec(memory_space=pltpu.SMEM),
            pl.BlockSpec(memory_space=pltpu.SMEM),
            pl.BlockSpec(memory_space=pltpu.VMEM),
        ],
        out_specs=pl.BlockSpec(memory_space=pltpu.VMEM),
    )(rows, weights, table)


def metric(row_index, total_rows):
    colatitude = (
        math.pi / 4.0 + (row_index.astype(jnp.float32) + 0.5) * (math.pi / 2.0) / total_rows
    )
    inv_sine = 1.0 / jnp.sin(colatitude)
    return (inv_sine, inv_sine * inv_sine)


def lap_shrink(field, row_gain):
    centre = field[..., 1:-1, 1:-1]
    padded = jnp.pad(centre, [(0, 0)] * (centre.ndim - 3) + [(1, 1), (0, 0), (0, 0)])
    lat_term = field[..., 2:, 1:-1] + field[..., :-2, 1:-1] - 2.0 * centre
    lon_term = field[..., 1:-1, 2:] + field[..., 1:-1, :-2] - 2.0 * centre
    radial = padded[..., 2:, :, :] + padded[..., :-2, :, :] - 2.0 * centre
    return lat_term + row_gain[:, None] * lon_term + radial


def diverge(velocity, inv_sine):
    radial_pad = jnp.pad(velocity[0, :, 1:-1, 1:-1], ((1, 1), (0, 0), (0, 0)))
    lat_part = velocity[1, :, 2:, 1:-1] - velocity[1, :, :-2, 1:-1]
    lon_part = velocity[2, :, 1:-1, 2:] - velocity[2, :, 1:-1, :-2]
    rad_part = radial_pad[2:] - radial_pad[:-2]
    return 0.5 * (lat_part + inv_sine[:, None] * lon_part + rad_part)


def gradient(pressure, inv_sine):
    radial_pad = jnp.pad(pressure[:, 1:-1, 1:-1], ((1, 1), (0, 0), (0, 0)))
    grad_rad = 0.5 * (radial_pad[2:] - radial_pad[:-2])
    grad_lat = 0.5 * (pressure[:, 2:, 1:-1] - pressure[:, :-2, 1:-1])
    grad_lon = 0.5 * inv_sine[:, None] * (pressure[:, 1:-1, 2:] - pressure[:, 1:-1, :-2])
    return (grad_rad, grad_lat, grad_lon)


def cosine_table(length):
    mode_ids = jnp.arange(length, dtype=jnp.float32)
    cell_mid = jnp.arange(length, dtype=jnp.float32) + 0.5
    row_norm = jnp.sqrt(jnp.where(mode_ids > 0, 2.0, 1.0) / length)
    cos_table = row_norm[:, None] * jnp.cos(
        math.pi * mode_ids[:, None] * cell_mid[None, :] / length
    )
    eigenvalue = 4.0 * jnp.sin(math.pi * mode_ids / (2.0 * length)) ** 2
    return (cos_table, eigenvalue)


def coarse_divisor(levels, n_lat, n_lon):
    eig_rad = cosine_table(levels)[1]
    eig_lat = cosine_table(n_lat)[1]
    eig_lon = cosine_table(n_lon)[1]
    return (
        eig_rad[:, None, None]
        + eig_lat[None, :, None]
        + eig_lon[None, None, :]
        + 1.0 / (n_lat * n_lon)
    )


def coarse_solve(block_sum, n_lat, n_lon):
    highest = lax.Precision.HIGHEST
    tab_rad = cosine_table(block_sum.shape[0])[0]
    tab_lat = cosine_table(n_lat)[0]
    tab_lon = cosine_table(n_lon)[0]
    spectrum = jnp.einsum("kr,rlo->klo", tab_rad, block_sum, precision=highest)
    spectrum = jnp.einsum("kl,rlo->rko", tab_lat, spectrum, precision=highest)
    spectrum = jnp.einsum("ko,rlo->rlk", tab_lon, spectrum, precision=highest)
    spectrum = spectrum / coarse_divisor(block_sum.shape[0], n_lat, n_lon)
    restored = jnp.einsum("kr,klo->rlo", tab_rad, spectrum, precision=highest)
    restored = jnp.einsum("kl,rko->rlo", tab_lat, restored, precision=highest)
    restored = jnp.einsum("ko,rlk->rlo", tab_lon, restored, precision=highest)
    return restored / math.sqrt(n_lat * n_lon)


def fractions(weight_ids):
    frac_lat = ((weight_ids // WQ).astype(jnp.float32) + 0.5) / WQ
    frac_lon = ((weight_ids % WQ).astype(jnp.float32) + 0.5) / WQ
    return (frac_lat, frac_lon)


def bilinear(lower_left, lower_right, upper_left, upper_right, frac_lat, frac_lon):
    return (
        (1.0 - frac_lat) * (1.0 - frac_lon) * lower_left
        + (1.0 - frac_lat) * frac_lon * lower_right
        + frac_lat * (1.0 - frac_lon) * upper_left
        + frac_lat * frac_lon * upper_right
    )


def shards(fields, viscosity, partner, src_row, src_col, weight_id, border_angle, dest_cell):
    n_lat = lax.axis_size("lat")
    n_lon = lax.axis_size("lon")
    lat_pos = lax.axis_index("lat")
    lon_pos = lax.axis_index("lon")
    own_fields = fields[0]
    levels, rows_dev, cols_dev = (own_fields.shape[1], own_fields.shape[2], own_fields.shape[3])
    channels = 6 * levels
    blocks = partner.shape[2]
    block_cells = src_row.shape[2] // blocks
    capacity = CAP
    slot_count = n_lon * capacity
    total_rows = rows_dev * n_lat
    flat_cells = own_fields.reshape(channels, rows_dev * cols_dev)
    target = partner[0, 0, :, 0]
    onehot = (target[:, None] == jnp.arange(n_lon, dtype=jnp.int32)[None, :]).astype(jnp.int32)
    before = jnp.sum(
        (jnp.cumsum(onehot, axis=0, dtype=jnp.int32) - onehot) * onehot, axis=1, dtype=jnp.int32
    )
    slot_of = target * capacity + before
    base_cell = (src_row[0, 0] * cols_dev + src_col[0, 0]).reshape(blocks, block_cells)
    weight_ids = weight_id[0, 0].reshape(blocks, block_cells)
    empty = jnp.zeros((slot_count, block_cells), jnp.int32)
    asked = jnp.stack(
        [empty.at[slot_of].set(base_cell), empty.at[slot_of].set(weight_ids)], axis=1
    ).reshape(n_lon, capacity, 2, block_cells)
    panel_pos = lax.axis_index("panel")
    panel_count = lax.axis_size("panel")
    mine = jnp.arange(panel_count, dtype=jnp.int32) != panel_pos
    routed = jnp.where(mine[:, None, None, None, None], asked[None], 0)
    routed = routed.reshape((panel_count * n_lon,) + asked.shape[1:])
    slot_mirror = partner_2(slot_of, "panel", 0)
    routed = lax.all_to_all(routed, ("panel", "lon"), split_axis=0, concat_axis=0, tiled=True)
    routed = routed.reshape((panel_count, n_lon) + asked.shape[1:])
    requests = jnp.sum(jnp.where(mine[:, None, None, None, None], routed, 0), axis=0)
    cells_asked = requests[:, :, 0, :].reshape(-1)
    frac_lat, frac_lon = fractions(requests[:, :, 1, :].reshape(-1))
    weights = jnp.stack(
        [
            (1.0 - frac_lat) * (1.0 - frac_lon),
            (1.0 - frac_lat) * frac_lon,
            frac_lat * (1.0 - frac_lon),
            frac_lat * frac_lon,
        ],
        axis=0,
    )
    served = corner_blend(flat_cells.T, cells_asked, weights, cols_dev)
    served = served.reshape(n_lon, capacity, block_cells, channels)
    served = lax.all_to_all(served, "lon", split_axis=0, concat_axis=0, tiled=True)
    served = served.reshape(slot_count, block_cells, channels)[slot_mirror]
    values = partner_2(served, "panel", 0)
    values = values.reshape(blocks * block_cells, channels).T.reshape(6, levels, blocks * block_cells)
    turn = border_angle[0, 0]
    cos_angle = jnp.cos(turn)
    sin_angle = jnp.sin(turn)
    rotated = jnp.stack(
        [
            values[0],
            cos_angle * values[1] + sin_angle * values[2],
            cos_angle * values[2] - sin_angle * values[1],
            values[3],
            cos_angle * values[4] + sin_angle * values[5],
            cos_angle * values[5] - sin_angle * values[4],
        ],
        axis=0,
    ).reshape(channels, blocks * block_cells)
    filled = flat_cells.at[:, dest_cell[0, 0]].set(rotated).reshape(6, levels, rows_dev, cols_dev)
    diffusivity = viscosity[0]
    inv_own, gain_own = metric(
        lat_pos * rows_dev + jnp.arange(-0, rows_dev + 0, dtype=jnp.int32), total_rows
    )
    halo = 3
    total_cols = cols_dev * n_lon
    row_first = lat_pos * rows_dev
    col_first = lon_pos * cols_dev

    def inside(reach):
        rows = row_first - reach + jnp.arange(rows_dev + 2 * reach, dtype=jnp.int32)
        cols = col_first - reach + jnp.arange(cols_dev + 2 * reach, dtype=jnp.int32)
        return ((rows >= 0) & (rows < total_rows))[:, None] & ((cols >= 0) & (cols < total_cols))[
            None, :
        ]

    stack = jnp.concatenate([filled.reshape(channels, rows_dev, cols_dev), diffusivity], axis=0)
    wide = padded_2(stack, (("lat", 1), ("lon", 2)), halo)
    wide_fields = wide[:channels].reshape(6, levels, rows_dev + 2 * halo, cols_dev + 2 * halo)
    wide_visc = wide[channels:]
    inv_two, gain_two = metric(row_first + jnp.arange(-2, rows_dev + 2, dtype=jnp.int32), total_rows)
    inv_one, gain_one = metric(row_first + jnp.arange(-1, rows_dev + 1, dtype=jnp.int32), total_rows)
    centre = wide_fields[..., 1:-1, 1:-1]
    stepped_wide = centre + wide_visc[None, :, 1:-1, 1:-1] * lap_shrink(wide_fields, gain_two)
    stepped_wide = jnp.concatenate(
        [stepped_wide[0:1] + BUOYANCY * centre[3:4], stepped_wide[1:]], axis=0
    )
    velocity = jnp.where(inside(2), stepped_wide[0:3], 0.0)
    divergence_wide = diverge(velocity, inv_one)
    press_wide = jnp.where(inside(1), -divergence_wide / (4.0 + 2.0 * gain_one)[:, None], 0.0)
    divergence = divergence_wide[:, 1:-1, 1:-1]
    press_one = press_wide[:, 1:-1, 1:-1]
    stepped = stepped_wide[:, :, 2:-2, 2:-2]
    resid_one = -divergence + lap_shrink(press_wide, gain_own)
    block_sum = jnp.sum(resid_one, axis=(1, 2)) * (1.0 / math.sqrt(rows_dev * cols_dev))
    gathered = gather_by_exchange(block_sum[None], "lon")
    gathered = gather_by_exchange(gathered[None], "lat")
    coarse = coarse_solve(jnp.transpose(gathered, (2, 0, 1)), n_lat, n_lon)
    start = jnp.zeros((), jnp.int32)
    near = lax.dynamic_slice(
        jnp.pad(coarse, ((0, 0), (1, 1), (1, 1))), (start, lat_pos, lon_pos), (levels, 3, 3)
    )
    own_coarse = near[:, 1, 1]
    pressure = press_one + own_coarse[:, None, None]
    row_at = lax.broadcasted_iota(jnp.int32, (rows_dev + 2, cols_dev + 2), 0)
    col_at = lax.broadcasted_iota(jnp.int32, (rows_dev + 2, cols_dev + 2), 1)
    rim_coarse = jnp.where(
        row_at == 0,
        near[:, 0, 1][:, None, None],
        jnp.where(
            row_at == rows_dev + 1,
            near[:, 2, 1][:, None, None],
            jnp.where(
                col_at == 0,
                near[:, 1, 0][:, None, None],
                jnp.where(
                    col_at == cols_dev + 1, near[:, 1, 2][:, None, None], own_coarse[:, None, None]
                ),
            ),
        ),
    )
    press_rim = press_wide + rim_coarse
    grad_rad, grad_lat, grad_lon = gradient(press_rim, inv_own)
    result = jnp.stack(
        [
            stepped[0] - grad_rad,
            stepped[1] - grad_lat,
            stepped[2] - grad_lon,
            stepped[3],
            stepped[4],
            stepped[5],
        ],
        axis=0,
    )
    return (result[None], pressure[None])


def solution(mesh):
    return jax.shard_map(
        shards,
        mesh=mesh,
        in_specs=(
            P("panel", None, None, "lat", "lon"),
            P("panel", None, "lat", "lon"),
            P("panel", "lat", "lon", None),
            P("panel", "lat", "lon"),
            P("panel", "lat", "lon"),
            P("panel", "lat", "lon"),
            P("panel", "lat", "lon"),
            P("panel", "lat", "lon"),
        ),
        out_specs=(P("panel", None, None, "lat", "lon"), P("panel", None, "lat", "lon")),
        check_vma=False,
    )
```

```python
import math

import jax
import jax.numpy as jnp
from jax import lax
from jax.experimental import pallas as pl
from jax.experimental.pallas import tpu as pltpu
from jax.sharding import PartitionSpec as P

CAP = 2
WQ = 8


BUOYANCY = 0.5


def partner_2(block, axis, apart):
    count = lax.axis_size(axis)
    route = []
    for low in range(count):
        high = low | 1 << apart
        if high != low and high < count:
            route += [(low, high), (high, low)]
    return lax.ppermute(block, axis, route)


def padded_2(shard, sides, width):
    for axis, dim in sides:
        size, length = (lax.axis_size(axis), shard.shape[dim])
        up = [(i, (i + 1) % size) for i in range(size - 1)]
        down = [(j, i) for i, j in up]
        last = lax.slice_in_dim(shard, length - width, length, axis=dim)
        leading = lax.slice_in_dim(shard, 0, width, axis=dim)
        before = lax.ppermute(last, axis, up)
        after = lax.ppermute(leading, axis, down)
        shard = jnp.concatenate([before, shard, after], axis=dim)
    return shard


def gather_by_exchange(block, axis):
    count = lax.axis_size(axis)
    repeated = jnp.broadcast_to(block[None], (count,) + block.shape)
    gathered = lax.all_to_all(repeated, axis, split_axis=0, concat_axis=0, tiled=True)
    return gathered.reshape((count * block.shape[0],) + block.shape[1:])


def corner_blend(table, rows, weights, width):
    count = rows.shape[0]

    def kernel(rows_ref, weights_ref, table_ref, out_ref):
        def body(t, carry):
            at = rows_ref[t]
            total = weights_ref[0, t] * table_ref[pl.ds(at, 1), :]
            for k, offset in enumerate((1, width, width + 1)):
                total = total + weights_ref[k + 1, t] * table_ref[pl.ds(at + offset, 1), :]
            out_ref[pl.ds(t, 1), :] = total
            return carry

        lax.fori_loop(0, count, body, 0, unroll=16)

    return pl.pallas_call(
        kernel,
        out_shape=jax.ShapeDtypeStruct((count, table.shape[1]), table.dtype),
        in_specs=[
            pl.BlockSpec(memory_space=pltpu.SMEM),
            pl.BlockSpec(memory_space=pltpu.SMEM),
            pl.BlockSpec(memory_space=pltpu.VMEM),
        ],
        out_specs=pl.BlockSpec(memory_space=pltpu.VMEM),
    )(rows, weights, table)


def metric(row_index, total_rows):
    colatitude = (
        math.pi / 4.0 + (row_index.astype(jnp.float32) + 0.5) * (math.pi / 2.0) / total_rows
    )
    inv_sine = 1.0 / jnp.sin(colatitude)
    return (inv_sine, inv_sine * inv_sine)


def lap_shrink(field, row_gain):
    centre = field[..., 1:-1, 1:-1]
    padded = jnp.pad(centre, [(0, 0)] * (centre.ndim - 3) + [(1, 1), (0, 0), (0, 0)])
    lat_term = field[..., 2:, 1:-1] + field[..., :-2, 1:-1] - 2.0 * centre
    lon_term = field[..., 1:-1, 2:] + field[..., 1:-1, :-2] - 2.0 * centre
    radial = padded[..., 2:, :, :] + padded[..., :-2, :, :] - 2.0 * centre
    return lat_term + row_gain[:, None] * lon_term + radial


def diverge(velocity, inv_sine):
    radial_pad = jnp.pad(velocity[0, :, 1:-1, 1:-1], ((1, 1), (0, 0), (0, 0)))
    lat_part = velocity[1, :, 2:, 1:-1] - velocity[1, :, :-2, 1:-1]
    lon_part = velocity[2, :, 1:-1, 2:] - velocity[2, :, 1:-1, :-2]
    rad_part = radial_pad[2:] - radial_pad[:-2]
    return 0.5 * (lat_part + inv_sine[:, None] * lon_part + rad_part)


def gradient(pressure, inv_sine):
    radial_pad = jnp.pad(pressure[:, 1:-1, 1:-1], ((1, 1), (0, 0), (0, 0)))
    grad_rad = 0.5 * (radial_pad[2:] - radial_pad[:-2])
    grad_lat = 0.5 * (pressure[:, 2:, 1:-1] - pressure[:, :-2, 1:-1])
    grad_lon = 0.5 * inv_sine[:, None] * (pressure[:, 1:-1, 2:] - pressure[:, 1:-1, :-2])
    return (grad_rad, grad_lat, grad_lon)


def cosine_table(length):
    mode_ids = jnp.arange(length, dtype=jnp.float32)
    cell_mid = jnp.arange(length, dtype=jnp.float32) + 0.5
    row_norm = jnp.sqrt(jnp.where(mode_ids > 0, 2.0, 1.0) / length)
    cos_table = row_norm[:, None] * jnp.cos(
        math.pi * mode_ids[:, None] * cell_mid[None, :] / length
    )
    eigenvalue = 4.0 * jnp.sin(math.pi * mode_ids / (2.0 * length)) ** 2
    return (cos_table, eigenvalue)


def coarse_divisor(levels, n_lat, n_lon):
    eig_rad = cosine_table(levels)[1]
    eig_lat = cosine_table(n_lat)[1]
    eig_lon = cosine_table(n_lon)[1]
    return (
        eig_rad[:, None, None]
        + eig_lat[None, :, None]
        + eig_lon[None, None, :]
        + 1.0 / (n_lat * n_lon)
    )


def coarse_solve(block_sum, n_lat, n_lon):
    highest = lax.Precision.HIGHEST
    tab_rad = cosine_table(block_sum.shape[0])[0]
    tab_lat = cosine_table(n_lat)[0]
    tab_lon = cosine_table(n_lon)[0]
    spectrum = jnp.einsum("kr,rlo->klo", tab_rad, block_sum, precision=highest)
    spectrum = jnp.einsum("kl,rlo->rko", tab_lat, spectrum, precision=highest)
    spectrum = jnp.einsum("ko,rlo->rlk", tab_lon, spectrum, precision=highest)
    spectrum = spectrum / coarse_divisor(block_sum.shape[0], n_lat, n_lon)
    restored = jnp.einsum("kr,klo->rlo", tab_rad, spectrum, precision=highest)
    restored = jnp.einsum("kl,rko->rlo", tab_lat, restored, precision=highest)
    restored = jnp.einsum("ko,rlk->rlo", tab_lon, restored, precision=highest)
    return restored / math.sqrt(n_lat * n_lon)


def fractions(weight_ids):
    frac_lat = ((weight_ids // WQ).astype(jnp.float32) + 0.5) / WQ
    frac_lon = ((weight_ids % WQ).astype(jnp.float32) + 0.5) / WQ
    return (frac_lat, frac_lon)


def bilinear(lower_left, lower_right, upper_left, upper_right, frac_lat, frac_lon):
    return (
        (1.0 - frac_lat) * (1.0 - frac_lon) * lower_left
        + (1.0 - frac_lat) * frac_lon * lower_right
        + frac_lat * (1.0 - frac_lon) * upper_left
        + frac_lat * frac_lon * upper_right
    )


def shards(fields, viscosity, partner, src_row, src_col, weight_id, border_angle, dest_cell):
    n_lat = lax.axis_size("lat")
    n_lon = lax.axis_size("lon")
    lat_pos = lax.axis_index("lat")
    lon_pos = lax.axis_index("lon")
    own_fields = fields[0]
    levels, rows_dev, cols_dev = (own_fields.shape[1], own_fields.shape[2], own_fields.shape[3])
    channels = 6 * levels
    blocks = partner.shape[2]
    block_cells = src_row.shape[2] // blocks
    capacity = CAP
    slot_count = n_lon * capacity
    total_rows = rows_dev * n_lat
    flat_cells = own_fields.reshape(channels, rows_dev * cols_dev)
    target = partner[0, 0, :, 0]
    onehot = (target[:, None] == jnp.arange(n_lon, dtype=jnp.int32)[None, :]).astype(jnp.int32)
    before = jnp.sum(
        (jnp.cumsum(onehot, axis=0, dtype=jnp.int32) - onehot) * onehot, axis=1, dtype=jnp.int32
    )
    slot_of = target * capacity + before
    base_cell = (src_row[0, 0] * cols_dev + src_col[0, 0]).reshape(blocks, block_cells)
    weight_ids = weight_id[0, 0].reshape(blocks, block_cells)
    empty = jnp.zeros((slot_count, block_cells), jnp.int32)
    slot_row = jnp.broadcast_to(jnp.pad(slot_of, (0, block_cells - blocks)), empty.shape)
    asked = jnp.stack(
        [empty.at[slot_of].set(base_cell), empty.at[slot_of].set(weight_ids), slot_row], axis=1
    ).reshape(n_lon, capacity, 3, block_cells)
    panel_pos = lax.axis_index("panel")
    panel_count = lax.axis_size("panel")
    mine = jnp.arange(panel_count, dtype=jnp.int32) != panel_pos
    routed = jnp.where(mine[:, None, None, None, None], asked[None], 0)
    routed = routed.reshape((panel_count * n_lon,) + asked.shape[1:])
    routed = lax.all_to_all(routed, ("panel", "lon"), split_axis=0, concat_axis=0, tiled=True)
    routed = routed.reshape((panel_count, n_lon) + asked.shape[1:])
    requests = jnp.sum(jnp.where(mine[:, None, None, None, None], routed, 0), axis=0)
    slot_mirror = lax.dynamic_index_in_dim(requests, lon_pos, 0, keepdims=False)[0, 2, :blocks]
    cells_asked = requests[:, :, 0, :].reshape(-1)
    frac_lat, frac_lon = fractions(requests[:, :, 1, :].reshape(-1))
    weights = jnp.stack(
        [
            (1.0 - frac_lat) * (1.0 - frac_lon),
            (1.0 - frac_lat) * frac_lon,
            frac_lat * (1.0 - frac_lon),
            frac_lat * frac_lon,
        ],
        axis=0,
    )
    served = corner_blend(flat_cells.T, cells_asked, weights, cols_dev)
    served = served.reshape(n_lon, capacity, block_cells, channels)
    served = lax.all_to_all(served, "lon", split_axis=0, concat_axis=0, tiled=True)
    served = served.reshape(slot_count, block_cells, channels)[slot_mirror]
    values = partner_2(served, "panel", 0)
    values = values.reshape(blocks * block_cells, channels).T.reshape(6, levels, blocks * block_cells)
    turn = border_angle[0, 0]
    cos_angle = jnp.cos(turn)
    sin_angle = jnp.sin(turn)
    rotated = jnp.stack(
        [
            values[0],
            cos_angle * values[1] + sin_angle * values[2],
            cos_angle * values[2] - sin_angle * values[1],
            values[3],
            cos_angle * values[4] + sin_angle * values[5],
            cos_angle * values[5] - sin_angle * values[4],
        ],
        axis=0,
    ).reshape(channels, blocks * block_cells)
    filled = flat_cells.at[:, dest_cell[0, 0]].set(rotated).reshape(6, levels, rows_dev, cols_dev)
    diffusivity = viscosity[0]
    inv_own, gain_own = metric(
        lat_pos * rows_dev + jnp.arange(-0, rows_dev + 0, dtype=jnp.int32), total_rows
    )
    halo = 3
    total_cols = cols_dev * n_lon
    row_first = lat_pos * rows_dev
    col_first = lon_pos * cols_dev

    def inside(reach):
        rows = row_first - reach + jnp.arange(rows_dev + 2 * reach, dtype=jnp.int32)
        cols = col_first - reach + jnp.arange(cols_dev + 2 * reach, dtype=jnp.int32)
        return ((rows >= 0) & (rows < total_rows))[:, None] & ((cols >= 0) & (cols < total_cols))[
            None, :
        ]

    stack = jnp.concatenate([filled.reshape(channels, rows_dev, cols_dev), diffusivity], axis=0)
    wide = padded_2(stack, (("lat", 1), ("lon", 2)), halo)
    wide_fields = wide[:channels].reshape(6, levels, rows_dev + 2 * halo, cols_dev + 2 * halo)
    wide_visc = wide[channels:]
    inv_two, gain_two = metric(row_first + jnp.arange(-2, rows_dev + 2, dtype=jnp.int32), total_rows)
    inv_one, gain_one = metric(row_first + jnp.arange(-1, rows_dev + 1, dtype=jnp.int32), total_rows)
    centre = wide_fields[..., 1:-1, 1:-1]
    stepped_wide = centre + wide_visc[None, :, 1:-1, 1:-1] * lap_shrink(wide_fields, gain_two)
    stepped_wide = jnp.concatenate(
        [stepped_wide[0:1] + BUOYANCY * centre[3:4], stepped_wide[1:]], axis=0
    )
    velocity = jnp.where(inside(2), stepped_wide[0:3], 0.0)
    divergence_wide = diverge(velocity, inv_one)
    press_wide = jnp.where(inside(1), -divergence_wide / (4.0 + 2.0 * gain_one)[:, None], 0.0)
    divergence = divergence_wide[:, 1:-1, 1:-1]
    press_one = press_wide[:, 1:-1, 1:-1]
    stepped = stepped_wide[:, :, 2:-2, 2:-2]
    resid_one = -divergence + lap_shrink(press_wide, gain_own)
    block_sum = jnp.sum(resid_one, axis=(1, 2)) * (1.0 / math.sqrt(rows_dev * cols_dev))
    gathered = gather_by_exchange(block_sum[None], "lon")
    gathered = gather_by_exchange(gathered[None], "lat")
    coarse = coarse_solve(jnp.transpose(gathered, (2, 0, 1)), n_lat, n_lon)
    start = jnp.zeros((), jnp.int32)
    near = lax.dynamic_slice(
        jnp.pad(coarse, ((0, 0), (1, 1), (1, 1))), (start, lat_pos, lon_pos), (levels, 3, 3)
    )
    own_coarse = near[:, 1, 1]
    pressure = press_one + own_coarse[:, None, None]
    row_at = lax.broadcasted_iota(jnp.int32, (rows_dev + 2, cols_dev + 2), 0)
    col_at = lax.broadcasted_iota(jnp.int32, (rows_dev + 2, cols_dev + 2), 1)
    rim_coarse = jnp.where(
        row_at == 0,
        near[:, 0, 1][:, None, None],
        jnp.where(
            row_at == rows_dev + 1,
            near[:, 2, 1][:, None, None],
            jnp.where(
                col_at == 0,
                near[:, 1, 0][:, None, None],
                jnp.where(
                    col_at == cols_dev + 1, near[:, 1, 2][:, None, None], own_coarse[:, None, None]
                ),
            ),
        ),
    )
    press_rim = press_wide + rim_coarse
    grad_rad, grad_lat, grad_lon = gradient(press_rim, inv_own)
    result = jnp.stack(
        [
            stepped[0] - grad_rad,
            stepped[1] - grad_lat,
            stepped[2] - grad_lon,
            stepped[3],
            stepped[4],
            stepped[5],
        ],
        axis=0,
    )
    return (result[None], pressure[None])


def solution(mesh):
    return jax.shard_map(
        shards,
        mesh=mesh,
        in_specs=(
            P("panel", None, None, "lat", "lon"),
            P("panel", None, "lat", "lon"),
            P("panel", "lat", "lon", None),
            P("panel", "lat", "lon"),
            P("panel", "lat", "lon"),
            P("panel", "lat", "lon"),
            P("panel", "lat", "lon"),
            P("panel", "lat", "lon"),
        ),
        out_specs=(P("panel", None, None, "lat", "lon"), P("panel", None, "lat", "lon")),
        check_vma=False,
    )
```

```python
import math

import jax
import jax.numpy as jnp
from jax import lax
from jax.experimental import pallas as pl
from jax.experimental.pallas import tpu as pltpu
from jax.sharding import PartitionSpec as P

CAP = 2
WQ = 8


BUOYANCY = 0.5


def partner_2(block, axis, apart):
    count = lax.axis_size(axis)
    route = []
    for low in range(count):
        high = low | 1 << apart
        if high != low and high < count:
            route += [(low, high), (high, low)]
    return lax.ppermute(block, axis, route)


def padded_2(shard, sides, width):
    for axis, dim in sides:
        size, length = (lax.axis_size(axis), shard.shape[dim])
        up = [(i, (i + 1) % size) for i in range(size - 1)]
        down = [(j, i) for i, j in up]
        last = lax.slice_in_dim(shard, length - width, length, axis=dim)
        leading = lax.slice_in_dim(shard, 0, width, axis=dim)
        before = lax.ppermute(last, axis, up)
        after = lax.ppermute(leading, axis, down)
        shard = jnp.concatenate([before, shard, after], axis=dim)
    return shard


def gather_by_exchange(block, axis):
    count = lax.axis_size(axis)
    repeated = jnp.broadcast_to(block[None], (count,) + block.shape)
    gathered = lax.all_to_all(repeated, axis, split_axis=0, concat_axis=0, tiled=True)
    return gathered.reshape((count * block.shape[0],) + block.shape[1:])


def corner_blend(table, rows, weights, width):
    count = rows.shape[0]

    def kernel(rows_ref, weights_ref, table_ref, out_ref):
        def body(t, carry):
            at = rows_ref[t]
            total = weights_ref[0, t] * table_ref[pl.ds(at, 1), :]
            for k, offset in enumerate((1, width, width + 1)):
                total = total + weights_ref[k + 1, t] * table_ref[pl.ds(at + offset, 1), :]
            out_ref[pl.ds(t, 1), :] = total
            return carry

        lax.fori_loop(0, count, body, 0, unroll=16)

    return pl.pallas_call(
        kernel,
        out_shape=jax.ShapeDtypeStruct((count, table.shape[1]), table.dtype),
        in_specs=[
            pl.BlockSpec(memory_space=pltpu.SMEM),
            pl.BlockSpec(memory_space=pltpu.SMEM),
            pl.BlockSpec(memory_space=pltpu.VMEM),
        ],
        out_specs=pl.BlockSpec(memory_space=pltpu.VMEM),
    )(rows, weights, table)


def metric(row_index, total_rows):
    colatitude = (
        math.pi / 4.0 + (row_index.astype(jnp.float32) + 0.5) * (math.pi / 2.0) / total_rows
    )
    inv_sine = 1.0 / jnp.sin(colatitude)
    return (inv_sine, inv_sine * inv_sine)


def lap_shrink(field, row_gain):
    centre = field[..., 1:-1, 1:-1]
    padded = jnp.pad(centre, [(0, 0)] * (centre.ndim - 3) + [(1, 1), (0, 0), (0, 0)])
    lat_term = field[..., 2:, 1:-1] + field[..., :-2, 1:-1] - 2.0 * centre
    lon_term = field[..., 1:-1, 2:] + field[..., 1:-1, :-2] - 2.0 * centre
    radial = padded[..., 2:, :, :] + padded[..., :-2, :, :] - 2.0 * centre
    return lat_term + row_gain[:, None] * lon_term + radial


def diverge(velocity, inv_sine):
    radial_pad = jnp.pad(velocity[0, :, 1:-1, 1:-1], ((1, 1), (0, 0), (0, 0)))
    lat_part = velocity[1, :, 2:, 1:-1] - velocity[1, :, :-2, 1:-1]
    lon_part = velocity[2, :, 1:-1, 2:] - velocity[2, :, 1:-1, :-2]
    rad_part = radial_pad[2:] - radial_pad[:-2]
    return 0.5 * (lat_part + inv_sine[:, None] * lon_part + rad_part)


def gradient(pressure, inv_sine):
    radial_pad = jnp.pad(pressure[:, 1:-1, 1:-1], ((1, 1), (0, 0), (0, 0)))
    grad_rad = 0.5 * (radial_pad[2:] - radial_pad[:-2])
    grad_lat = 0.5 * (pressure[:, 2:, 1:-1] - pressure[:, :-2, 1:-1])
    grad_lon = 0.5 * inv_sine[:, None] * (pressure[:, 1:-1, 2:] - pressure[:, 1:-1, :-2])
    return (grad_rad, grad_lat, grad_lon)


def cosine_table(length):
    mode_ids = jnp.arange(length, dtype=jnp.float32)
    cell_mid = jnp.arange(length, dtype=jnp.float32) + 0.5
    row_norm = jnp.sqrt(jnp.where(mode_ids > 0, 2.0, 1.0) / length)
    cos_table = row_norm[:, None] * jnp.cos(
        math.pi * mode_ids[:, None] * cell_mid[None, :] / length
    )
    eigenvalue = 4.0 * jnp.sin(math.pi * mode_ids / (2.0 * length)) ** 2
    return (cos_table, eigenvalue)


def coarse_divisor(levels, n_lat, n_lon):
    eig_rad = cosine_table(levels)[1]
    eig_lat = cosine_table(n_lat)[1]
    eig_lon = cosine_table(n_lon)[1]
    return (
        eig_rad[:, None, None]
        + eig_lat[None, :, None]
        + eig_lon[None, None, :]
        + 1.0 / (n_lat * n_lon)
    )


def coarse_solve(block_sum, n_lat, n_lon):
    highest = lax.Precision.HIGHEST
    tab_rad = cosine_table(block_sum.shape[0])[0]
    tab_lat = cosine_table(n_lat)[0]
    tab_lon = cosine_table(n_lon)[0]
    spectrum = jnp.einsum("kr,rlo->klo", tab_rad, block_sum, precision=highest)
    spectrum = jnp.einsum("kl,rlo->rko", tab_lat, spectrum, precision=highest)
    spectrum = jnp.einsum("ko,rlo->rlk", tab_lon, spectrum, precision=highest)
    spectrum = spectrum / coarse_divisor(block_sum.shape[0], n_lat, n_lon)
    restored = jnp.einsum("kr,klo->rlo", tab_rad, spectrum, precision=highest)
    restored = jnp.einsum("kl,rko->rlo", tab_lat, restored, precision=highest)
    restored = jnp.einsum("ko,rlk->rlo", tab_lon, restored, precision=highest)
    return restored / math.sqrt(n_lat * n_lon)


def fractions(weight_ids):
    frac_lat = ((weight_ids // WQ).astype(jnp.float32) + 0.5) / WQ
    frac_lon = ((weight_ids % WQ).astype(jnp.float32) + 0.5) / WQ
    return (frac_lat, frac_lon)


def bilinear(lower_left, lower_right, upper_left, upper_right, frac_lat, frac_lon):
    return (
        (1.0 - frac_lat) * (1.0 - frac_lon) * lower_left
        + (1.0 - frac_lat) * frac_lon * lower_right
        + frac_lat * (1.0 - frac_lon) * upper_left
        + frac_lat * frac_lon * upper_right
    )


def shards(fields, viscosity, partner, src_row, src_col, weight_id, border_angle, dest_cell):
    n_lat = lax.axis_size("lat")
    n_lon = lax.axis_size("lon")
    lat_pos = lax.axis_index("lat")
    lon_pos = lax.axis_index("lon")
    own_fields = fields[0]
    levels, rows_dev, cols_dev = (own_fields.shape[1], own_fields.shape[2], own_fields.shape[3])
    channels = 6 * levels
    blocks = partner.shape[2]
    block_cells = src_row.shape[2] // blocks
    capacity = CAP
    slot_count = n_lon * capacity
    total_rows = rows_dev * n_lat
    flat_cells = own_fields.reshape(channels, rows_dev * cols_dev)
    target = partner[0, 0, :, 0]
    onehot = (target[:, None] == jnp.arange(n_lon, dtype=jnp.int32)[None, :]).astype(jnp.int32)
    before = jnp.sum(
        (jnp.cumsum(onehot, axis=0, dtype=jnp.int32) - onehot) * onehot, axis=1, dtype=jnp.int32
    )
    slot_of = target * capacity + before
    base_cell = (src_row[0, 0] * cols_dev + src_col[0, 0]).reshape(blocks, block_cells)
    weight_ids = weight_id[0, 0].reshape(blocks, block_cells)
    empty = jnp.zeros((slot_count, block_cells), jnp.int32)
    asked = jnp.stack(
        [empty.at[slot_of].set(base_cell), empty.at[slot_of].set(weight_ids)], axis=1
    ).reshape(n_lon, capacity, 2, block_cells)
    panel_pos = lax.axis_index("panel")
    panel_count = lax.axis_size("panel")
    mine = jnp.arange(panel_count, dtype=jnp.int32) != panel_pos
    routed = jnp.where(mine[:, None, None, None, None], asked[None], 0)
    routed = routed.reshape((panel_count * n_lon,) + asked.shape[1:])
    routed = lax.all_to_all(routed, ("panel", "lon"), split_axis=0, concat_axis=0, tiled=True)
    routed = routed.reshape((panel_count, n_lon) + asked.shape[1:])
    requests = jnp.sum(jnp.where(mine[:, None, None, None, None], routed, 0), axis=0)
    cells_asked = requests[:, :, 0, :].reshape(-1)
    frac_lat, frac_lon = fractions(requests[:, :, 1, :].reshape(-1))
    weights = jnp.stack(
        [
            (1.0 - frac_lat) * (1.0 - frac_lon),
            (1.0 - frac_lat) * frac_lon,
            frac_lat * (1.0 - frac_lon),
            frac_lat * frac_lon,
        ],
        axis=0,
    )
    served = corner_blend(flat_cells.T, cells_asked, weights, cols_dev)
    served = served.reshape(n_lon, capacity, block_cells, channels)
    sent = jnp.where(mine[:, None, None, None, None], served[None], 0.0)
    sent = sent.reshape((panel_count * n_lon,) + served.shape[1:])
    sent = lax.all_to_all(sent, ("panel", "lon"), split_axis=0, concat_axis=0, tiled=True)
    sent = sent.reshape((panel_count, n_lon) + served.shape[1:])
    back = lax.dynamic_index_in_dim(sent, 1 - panel_pos, 0, keepdims=False)
    values = back.reshape(slot_count, block_cells, channels)[slot_of]
    values = values.reshape(blocks * block_cells, channels).T.reshape(6, levels, blocks * block_cells)
    turn = border_angle[0, 0]
    cos_angle = jnp.cos(turn)
    sin_angle = jnp.sin(turn)
    rotated = jnp.stack(
        [
            values[0],
            cos_angle * values[1] + sin_angle * values[2],
            cos_angle * values[2] - sin_angle * values[1],
            values[3],
            cos_angle * values[4] + sin_angle * values[5],
            cos_angle * values[5] - sin_angle * values[4],
        ],
        axis=0,
    ).reshape(channels, blocks * block_cells)
    filled = flat_cells.at[:, dest_cell[0, 0]].set(rotated).reshape(6, levels, rows_dev, cols_dev)
    diffusivity = viscosity[0]
    inv_own, gain_own = metric(
        lat_pos * rows_dev + jnp.arange(-0, rows_dev + 0, dtype=jnp.int32), total_rows
    )
    halo = 3
    total_cols = cols_dev * n_lon
    row_first = lat_pos * rows_dev
    col_first = lon_pos * cols_dev

    def inside(reach):
        rows = row_first - reach + jnp.arange(rows_dev + 2 * reach, dtype=jnp.int32)
        cols = col_first - reach + jnp.arange(cols_dev + 2 * reach, dtype=jnp.int32)
        return ((rows >= 0) & (rows < total_rows))[:, None] & ((cols >= 0) & (cols < total_cols))[
            None, :
        ]

    stack = jnp.concatenate([filled.reshape(channels, rows_dev, cols_dev), diffusivity], axis=0)
    wide = padded_2(stack, (("lat", 1), ("lon", 2)), halo)
    wide_fields = wide[:channels].reshape(6, levels, rows_dev + 2 * halo, cols_dev + 2 * halo)
    wide_visc = wide[channels:]
    inv_two, gain_two = metric(row_first + jnp.arange(-2, rows_dev + 2, dtype=jnp.int32), total_rows)
    inv_one, gain_one = metric(row_first + jnp.arange(-1, rows_dev + 1, dtype=jnp.int32), total_rows)
    centre = wide_fields[..., 1:-1, 1:-1]
    stepped_wide = centre + wide_visc[None, :, 1:-1, 1:-1] * lap_shrink(wide_fields, gain_two)
    stepped_wide = jnp.concatenate(
        [stepped_wide[0:1] + BUOYANCY * centre[3:4], stepped_wide[1:]], axis=0
    )
    velocity = jnp.where(inside(2), stepped_wide[0:3], 0.0)
    divergence_wide = diverge(velocity, inv_one)
    press_wide = jnp.where(inside(1), -divergence_wide / (4.0 + 2.0 * gain_one)[:, None], 0.0)
    divergence = divergence_wide[:, 1:-1, 1:-1]
    press_one = press_wide[:, 1:-1, 1:-1]
    stepped = stepped_wide[:, :, 2:-2, 2:-2]
    resid_one = -divergence + lap_shrink(press_wide, gain_own)
    block_sum = jnp.sum(resid_one, axis=(1, 2)) * (1.0 / math.sqrt(rows_dev * cols_dev))
    gathered = gather_by_exchange(block_sum[None], "lon")
    gathered = gather_by_exchange(gathered[None], "lat")
    coarse = coarse_solve(jnp.transpose(gathered, (2, 0, 1)), n_lat, n_lon)
    start = jnp.zeros((), jnp.int32)
    near = lax.dynamic_slice(
        jnp.pad(coarse, ((0, 0), (1, 1), (1, 1))), (start, lat_pos, lon_pos), (levels, 3, 3)
    )
    own_coarse = near[:, 1, 1]
    pressure = press_one + own_coarse[:, None, None]
    row_at = lax.broadcasted_iota(jnp.int32, (rows_dev + 2, cols_dev + 2), 0)
    col_at = lax.broadcasted_iota(jnp.int32, (rows_dev + 2, cols_dev + 2), 1)
    rim_coarse = jnp.where(
        row_at == 0,
        near[:, 0, 1][:, None, None],
        jnp.where(
            row_at == rows_dev + 1,
            near[:, 2, 1][:, None, None],
            jnp.where(
                col_at == 0,
                near[:, 1, 0][:, None, None],
                jnp.where(
                    col_at == cols_dev + 1, near[:, 1, 2][:, None, None], own_coarse[:, None, None]
                ),
            ),
        ),
    )
    press_rim = press_wide + rim_coarse
    grad_rad, grad_lat, grad_lon = gradient(press_rim, inv_own)
    result = jnp.stack(
        [
            stepped[0] - grad_rad,
            stepped[1] - grad_lat,
            stepped[2] - grad_lon,
            stepped[3],
            stepped[4],
            stepped[5],
        ],
        axis=0,
    )
    return (result[None], pressure[None])


def solution(mesh):
    return jax.shard_map(
        shards,
        mesh=mesh,
        in_specs=(
            P("panel", None, None, "lat", "lon"),
            P("panel", None, "lat", "lon"),
            P("panel", "lat", "lon", None),
            P("panel", "lat", "lon"),
            P("panel", "lat", "lon"),
            P("panel", "lat", "lon"),
            P("panel", "lat", "lon"),
            P("panel", "lat", "lon"),
        ),
        out_specs=(P("panel", None, None, "lat", "lon"), P("panel", None, "lat", "lon")),
        check_vma=False,
    )
```

```python
import math

import jax
import jax.numpy as jnp
from jax import lax
from jax.experimental import pallas as pl
from jax.experimental.pallas import tpu as pltpu
from jax.sharding import PartitionSpec as P

CAP = 2
WQ = 8


BUOYANCY = 0.5


def partner_2(block, axis, apart):
    count = lax.axis_size(axis)
    route = []
    for low in range(count):
        high = low | 1 << apart
        if high != low and high < count:
            route += [(low, high), (high, low)]
    return lax.ppermute(block, axis, route)


def padded_2(shard, sides, width):
    for axis, dim in sides:
        size, length = (lax.axis_size(axis), shard.shape[dim])
        up = [(i, (i + 1) % size) for i in range(size - 1)]
        down = [(j, i) for i, j in up]
        last = lax.slice_in_dim(shard, length - width, length, axis=dim)
        leading = lax.slice_in_dim(shard, 0, width, axis=dim)
        before = lax.ppermute(last, axis, up)
        after = lax.ppermute(leading, axis, down)
        shard = jnp.concatenate([before, shard, after], axis=dim)
    return shard


def gather_by_exchange(block, axis):
    count = lax.axis_size(axis)
    repeated = jnp.broadcast_to(block[None], (count,) + block.shape)
    gathered = lax.all_to_all(repeated, axis, split_axis=0, concat_axis=0, tiled=True)
    return gathered.reshape((count * block.shape[0],) + block.shape[1:])


def corner_blend(table, rows, weights, width):
    count = rows.shape[0]

    def kernel(rows_ref, weights_ref, table_ref, out_ref):
        def body(t, carry):
            at = rows_ref[t]
            total = weights_ref[0, t] * table_ref[pl.ds(at, 1), :]
            for k, offset in enumerate((1, width, width + 1)):
                total = total + weights_ref[k + 1, t] * table_ref[pl.ds(at + offset, 1), :]
            out_ref[pl.ds(t, 1), :] = total
            return carry

        lax.fori_loop(0, count, body, 0, unroll=32)

    return pl.pallas_call(
        kernel,
        out_shape=jax.ShapeDtypeStruct((count, table.shape[1]), table.dtype),
        in_specs=[
            pl.BlockSpec(memory_space=pltpu.SMEM),
            pl.BlockSpec(memory_space=pltpu.SMEM),
            pl.BlockSpec(memory_space=pltpu.VMEM),
        ],
        out_specs=pl.BlockSpec(memory_space=pltpu.VMEM),
    )(rows, weights, table)


def metric(row_index, total_rows):
    colatitude = (
        math.pi / 4.0 + (row_index.astype(jnp.float32) + 0.5) * (math.pi / 2.0) / total_rows
    )
    inv_sine = 1.0 / jnp.sin(colatitude)
    return (inv_sine, inv_sine * inv_sine)


def lap_shrink(field, row_gain):
    centre = field[..., 1:-1, 1:-1]
    padded = jnp.pad(centre, [(0, 0)] * (centre.ndim - 3) + [(1, 1), (0, 0), (0, 0)])
    lat_term = field[..., 2:, 1:-1] + field[..., :-2, 1:-1] - 2.0 * centre
    lon_term = field[..., 1:-1, 2:] + field[..., 1:-1, :-2] - 2.0 * centre
    radial = padded[..., 2:, :, :] + padded[..., :-2, :, :] - 2.0 * centre
    return lat_term + row_gain[:, None] * lon_term + radial


def diverge(velocity, inv_sine):
    radial_pad = jnp.pad(velocity[0, :, 1:-1, 1:-1], ((1, 1), (0, 0), (0, 0)))
    lat_part = velocity[1, :, 2:, 1:-1] - velocity[1, :, :-2, 1:-1]
    lon_part = velocity[2, :, 1:-1, 2:] - velocity[2, :, 1:-1, :-2]
    rad_part = radial_pad[2:] - radial_pad[:-2]
    return 0.5 * (lat_part + inv_sine[:, None] * lon_part + rad_part)


def gradient(pressure, inv_sine):
    radial_pad = jnp.pad(pressure[:, 1:-1, 1:-1], ((1, 1), (0, 0), (0, 0)))
    grad_rad = 0.5 * (radial_pad[2:] - radial_pad[:-2])
    grad_lat = 0.5 * (pressure[:, 2:, 1:-1] - pressure[:, :-2, 1:-1])
    grad_lon = 0.5 * inv_sine[:, None] * (pressure[:, 1:-1, 2:] - pressure[:, 1:-1, :-2])
    return (grad_rad, grad_lat, grad_lon)


def cosine_table(length):
    mode_ids = jnp.arange(length, dtype=jnp.float32)
    cell_mid = jnp.arange(length, dtype=jnp.float32) + 0.5
    row_norm = jnp.sqrt(jnp.where(mode_ids > 0, 2.0, 1.0) / length)
    cos_table = row_norm[:, None] * jnp.cos(
        math.pi * mode_ids[:, None] * cell_mid[None, :] / length
    )
    eigenvalue = 4.0 * jnp.sin(math.pi * mode_ids / (2.0 * length)) ** 2
    return (cos_table, eigenvalue)


def coarse_divisor(levels, n_lat, n_lon):
    eig_rad = cosine_table(levels)[1]
    eig_lat = cosine_table(n_lat)[1]
    eig_lon = cosine_table(n_lon)[1]
    return (
        eig_rad[:, None, None]
        + eig_lat[None, :, None]
        + eig_lon[None, None, :]
        + 1.0 / (n_lat * n_lon)
    )


def coarse_solve(block_sum, n_lat, n_lon):
    highest = lax.Precision.HIGHEST
    tab_rad = cosine_table(block_sum.shape[0])[0]
    tab_lat = cosine_table(n_lat)[0]
    tab_lon = cosine_table(n_lon)[0]
    spectrum = jnp.einsum("kr,rlo->klo", tab_rad, block_sum, precision=highest)
    spectrum = jnp.einsum("kl,rlo->rko", tab_lat, spectrum, precision=highest)
    spectrum = jnp.einsum("ko,rlo->rlk", tab_lon, spectrum, precision=highest)
    spectrum = spectrum / coarse_divisor(block_sum.shape[0], n_lat, n_lon)
    restored = jnp.einsum("kr,klo->rlo", tab_rad, spectrum, precision=highest)
    restored = jnp.einsum("kl,rko->rlo", tab_lat, restored, precision=highest)
    restored = jnp.einsum("ko,rlk->rlo", tab_lon, restored, precision=highest)
    return restored / math.sqrt(n_lat * n_lon)


def fractions(weight_ids):
    frac_lat = ((weight_ids // WQ).astype(jnp.float32) + 0.5) / WQ
    frac_lon = ((weight_ids % WQ).astype(jnp.float32) + 0.5) / WQ
    return (frac_lat, frac_lon)


def bilinear(lower_left, lower_right, upper_left, upper_right, frac_lat, frac_lon):
    return (
        (1.0 - frac_lat) * (1.0 - frac_lon) * lower_left
        + (1.0 - frac_lat) * frac_lon * lower_right
        + frac_lat * (1.0 - frac_lon) * upper_left
        + frac_lat * frac_lon * upper_right
    )


def shards(fields, viscosity, partner, src_row, src_col, weight_id, border_angle, dest_cell):
    n_lat = lax.axis_size("lat")
    n_lon = lax.axis_size("lon")
    lat_pos = lax.axis_index("lat")
    lon_pos = lax.axis_index("lon")
    own_fields = fields[0]
    levels, rows_dev, cols_dev = (own_fields.shape[1], own_fields.shape[2], own_fields.shape[3])
    channels = 6 * levels
    blocks = partner.shape[2]
    block_cells = src_row.shape[2] // blocks
    capacity = CAP
    slot_count = n_lon * capacity
    total_rows = rows_dev * n_lat
    flat_cells = own_fields.reshape(channels, rows_dev * cols_dev)
    target = partner[0, 0, :, 0]
    onehot = (target[:, None] == jnp.arange(n_lon, dtype=jnp.int32)[None, :]).astype(jnp.int32)
    before = jnp.sum(
        (jnp.cumsum(onehot, axis=0, dtype=jnp.int32) - onehot) * onehot, axis=1, dtype=jnp.int32
    )
    slot_of = target * capacity + before
    base_cell = (src_row[0, 0] * cols_dev + src_col[0, 0]).reshape(blocks, block_cells)
    weight_ids = weight_id[0, 0].reshape(blocks, block_cells)
    empty = jnp.zeros((slot_count, block_cells), jnp.int32)
    slot_row = jnp.broadcast_to(jnp.pad(slot_of, (0, block_cells - blocks)), empty.shape)
    asked = jnp.stack(
        [empty.at[slot_of].set(base_cell), empty.at[slot_of].set(weight_ids), slot_row], axis=1
    ).reshape(n_lon, capacity, 3, block_cells)
    panel_pos = lax.axis_index("panel")
    panel_count = lax.axis_size("panel")
    mine = jnp.arange(panel_count, dtype=jnp.int32) != panel_pos
    routed = jnp.where(mine[:, None, None, None, None], asked[None], 0)
    routed = routed.reshape((panel_count * n_lon,) + asked.shape[1:])
    routed = lax.all_to_all(routed, ("panel", "lon"), split_axis=0, concat_axis=0, tiled=True)
    routed = routed.reshape((panel_count, n_lon) + asked.shape[1:])
    requests = jnp.sum(jnp.where(mine[:, None, None, None, None], routed, 0), axis=0)
    slot_mirror = lax.dynamic_index_in_dim(requests, lon_pos, 0, keepdims=False)[0, 2, :blocks]
    cells_asked = requests[:, :, 0, :].reshape(-1)
    frac_lat, frac_lon = fractions(requests[:, :, 1, :].reshape(-1))
    weights = jnp.stack(
        [
            (1.0 - frac_lat) * (1.0 - frac_lon),
            (1.0 - frac_lat) * frac_lon,
            frac_lat * (1.0 - frac_lon),
            frac_lat * frac_lon,
        ],
        axis=0,
    )
    served = corner_blend(flat_cells.T, cells_asked, weights, cols_dev)
    served = served.reshape(n_lon, capacity, block_cells, channels)
    served = lax.all_to_all(served, "lon", split_axis=0, concat_axis=0, tiled=True)
    served = served.reshape(slot_count, block_cells, channels)[slot_mirror]
    values = partner_2(served, "panel", 0)
    values = values.reshape(blocks * block_cells, channels).T.reshape(6, levels, blocks * block_cells)
    turn = border_angle[0, 0]
    cos_angle = jnp.cos(turn)
    sin_angle = jnp.sin(turn)
    rotated = jnp.stack(
        [
            values[0],
            cos_angle * values[1] + sin_angle * values[2],
            cos_angle * values[2] - sin_angle * values[1],
            values[3],
            cos_angle * values[4] + sin_angle * values[5],
            cos_angle * values[5] - sin_angle * values[4],
        ],
        axis=0,
    ).reshape(channels, blocks * block_cells)
    filled = flat_cells.at[:, dest_cell[0, 0]].set(rotated).reshape(6, levels, rows_dev, cols_dev)
    diffusivity = viscosity[0]
    inv_own, gain_own = metric(
        lat_pos * rows_dev + jnp.arange(-0, rows_dev + 0, dtype=jnp.int32), total_rows
    )
    halo = 3
    total_cols = cols_dev * n_lon
    row_first = lat_pos * rows_dev
    col_first = lon_pos * cols_dev

    def inside(reach):
        rows = row_first - reach + jnp.arange(rows_dev + 2 * reach, dtype=jnp.int32)
        cols = col_first - reach + jnp.arange(cols_dev + 2 * reach, dtype=jnp.int32)
        return ((rows >= 0) & (rows < total_rows))[:, None] & ((cols >= 0) & (cols < total_cols))[
            None, :
        ]

    stack = jnp.concatenate([filled.reshape(channels, rows_dev, cols_dev), diffusivity], axis=0)
    wide = padded_2(stack, (("lat", 1), ("lon", 2)), halo)
    wide_fields = wide[:channels].reshape(6, levels, rows_dev + 2 * halo, cols_dev + 2 * halo)
    wide_visc = wide[channels:]
    inv_two, gain_two = metric(row_first + jnp.arange(-2, rows_dev + 2, dtype=jnp.int32), total_rows)
    inv_one, gain_one = metric(row_first + jnp.arange(-1, rows_dev + 1, dtype=jnp.int32), total_rows)
    centre = wide_fields[..., 1:-1, 1:-1]
    stepped_wide = centre + wide_visc[None, :, 1:-1, 1:-1] * lap_shrink(wide_fields, gain_two)
    stepped_wide = jnp.concatenate(
        [stepped_wide[0:1] + BUOYANCY * centre[3:4], stepped_wide[1:]], axis=0
    )
    velocity = jnp.where(inside(2), stepped_wide[0:3], 0.0)
    divergence_wide = diverge(velocity, inv_one)
    press_wide = jnp.where(inside(1), -divergence_wide / (4.0 + 2.0 * gain_one)[:, None], 0.0)
    divergence = divergence_wide[:, 1:-1, 1:-1]
    press_one = press_wide[:, 1:-1, 1:-1]
    stepped = stepped_wide[:, :, 2:-2, 2:-2]
    resid_one = -divergence + lap_shrink(press_wide, gain_own)
    block_sum = jnp.sum(resid_one, axis=(1, 2)) * (1.0 / math.sqrt(rows_dev * cols_dev))
    gathered = gather_by_exchange(block_sum[None], "lon")
    gathered = gather_by_exchange(gathered[None], "lat")
    coarse = coarse_solve(jnp.transpose(gathered, (2, 0, 1)), n_lat, n_lon)
    start = jnp.zeros((), jnp.int32)
    near = lax.dynamic_slice(
        jnp.pad(coarse, ((0, 0), (1, 1), (1, 1))), (start, lat_pos, lon_pos), (levels, 3, 3)
    )
    own_coarse = near[:, 1, 1]
    pressure = press_one + own_coarse[:, None, None]
    row_at = lax.broadcasted_iota(jnp.int32, (rows_dev + 2, cols_dev + 2), 0)
    col_at = lax.broadcasted_iota(jnp.int32, (rows_dev + 2, cols_dev + 2), 1)
    rim_coarse = jnp.where(
        row_at == 0,
        near[:, 0, 1][:, None, None],
        jnp.where(
            row_at == rows_dev + 1,
            near[:, 2, 1][:, None, None],
            jnp.where(
                col_at == 0,
                near[:, 1, 0][:, None, None],
                jnp.where(
                    col_at == cols_dev + 1, near[:, 1, 2][:, None, None], own_coarse[:, None, None]
                ),
            ),
        ),
    )
    press_rim = press_wide + rim_coarse
    grad_rad, grad_lat, grad_lon = gradient(press_rim, inv_own)
    result = jnp.stack(
        [
            stepped[0] - grad_rad,
            stepped[1] - grad_lat,
            stepped[2] - grad_lon,
            stepped[3],
            stepped[4],
            stepped[5],
        ],
        axis=0,
    )
    return (result[None], pressure[None])


def solution(mesh):
    return jax.shard_map(
        shards,
        mesh=mesh,
        in_specs=(
            P("panel", None, None, "lat", "lon"),
            P("panel", None, "lat", "lon"),
            P("panel", "lat", "lon", None),
            P("panel", "lat", "lon"),
            P("panel", "lat", "lon"),
            P("panel", "lat", "lon"),
            P("panel", "lat", "lon"),
            P("panel", "lat", "lon"),
        ),
        out_specs=(P("panel", None, None, "lat", "lon"), P("panel", None, "lat", "lon")),
        check_vma=False,
    )
```

```python
import math

import jax
import jax.numpy as jnp
from jax import lax
from jax.experimental import pallas as pl
from jax.experimental.pallas import tpu as pltpu
from jax.sharding import PartitionSpec as P

CAP = 2
WQ = 8


BUOYANCY = 0.5


def partner_2(block, axis, apart):
    count = lax.axis_size(axis)
    route = []
    for low in range(count):
        high = low | 1 << apart
        if high != low and high < count:
            route += [(low, high), (high, low)]
    return lax.ppermute(block, axis, route)


def padded_2(shard, sides, width):
    for axis, dim in sides:
        size, length = (lax.axis_size(axis), shard.shape[dim])
        up = [(i, (i + 1) % size) for i in range(size - 1)]
        down = [(j, i) for i, j in up]
        last = lax.slice_in_dim(shard, length - width, length, axis=dim)
        leading = lax.slice_in_dim(shard, 0, width, axis=dim)
        before = lax.ppermute(last, axis, up)
        after = lax.ppermute(leading, axis, down)
        shard = jnp.concatenate([before, shard, after], axis=dim)
    return shard


def gather_by_exchange(block, axis):
    count = lax.axis_size(axis)
    repeated = jnp.broadcast_to(block[None], (count,) + block.shape)
    gathered = lax.all_to_all(repeated, axis, split_axis=0, concat_axis=0, tiled=True)
    return gathered.reshape((count * block.shape[0],) + block.shape[1:])


def corner_blend(table, rows, weights, width):
    count = rows.shape[0]

    def kernel(rows_ref, weights_ref, table_ref, out_ref):
        def body(t, carry):
            at = rows_ref[t]
            total = weights_ref[0, t] * table_ref[pl.ds(at, 1), :]
            for k, offset in enumerate((1, width, width + 1)):
                total = total + weights_ref[k + 1, t] * table_ref[pl.ds(at + offset, 1), :]
            out_ref[pl.ds(t, 1), :] = total
            return carry

        lax.fori_loop(0, count, body, 0, unroll=32)

    return pl.pallas_call(
        kernel,
        out_shape=jax.ShapeDtypeStruct((count, table.shape[1]), table.dtype),
        in_specs=[
            pl.BlockSpec(memory_space=pltpu.SMEM),
            pl.BlockSpec(memory_space=pltpu.SMEM),
            pl.BlockSpec(memory_space=pltpu.VMEM),
        ],
        out_specs=pl.BlockSpec(memory_space=pltpu.VMEM),
    )(rows, weights, table)


def metric(row_index, total_rows):
    colatitude = (
        math.pi / 4.0 + (row_index.astype(jnp.float32) + 0.5) * (math.pi / 2.0) / total_rows
    )
    inv_sine = 1.0 / jnp.sin(colatitude)
    return (inv_sine, inv_sine * inv_sine)


def lap_shrink(field, row_gain):
    centre = field[..., 1:-1, 1:-1]
    padded = jnp.pad(centre, [(0, 0)] * (centre.ndim - 3) + [(1, 1), (0, 0), (0, 0)])
    lat_term = field[..., 2:, 1:-1] + field[..., :-2, 1:-1] - 2.0 * centre
    lon_term = field[..., 1:-1, 2:] + field[..., 1:-1, :-2] - 2.0 * centre
    radial = padded[..., 2:, :, :] + padded[..., :-2, :, :] - 2.0 * centre
    return lat_term + row_gain[:, None] * lon_term + radial


def diverge(velocity, inv_sine):
    radial_pad = jnp.pad(velocity[0, :, 1:-1, 1:-1], ((1, 1), (0, 0), (0, 0)))
    lat_part = velocity[1, :, 2:, 1:-1] - velocity[1, :, :-2, 1:-1]
    lon_part = velocity[2, :, 1:-1, 2:] - velocity[2, :, 1:-1, :-2]
    rad_part = radial_pad[2:] - radial_pad[:-2]
    return 0.5 * (lat_part + inv_sine[:, None] * lon_part + rad_part)


def gradient(pressure, inv_sine):
    radial_pad = jnp.pad(pressure[:, 1:-1, 1:-1], ((1, 1), (0, 0), (0, 0)))
    grad_rad = 0.5 * (radial_pad[2:] - radial_pad[:-2])
    grad_lat = 0.5 * (pressure[:, 2:, 1:-1] - pressure[:, :-2, 1:-1])
    grad_lon = 0.5 * inv_sine[:, None] * (pressure[:, 1:-1, 2:] - pressure[:, 1:-1, :-2])
    return (grad_rad, grad_lat, grad_lon)


def cosine_table(length):
    mode_ids = jnp.arange(length, dtype=jnp.float32)
    cell_mid = jnp.arange(length, dtype=jnp.float32) + 0.5
    row_norm = jnp.sqrt(jnp.where(mode_ids > 0, 2.0, 1.0) / length)
    cos_table = row_norm[:, None] * jnp.cos(
        math.pi * mode_ids[:, None] * cell_mid[None, :] / length
    )
    eigenvalue = 4.0 * jnp.sin(math.pi * mode_ids / (2.0 * length)) ** 2
    return (cos_table, eigenvalue)


def coarse_divisor(levels, n_lat, n_lon):
    eig_rad = cosine_table(levels)[1]
    eig_lat = cosine_table(n_lat)[1]
    eig_lon = cosine_table(n_lon)[1]
    return (
        eig_rad[:, None, None]
        + eig_lat[None, :, None]
        + eig_lon[None, None, :]
        + 1.0 / (n_lat * n_lon)
    )


def coarse_solve(block_sum, n_lat, n_lon):
    highest = lax.Precision.HIGHEST
    tab_rad = cosine_table(block_sum.shape[0])[0]
    tab_lat = cosine_table(n_lat)[0]
    tab_lon = cosine_table(n_lon)[0]
    spectrum = jnp.einsum("kr,rlo->klo", tab_rad, block_sum, precision=highest)
    spectrum = jnp.einsum("kl,rlo->rko", tab_lat, spectrum, precision=highest)
    spectrum = jnp.einsum("ko,rlo->rlk", tab_lon, spectrum, precision=highest)
    spectrum = spectrum / coarse_divisor(block_sum.shape[0], n_lat, n_lon)
    restored = jnp.einsum("kr,klo->rlo", tab_rad, spectrum, precision=highest)
    restored = jnp.einsum("kl,rko->rlo", tab_lat, restored, precision=highest)
    restored = jnp.einsum("ko,rlk->rlo", tab_lon, restored, precision=highest)
    return restored / math.sqrt(n_lat * n_lon)


def fractions(weight_ids):
    frac_lat = ((weight_ids // WQ).astype(jnp.float32) + 0.5) / WQ
    frac_lon = ((weight_ids % WQ).astype(jnp.float32) + 0.5) / WQ
    return (frac_lat, frac_lon)


def bilinear(lower_left, lower_right, upper_left, upper_right, frac_lat, frac_lon):
    return (
        (1.0 - frac_lat) * (1.0 - frac_lon) * lower_left
        + (1.0 - frac_lat) * frac_lon * lower_right
        + frac_lat * (1.0 - frac_lon) * upper_left
        + frac_lat * frac_lon * upper_right
    )


def shards(fields, viscosity, partner, src_row, src_col, weight_id, border_angle, dest_cell):
    n_lat = lax.axis_size("lat")
    n_lon = lax.axis_size("lon")
    lat_pos = lax.axis_index("lat")
    lon_pos = lax.axis_index("lon")
    own_fields = fields[0]
    levels, rows_dev, cols_dev = (own_fields.shape[1], own_fields.shape[2], own_fields.shape[3])
    channels = 6 * levels
    blocks = partner.shape[2]
    block_cells = src_row.shape[2] // blocks
    capacity = CAP
    slot_count = n_lon * capacity
    total_rows = rows_dev * n_lat
    flat_cells = own_fields.reshape(channels, rows_dev * cols_dev)
    target = partner[0, 0, :, 0]
    onehot = (target[:, None] == jnp.arange(n_lon, dtype=jnp.int32)[None, :]).astype(jnp.int32)
    before = jnp.sum(
        (jnp.cumsum(onehot, axis=0, dtype=jnp.int32) - onehot) * onehot, axis=1, dtype=jnp.int32
    )
    slot_of = target * capacity + before
    base_cell = (src_row[0, 0] * cols_dev + src_col[0, 0]).reshape(blocks, block_cells)
    weight_ids = weight_id[0, 0].reshape(blocks, block_cells)
    empty = jnp.zeros((slot_count, block_cells), jnp.int32)
    slot_row = jnp.broadcast_to(jnp.pad(slot_of, (0, block_cells - blocks)), empty.shape)
    asked = jnp.stack(
        [empty.at[slot_of].set(base_cell), empty.at[slot_of].set(weight_ids), slot_row], axis=1
    ).reshape(n_lon, capacity, 3, block_cells)
    panel_pos = lax.axis_index("panel")
    panel_count = lax.axis_size("panel")
    mine = jnp.arange(panel_count, dtype=jnp.int32) != panel_pos
    routed = jnp.where(mine[:, None, None, None, None], asked[None], 0)
    routed = routed.reshape((panel_count * n_lon,) + asked.shape[1:])
    routed = lax.all_to_all(routed, ("panel", "lon"), split_axis=0, concat_axis=0, tiled=True)
    routed = routed.reshape((panel_count, n_lon) + asked.shape[1:])
    requests = jnp.sum(jnp.where(mine[:, None, None, None, None], routed, 0), axis=0)
    slot_mirror = lax.dynamic_index_in_dim(requests, lon_pos, 0, keepdims=False)[0, 2, :blocks]
    cells_asked = requests[:, :, 0, :].reshape(-1)
    frac_lat, frac_lon = fractions(requests[:, :, 1, :].reshape(-1))
    weights = jnp.stack(
        [
            (1.0 - frac_lat) * (1.0 - frac_lon),
            (1.0 - frac_lat) * frac_lon,
            frac_lat * (1.0 - frac_lon),
            frac_lat * frac_lon,
        ],
        axis=0,
    )
    served = corner_blend(flat_cells.T, cells_asked, weights, cols_dev)
    served = served.reshape(n_lon, capacity, block_cells, channels)
    served = lax.all_to_all(served, "lon", split_axis=0, concat_axis=0, tiled=True)
    served = served.reshape(slot_count, block_cells, channels)[slot_mirror]
    values = partner_2(served, "panel", 0)
    values = values.reshape(blocks * block_cells, channels).T.reshape(6, levels, blocks * block_cells)
    turn = border_angle[0, 0]
    cos_angle = jnp.cos(turn)
    sin_angle = jnp.sin(turn)
    rotated = jnp.stack(
        [
            values[0],
            cos_angle * values[1] + sin_angle * values[2],
            cos_angle * values[2] - sin_angle * values[1],
            values[3],
            cos_angle * values[4] + sin_angle * values[5],
            cos_angle * values[5] - sin_angle * values[4],
        ],
        axis=0,
    ).reshape(channels, blocks * block_cells)
    filled = flat_cells.at[:, dest_cell[0, 0]].set(rotated).reshape(6, levels, rows_dev, cols_dev)
    diffusivity = viscosity[0]
    inv_own, gain_own = metric(
        lat_pos * rows_dev + jnp.arange(-0, rows_dev + 0, dtype=jnp.int32), total_rows
    )
    halo = 3
    total_cols = cols_dev * n_lon
    row_first = lat_pos * rows_dev
    col_first = lon_pos * cols_dev

    def inside(reach):
        rows = row_first - reach + jnp.arange(rows_dev + 2 * reach, dtype=jnp.int32)
        cols = col_first - reach + jnp.arange(cols_dev + 2 * reach, dtype=jnp.int32)
        return ((rows >= 0) & (rows < total_rows))[:, None] & ((cols >= 0) & (cols < total_cols))[
            None, :
        ]

    stack = jnp.concatenate([filled.reshape(channels, rows_dev, cols_dev), diffusivity], axis=0)
    wide = padded_2(stack, (("lat", 1), ("lon", 2)), halo)
    wide_fields = wide[:channels].reshape(6, levels, rows_dev + 2 * halo, cols_dev + 2 * halo)
    wide_visc = wide[channels:]
    inv_two, gain_two = metric(row_first + jnp.arange(-2, rows_dev + 2, dtype=jnp.int32), total_rows)
    inv_one, gain_one = metric(row_first + jnp.arange(-1, rows_dev + 1, dtype=jnp.int32), total_rows)
    centre = wide_fields[..., 1:-1, 1:-1]
    stepped_wide = centre[0:3] + wide_visc[None, :, 1:-1, 1:-1] * lap_shrink(
        wide_fields[0:3], gain_two
    )
    stepped_wide = jnp.concatenate(
        [stepped_wide[0:1] + BUOYANCY * centre[3:4], stepped_wide[1:]], axis=0
    )
    scalars = wide_fields[3:6, :, 2:-2, 2:-2]
    stepped_rest = scalars[..., 1:-1, 1:-1] + wide_visc[None, :, 3:-3, 3:-3] * lap_shrink(
        scalars, gain_own
    )
    velocity = jnp.where(inside(2), stepped_wide, 0.0)
    divergence_wide = diverge(velocity, inv_one)
    press_wide = jnp.where(inside(1), -divergence_wide / (4.0 + 2.0 * gain_one)[:, None], 0.0)
    divergence = divergence_wide[:, 1:-1, 1:-1]
    press_one = press_wide[:, 1:-1, 1:-1]
    stepped = jnp.concatenate([stepped_wide[:, :, 2:-2, 2:-2], stepped_rest], axis=0)
    resid_one = -divergence + lap_shrink(press_wide, gain_own)
    block_sum = jnp.sum(resid_one, axis=(1, 2)) * (1.0 / math.sqrt(rows_dev * cols_dev))
    gathered = gather_by_exchange(block_sum[None], "lon")
    gathered = gather_by_exchange(gathered[None], "lat")
    coarse = coarse_solve(jnp.transpose(gathered, (2, 0, 1)), n_lat, n_lon)
    start = jnp.zeros((), jnp.int32)
    near = lax.dynamic_slice(
        jnp.pad(coarse, ((0, 0), (1, 1), (1, 1))), (start, lat_pos, lon_pos), (levels, 3, 3)
    )
    own_coarse = near[:, 1, 1]
    pressure = press_one + own_coarse[:, None, None]
    row_at = lax.broadcasted_iota(jnp.int32, (rows_dev + 2, cols_dev + 2), 0)
    col_at = lax.broadcasted_iota(jnp.int32, (rows_dev + 2, cols_dev + 2), 1)
    rim_coarse = jnp.where(
        row_at == 0,
        near[:, 0, 1][:, None, None],
        jnp.where(
            row_at == rows_dev + 1,
            near[:, 2, 1][:, None, None],
            jnp.where(
                col_at == 0,
                near[:, 1, 0][:, None, None],
                jnp.where(
                    col_at == cols_dev + 1, near[:, 1, 2][:, None, None], own_coarse[:, None, None]
                ),
            ),
        ),
    )
    press_rim = press_wide + rim_coarse
    grad_rad, grad_lat, grad_lon = gradient(press_rim, inv_own)
    result = jnp.stack(
        [
            stepped[0] - grad_rad,
            stepped[1] - grad_lat,
            stepped[2] - grad_lon,
            stepped[3],
            stepped[4],
            stepped[5],
        ],
        axis=0,
    )
    return (result[None], pressure[None])


def solution(mesh):
    return jax.shard_map(
        shards,
        mesh=mesh,
        in_specs=(
            P("panel", None, None, "lat", "lon"),
            P("panel", None, "lat", "lon"),
            P("panel", "lat", "lon", None),
            P("panel", "lat", "lon"),
            P("panel", "lat", "lon"),
            P("panel", "lat", "lon"),
            P("panel", "lat", "lon"),
            P("panel", "lat", "lon"),
        ),
        out_specs=(P("panel", None, None, "lat", "lon"), P("panel", None, "lat", "lon")),
        check_vma=False,
    )
```
